256 devices in a mesh: seq: 32 (over z, x), tp: 8 (over y, core).
Axes of the slice: x: 4, y: 4, z: 8, core: 2. Of those that a mesh axis runs over, the one named last changes fastest.
Arguments:
- prefill_states: bfloat16 [8192, 1536], P('seq'), may hold values from -6 to 6
- decode_states: bfloat16 [256, 1536], P(('seq', 'tp')), may hold values from -6 to 6
- attn_gain: bfloat16 [1536], replicated, may hold values from 0.25 to 1.75
- query_weight: bfloat16 [1536, 1536], P(None, 'tp'), may hold values from -0.625 to 0.625
- keyvalue_weight: bfloat16 [1536, 8, 128], P(None, 'tp'), as said below
- output_weight: bfloat16 [1536, 1536], P('tp'), may hold values from -0.3125 to 0.3125
- cache_keyval: bfloat16 [256, 2048, 8, 128], P(None, 'seq', 'tp'), may hold values from -68 to 68, as said below
- cached_length: int32 [256], replicated, may hold values from 1 to 2048, as said below
- span_tenant: int32 [4], replicated, may hold values from 0 to 3
- ffn_gain: bfloat16 [1536], replicated, may hold values from 0.25 to 1.75
- expert_in: bfloat16 [32, 1536, 1024], P('seq'), may hold values from -0.15625 to 0.15625
- expert_out: bfloat16 [32, 512, 1536], P('seq'), may hold values from -0.25 to 0.25
- routes: int32 [8448, 8], P(('seq', 'tp')), may hold values from 0 to 31, all different within a row; in each aligned block of 33 rows (0 to 32, 33 to 65, ...) at most 18 rows name the same one
- gate_values: float32 [8448, 8], P(('seq', 'tp')), may hold values from 0.05 to 0.3
Outputs:
- prefill_out: bfloat16 [8192, 1536], P(('seq', 'tp'))
- decode_out: bfloat16 [256, 1536], P(('seq', 'tp'))
The draws below stay inside these ranges and needn't reach their ends.
Inputs may be any that keep to these rules, and one draw needn't show every extreme that they name: `cached_length`: positions at or beyond a request's length hold no key; the new token stands at that length. `cache_keyval`: keys are rotated at their positions. `keyvalue_weight`: keys first, then values, in each head. `routes`: in the rows of one device no expert is named more than 18 times, a bound that some block reaches.
All inputs are finite; a program needn't handle non-finite values.
Results may differ from the reference program's by a relative error of at most 0.02.
The reference program's roundings to bfloat16 on the way count: a program that leaves them out, or rounds other values in their place, can miss the bound.
Values may be sent and summed in bfloat16 or wider, within the bound.
No kernel may reach another device: no remote copies, remote signals or barrier semaphores. Data moves between devices by JAX's collectives and lax.ppermute only.
A program may use at most 128 MiB of HBM per device.

```python
import math
import jax
import jax.numpy as jnp
import numpy as np
from jax import lax

MODEL_DIM = 1536
QUERY_HEADS = 24
KEYVALUE_HEADS = 8
HEAD_SIZE = 64
FF = 512
TOP = 8
EXPERTS = 32
SPAN = 2048
TEN = 4
PRE_DEV = 256
DEC_DEV = 1
PREFILL_TOTAL = 8192
SPANS = 4
DECODE_REQUESTS = 256
CONTEXT_SLOTS = 2048
ROWS_DEV = 33
ROWS = 8448
CAP = 18
N_SEQ = 32
N_TP = 8


def draw_keyvalue_weight(key, part):
    weight_dimensions = (MODEL_DIM, KEYVALUE_HEADS, 2 * HEAD_SIZE)
    values = jnp.clip(jax.random.normal(jax.random.fold_in(key, 34), weight_dimensions, jnp.float32), -6.0, 6.0) * MODEL_DIM ** (-0.5)
    return values.astype(jnp.bfloat16)


def draw_cache_keyval(key, part):
    cache_dimensions = (DECODE_REQUESTS, CONTEXT_SLOTS, KEYVALUE_HEADS, 2 * HEAD_SIZE)
    values = jnp.clip(jax.random.normal(jax.random.fold_in(key, 11), cache_dimensions, jnp.float32), -6.0, 6.0)
    return values.astype(jnp.bfloat16)


def draw_cached_length(key, part):
    drawn = jax.random.randint(jax.random.fold_in(key, 21), (DECODE_REQUESTS,), 1, CONTEXT_SLOTS + 1, dtype=jnp.int32)
    chosen = jax.random.randint(jax.random.fold_in(key, 22), (), 0, DECODE_REQUESTS, dtype=jnp.int32)
    return drawn.at[chosen].set(CONTEXT_SLOTS)


def place_ends(array, rng, low, top_value):
    longest = array.shape.index(max(array.shape))
    spots = []
    for shift in (0, 1):
        where = [jax.random.randint(jax.random.fold_in(rng, axis), (), 0, length) for axis, length in enumerate(array.shape)]
        where[longest] = (where[longest] + shift) % array.shape[longest]
        spots.append(tuple(where))
    return array.at[spots[0]].set(low).at[spots[1]].set(top_value)


def block_scale(rng, shape, cuts, smallest, largest):
    loudness = 1.0
    for dim, parts in cuts:
        steps = jax.random.uniform(jax.random.fold_in(jax.random.fold_in(rng, 6), dim), (parts,), jnp.float32, smallest / len(cuts), largest / len(cuts))
        loudness = loudness * jnp.repeat(jnp.exp(steps), shape[dim] // parts).reshape((-1,) + (1,) * (len(shape) - 1 - dim))
    return loudness


def shared_out(key, own, number, rows, count, top, limit, lean):
    ranking = jax.random.permutation(key, count)
    packed, usual = load_shares(count, rows * top, limit, lean, True), load_shares(count, rows * top, limit, lean, False)
    places = jnp.arange(count)

    def named(tallies, turn):
        used = int((tallies > 0).sum())
        fixed = max(1, used // 4)
        shifted = fixed + (places - fixed + turn * (used - fixed)) % max(1, count - fixed)
        return jnp.zeros((count,), jnp.int32).at[ranking[jnp.where(places < fixed, places, shifted)]].set(jnp.asarray(tallies, jnp.int32))

    tallies = jnp.where(number % 4 == 0, named(packed, number // 4), named(usual, number - number // 4 - 1))
    mixed = jax.random.permutation(jax.random.fold_in(own, 3), count)
    giver, taker = mixed[0:count // 2 * 2:2], mixed[1:count // 2 * 2:2]
    margin = jnp.minimum(tallies[giver] - 1, limit - tallies[taker]) // 2
    margin = jnp.where((giver == ranking[0]) | (taker == ranking[0]) | (tallies[taker] == 0), 0, jnp.maximum(margin, 0))
    shifted = jax.random.randint(jax.random.fold_in(own, 4), (count // 2,), 0, 1 << 20) % (margin + 1)
    tallies = tallies.at[giver].add(-shifted).at[taker].add(shifted)
    members = jnp.searchsorted(jnp.cumsum(tallies), jnp.arange(rows * top), side="right").astype(jnp.int32)
    table = members.reshape(top, rows).T
    table = table[jax.random.permutation(jax.random.fold_in(own, 1), rows)]
    turn = jax.random.randint(jax.random.fold_in(own, 2), (rows, 1), 0, top)
    return jnp.take_along_axis(table, (jnp.arange(top)[None, :] + turn) % top, axis=1)


def load_shares(count, total, limit, skew, full):
    weights = [(1 << 20) // math.isqrt(standing ** skew) + 1 for standing in range(1, count + 1)]
    largest = limit if full else min(limit, max(-(-total // count), total * weights[0] // sum(weights)))
    least = 1 if total - largest >= count - 1 else 0
    given, surplus = [largest] + [least] * (count - 1), total - largest - least * (count - 1)
    while surplus > 0:
        free = [i for i in range(1, count) if given[i] < largest] or [i for i in range(1, count) if given[i] < limit]
        pool, budget = sum([weights[i] for i in free]), surplus
        for i in free:
            addition = min(limit - given[i], max(1, budget * weights[i] // pool), surplus)
            given[i] = given[i] + addition
            surplus = surplus - addition
    return np.array(given)


def noise(own_key, extent, scale, bound, shards=(), kind=jnp.bfloat16):
    array = scale * jax.random.normal(own_key, extent, jnp.float32)
    if shards:
        array = array * block_scale(own_key, extent, shards, -0.22, 0.18)
    return jnp.clip(array, -bound, bound).astype(kind)


def setup_inputs(seed: int = 0) -> dict:
    splits = jax.random.split(jax.random.key(seed), 15)
    prefill_states = noise(splits[0], (PREFILL_TOTAL, MODEL_DIM), 1.0, 6.0, ((0, 32),))
    decode_states = noise(splits[1], (DECODE_REQUESTS, MODEL_DIM), 1.0, 6.0, ((0, 256),))
    attn_gain = jnp.clip(1.0 + 0.15 * jax.random.normal(splits[2], (MODEL_DIM,), jnp.float32), 0.25, 1.75).astype(jnp.bfloat16)
    query_weight = noise(splits[3], (MODEL_DIM, QUERY_HEADS * HEAD_SIZE), (MODEL_DIM // 16) ** -0.5, 0.625, ((1, 8),))
    keyvalue_weight = draw_keyvalue_weight(jax.random.fold_in(splits[14], 71), 0)
    output_weight = noise(splits[5], (QUERY_HEADS * HEAD_SIZE, MODEL_DIM), (QUERY_HEADS * HEAD_SIZE // 4) ** -0.5, 0.3125, ((0, 8),))
    cache_keyval = draw_cache_keyval(jax.random.fold_in(splits[14], 71), 0)
    cached_length = draw_cached_length(jax.random.fold_in(splits[14], 71), 0)
    span_tenant = place_ends(jax.random.randint(splits[8], (SPANS,), 0, TEN), jax.random.fold_in(splits[8], 1), 0, TEN - 1).astype(jnp.int32)
    ffn_gain = jnp.clip(1.0 + 0.15 * jax.random.normal(splits[9], (MODEL_DIM,), jnp.float32), 0.25, 1.75).astype(jnp.bfloat16)
    expert_in = noise(splits[10], (EXPERTS, MODEL_DIM, 2 * FF), MODEL_DIM ** -0.5, 0.15625, ((0, 32),))
    expert_out = noise(splits[11], (EXPERTS, FF, MODEL_DIM), FF ** -0.5, 0.25, ((0, 32),))
    routes_keys = jax.random.split(jax.random.fold_in(splits[12], 1), ROWS // ROWS_DEV)
    routes_turns = jax.random.permutation(jax.random.fold_in(splits[12], 3), ROWS // ROWS_DEV)
    routes = jax.vmap(lambda own, number: shared_out(jax.random.fold_in(splits[12], 2), own, number, ROWS_DEV, EXPERTS, TOP, CAP, 2))(routes_keys, routes_turns).reshape((ROWS, TOP))
    gate_values = jnp.clip(0.05 + 0.25 * jax.random.uniform(splits[13], (ROWS, TOP), jnp.float32) ** block_scale(splits[13], (ROWS, TOP), ((0, 256),), -0.2, 0.2), 0.05, 0.3)
    return {"prefill_states": prefill_states, "decode_states": decode_states, "attn_gain": attn_gain, "query_weight": query_weight, "keyvalue_weight": keyvalue_weight, "output_weight": output_weight, "cache_keyval": cache_keyval, "cached_length": cached_length, "span_tenant": span_tenant, "ffn_gain": ffn_gain, "expert_in": expert_in, "expert_out": expert_out, "routes": routes, "gate_values": gate_values}


eps_norm = 1e-05
rope_base = 10000.0
masked_score = -1e+30

def rms_norm(values, scales):
    floats = values.astype(jnp.float32)
    factor = lax.rsqrt(lax.optimization_barrier(jnp.mean(floats * floats, axis=-1, keepdims=True)) + eps_norm)
    return (floats * factor * scales.astype(jnp.float32)).astype(jnp.bfloat16)

def apply_rotary(values, token_positions):
    half_dim = values.shape[-1] // 2
    frequency = rope_base ** (-2.0 * jnp.arange(half_dim, dtype=jnp.float32) / values.shape[-1])
    angles = token_positions.astype(jnp.float32)[:, None] * frequency[None, :]
    cosine = jnp.cos(angles)[:, None, :]
    sine_part = jnp.sin(angles)[:, None, :]
    first_half = values[..., :half_dim]
    second_half = values[..., half_dim:]
    return jnp.concatenate([first_half * cosine - second_half * sine_part, second_half * cosine + first_half * sine_part], axis=-1)

def span_tables(span_tenant):
    span_count = span_tenant.shape[0]
    ordinal = jnp.arange(span_count, dtype=jnp.int32)
    same_tenant = span_tenant[:, None] == span_tenant[None, :]
    earlier = ordinal[None, :] < ordinal[:, None]
    return lax.optimization_barrier(jnp.sum(jnp.where(same_tenant & earlier, 1, 0), axis=1)).astype(jnp.int32)

def token_tables(token_index, span_tenant, before):
    span_count = span_tenant.shape[0]
    span_index = token_index // SPAN
    onehot = span_index[:, None] == jnp.arange(span_count, dtype=jnp.int32)[None, :]
    tenant = lax.optimization_barrier(jnp.sum(jnp.where(onehot, span_tenant[None, :], 0), axis=1)).astype(jnp.int32)
    offset = lax.optimization_barrier(jnp.sum(jnp.where(onehot, before[None, :], 0), axis=1)).astype(jnp.int32)
    return (tenant, offset * SPAN + token_index % SPAN)

def reference(prefill_states, decode_states, attn_gain, query_weight, keyvalue_weight, output_weight, cache_keyval, cached_length, span_tenant, ffn_gain, expert_in, expert_out, routes, gate_values):
    query_group_count = QUERY_HEADS // KEYVALUE_HEADS
    score_scale = HEAD_SIZE ** (-0.5)
    normalised_input = rms_norm(prefill_states, attn_gain)
    query_matrix = jnp.dot(normalised_input, query_weight, preferred_element_type=jnp.float32).reshape(PREFILL_TOTAL, QUERY_HEADS, HEAD_SIZE)
    keyvalue_rows = jnp.dot(normalised_input, keyvalue_weight.reshape(MODEL_DIM, KEYVALUE_HEADS * 2 * HEAD_SIZE), preferred_element_type=jnp.float32).reshape(PREFILL_TOTAL, KEYVALUE_HEADS, 2 * HEAD_SIZE)
    before = span_tables(span_tenant)
    token_index = jnp.arange(PREFILL_TOTAL, dtype=jnp.int32)
    tenant, token_positions = token_tables(token_index, span_tenant, before)
    query_matrix = apply_rotary(query_matrix, token_positions).astype(jnp.bfloat16).reshape(PREFILL_TOTAL, KEYVALUE_HEADS, query_group_count, HEAD_SIZE)
    keys_all = apply_rotary(keyvalue_rows[..., :HEAD_SIZE], token_positions).astype(jnp.bfloat16).astype(jnp.float32)
    vals_all = keyvalue_rows[..., HEAD_SIZE:].astype(jnp.bfloat16).astype(jnp.float32)
    block_rows = math.gcd(PREFILL_TOTAL, 512)

    def attend_block(first_row):
        query_rows = lax.dynamic_slice_in_dim(query_matrix, first_row, block_rows, 0).astype(jnp.float32)
        query_tenant = lax.dynamic_slice_in_dim(tenant, first_row, block_rows, 0)
        query_index = first_row + jnp.arange(block_rows, dtype=jnp.int32)
        visible = (query_tenant[:, None] == tenant[None, :]) & (query_index[:, None] >= token_index[None, :])
        scores = jnp.einsum('qhgd,khd->qhgk', query_rows, keys_all) * score_scale
        scores = jnp.where(visible[:, None, None, :], scores, masked_score)
        row_max = lax.optimization_barrier(jnp.max(scores, axis=-1, keepdims=True))
        weights_exp = jnp.where(visible[:, None, None, :], jnp.exp(scores - row_max), 0.0)
        row_total = lax.optimization_barrier(jnp.sum(weights_exp, axis=-1))
        rounded = lax.optimization_barrier(weights_exp.astype(jnp.bfloat16)).astype(jnp.float32)
        mixture = jnp.einsum('qhgk,khd->qhgd', rounded, vals_all)
        return (mixture / row_total[..., None]).astype(jnp.bfloat16).reshape(block_rows, QUERY_HEADS * HEAD_SIZE)
    starts = jnp.arange(PREFILL_TOTAL // block_rows, dtype=jnp.int32) * block_rows
    attended = lax.map(attend_block, starts).reshape(PREFILL_TOTAL, QUERY_HEADS * HEAD_SIZE)
    projected = jnp.dot(attended, output_weight, preferred_element_type=jnp.float32)
    prefill_h = (prefill_states.astype(jnp.float32) + projected).astype(jnp.bfloat16)
    decode_normalised = rms_norm(decode_states, attn_gain)
    decode_queries = jnp.dot(decode_normalised, query_weight, preferred_element_type=jnp.float32).reshape(DECODE_REQUESTS, QUERY_HEADS, HEAD_SIZE)
    decode_queries = apply_rotary(decode_queries, cached_length).astype(jnp.bfloat16).reshape(DECODE_REQUESTS, KEYVALUE_HEADS, query_group_count, HEAD_SIZE)
    decode_keyvalues = jnp.dot(decode_normalised, keyvalue_weight.reshape(MODEL_DIM, KEYVALUE_HEADS * 2 * HEAD_SIZE), preferred_element_type=jnp.float32).reshape(DECODE_REQUESTS, KEYVALUE_HEADS, 2 * HEAD_SIZE)
    new_keys = apply_rotary(decode_keyvalues[..., :HEAD_SIZE], cached_length).astype(jnp.bfloat16)
    new_vals = decode_keyvalues[..., HEAD_SIZE:].astype(jnp.bfloat16)
    dec_block = math.gcd(DECODE_REQUESTS, 16)

    def decode_block(first_row):
        block_query = lax.dynamic_slice_in_dim(decode_queries, first_row, dec_block, 0).astype(jnp.float32)
        block_cache = lax.dynamic_slice_in_dim(cache_keyval, first_row, dec_block, 0).astype(jnp.float32)
        block_length = lax.dynamic_slice_in_dim(cached_length, first_row, dec_block, 0)
        block_keys = lax.dynamic_slice_in_dim(new_keys, first_row, dec_block, 0).astype(jnp.float32)
        block_vals = lax.dynamic_slice_in_dim(new_vals, first_row, dec_block, 0).astype(jnp.float32)
        visible = jnp.arange(CONTEXT_SLOTS, dtype=jnp.int32)[None, :] < block_length[:, None]
        scores = jnp.einsum('bhgd,bkhd->bhgk', block_query, block_cache[..., :HEAD_SIZE]) * score_scale
        scores = jnp.where(visible[:, None, None, :], scores, masked_score)
        own_score = lax.optimization_barrier(jnp.sum(block_query * block_keys[:, :, None, :], axis=-1)) * score_scale
        row_max = jnp.maximum(lax.optimization_barrier(jnp.max(scores, axis=-1)), own_score)
        weights_exp = jnp.where(visible[:, None, None, :], jnp.exp(scores - row_max[..., None]), 0.0)
        own_exp = jnp.exp(own_score - row_max)
        row_total = lax.optimization_barrier(jnp.sum(weights_exp, axis=-1)) + own_exp
        rounded = lax.optimization_barrier(weights_exp.astype(jnp.bfloat16)).astype(jnp.float32)
        own_rounded = lax.optimization_barrier(own_exp.astype(jnp.bfloat16)).astype(jnp.float32)
        mixture = jnp.einsum('bhgk,bkhd->bhgd', rounded, block_cache[..., HEAD_SIZE:])
        mixture = mixture + own_rounded[..., None] * block_vals[:, :, None, :]
        return (mixture / row_total[..., None]).astype(jnp.bfloat16).reshape(dec_block, QUERY_HEADS * HEAD_SIZE)
    dec_starts = jnp.arange(DECODE_REQUESTS // dec_block, dtype=jnp.int32) * dec_block
    decode_attended = lax.map(decode_block, dec_starts).reshape(DECODE_REQUESTS, QUERY_HEADS * HEAD_SIZE)
    decode_proj = jnp.dot(decode_attended, output_weight, preferred_element_type=jnp.float32)
    decode_h = (decode_states.astype(jnp.float32) + decode_proj).astype(jnp.bfloat16)
    devices_all = N_SEQ * N_TP
    pre_rows = PRE_DEV // N_TP
    moe_in = jnp.concatenate([prefill_h.reshape(devices_all, pre_rows, MODEL_DIM), decode_h.reshape(devices_all, DEC_DEV, MODEL_DIM)], axis=1).reshape(ROWS, MODEL_DIM)
    normed_moe = rms_norm(moe_in, ffn_gain)
    row_bound = min(ROWS, devices_all * CAP)

    def one_expert(running, expert):
        route_hits = routes == expert
        has_route = jnp.any(route_hits, axis=1)
        weight_row = lax.optimization_barrier(jnp.sum(jnp.where(route_hits, gate_values, 0.0), axis=1))
        picked = jnp.argsort(jnp.where(has_route, 0, 1).astype(jnp.int32), stable=True)[:row_bound].astype(jnp.int32)
        rows_in = normed_moe[picked]
        hidden = jnp.dot(rows_in, expert_in[expert], preferred_element_type=jnp.float32)
        active = (jax.nn.silu(hidden[:, :FF]) * hidden[:, FF:]).astype(jnp.bfloat16)
        result = jnp.dot(active, expert_out[expert], preferred_element_type=jnp.float32).astype(jnp.bfloat16)
        contrib = weight_row[picked][:, None] * result.astype(jnp.float32)
        return (running.at[picked].add(contrib), None)
    combined = lax.scan(one_expert, jnp.zeros((ROWS, MODEL_DIM), jnp.float32), jnp.arange(EXPERTS, dtype=jnp.int32))[0]
    layer_out = (moe_in.astype(jnp.float32) + combined).astype(jnp.bfloat16).reshape(devices_all, ROWS_DEV, MODEL_DIM)
    prefill_out = layer_out[:, :pre_rows].reshape(PREFILL_TOTAL, MODEL_DIM)
    decode_out = layer_out[:, pre_rows:].reshape(DECODE_REQUESTS, MODEL_DIM)
    return (prefill_out, decode_out)
```

```python
import math

import jax
import jax.numpy as jnp
from jax import lax
from jax.sharding import PartitionSpec as P

EXPERTS = 32
SPAN = 2048


eps_norm = 1e-05
rope_base = 10000.0
masked_score = -1e30
key_block = 512


def rms_norm(values, scales):
    floats = values.astype(jnp.float32)
    factor = lax.rsqrt(jnp.mean(floats * floats, axis=-1, keepdims=True) + eps_norm)
    return (floats * factor * scales.astype(jnp.float32)).astype(jnp.bfloat16)


def apply_rotary(values, token_positions):
    half_dim = values.shape[-1] // 2
    frequency = rope_base ** (-2.0 * jnp.arange(half_dim, dtype=jnp.float32) / values.shape[-1])
    angles = token_positions.astype(jnp.float32)[:, None] * frequency[None, :]
    cosine = jnp.cos(angles)[:, None, :]
    sine_part = jnp.sin(angles)[:, None, :]
    first_half = values[..., :half_dim]
    second_half = values[..., half_dim:]
    return jnp.concatenate(
        [
            first_half * cosine - second_half * sine_part,
            second_half * cosine + first_half * sine_part,
        ],
        axis=-1,
    )


def span_tables(span_tenant):
    span_count = span_tenant.shape[0]
    ordinal = jnp.arange(span_count, dtype=jnp.int32)
    same_tenant = span_tenant[:, None] == span_tenant[None, :]
    earlier = ordinal[None, :] < ordinal[:, None]
    return jnp.sum(jnp.where(same_tenant & earlier, 1, 0), axis=1).astype(jnp.int32)


def token_tables(token_index, span_tenant, before):
    span_count = span_tenant.shape[0]
    span_index = token_index // SPAN
    onehot = span_index[:, None] == jnp.arange(span_count, dtype=jnp.int32)[None, :]
    tenant = jnp.sum(jnp.where(onehot, span_tenant[None, :], 0), axis=1)
    offset = jnp.sum(jnp.where(onehot, before[None, :], 0), axis=1)
    return (tenant, offset * SPAN + token_index % SPAN)


def attend_keys(fold_state, keyvalue_rows, visible, query_matrix, score_scale):
    run_max, run_total, run_acc = fold_state
    head_dim = keyvalue_rows.shape[-1] // 2
    scores = (
        jnp.einsum(
            "qhgd,khd->qhgk",
            query_matrix,
            keyvalue_rows[..., :head_dim],
            preferred_element_type=jnp.float32,
        )
        * score_scale
    )
    mask_full = visible[:, None, None, :]
    scores = jnp.where(mask_full, scores, masked_score)
    new_max = jnp.maximum(run_max, jnp.max(scores, axis=-1))
    weights_exp = jnp.where(mask_full, jnp.exp(scores - new_max[..., None]), 0.0)
    factor = jnp.exp(run_max - new_max)
    new_total = run_total * factor + jnp.sum(weights_exp, axis=-1)
    new_acc = run_acc * factor[..., None] + jnp.einsum(
        "qhgk,khd->qhgd",
        weights_exp.astype(jnp.bfloat16),
        keyvalue_rows[..., head_dim:],
        preferred_element_type=jnp.float32,
    )
    return (new_max, new_total, new_acc)


def swap_partner(values, axis_name, distance):
    count = lax.axis_size(axis_name)
    pairs = [(i, i ^ distance) for i in range(count)]
    return lax.ppermute(values, axis_name, pairs)


def gather_blocks(block, axis_name, distances):
    index = lax.axis_index(axis_name)
    stacked = block
    done = []
    for distance in distances:
        theirs = swap_partner(stacked, axis_name, distance)
        upper = (index // distance) % 2 == 1
        low = jnp.where(upper, theirs, stacked)
        high = jnp.where(upper, stacked, theirs)
        place = sum(1 for d in done if d > distance)
        stacked = jnp.stack([low, high], axis=place)
        done.append(distance)
    return stacked.reshape((-1,) + block.shape[1:])


def scatter_blocks(values, axis_name, distances, combine, send_type=None):
    count = lax.axis_size(axis_name)
    index = lax.axis_index(axis_name)
    levels = count.bit_length() - 1
    rows = values.shape[0] // count
    stacked = values.reshape((2,) * levels + (rows,) + values.shape[1:])
    remaining = [count >> (j + 1) for j in range(levels)]
    for distance in distances:
        place = remaining.index(distance)
        low = lax.index_in_dim(stacked, 0, place, keepdims=False)
        high = lax.index_in_dim(stacked, 1, place, keepdims=False)
        upper = (index // distance) % 2 == 1
        keep = jnp.where(upper, high, low)
        send = jnp.where(upper, low, high)
        if send_type is not None:
            send = send.astype(send_type)
        received = swap_partner(send, axis_name, distance).astype(keep.dtype)
        stacked = combine(keep, received)
        remaining.pop(place)
    return stacked


def add_parts(first, second):
    return first + second


def merge_softmax(first, second):
    first_max, second_max = first[..., -1], second[..., -1]
    top = jnp.maximum(first_max, second_max)
    first_scale = jnp.exp(first_max - top)[..., None]
    second_scale = jnp.exp(second_max - top)[..., None]
    body = first[..., :-1] * first_scale + second[..., :-1] * second_scale
    return jnp.concatenate([body, top[..., None]], axis=-1)


def shards(
    prefill_states,
    decode_states,
    attn_gain,
    query_weight,
    keyvalue_weight,
    output_weight,
    cache_keyval,
    cached_length,
    span_tenant,
    ffn_gain,
    expert_in,
    expert_out,
    routes,
    gate_values,
):
    seq_count = lax.axis_size("seq")
    tp_count = lax.axis_size("tp")
    seq_index = lax.axis_index("seq")
    tp_index = lax.axis_index("tp")
    pre_local, model_width = prefill_states.shape
    dec_local = decode_states.shape[0]
    heads_kv = keyvalue_weight.shape[1]
    head_dim = keyvalue_weight.shape[2] // 2
    heads_q = query_weight.shape[1] // head_dim
    query_group_count = heads_q // heads_kv
    score_scale = head_dim ** (-0.5)
    pre_share = pre_local // tp_count
    normalised_input = rms_norm(prefill_states, attn_gain)
    query_matrix = jnp.dot(
        normalised_input, query_weight, preferred_element_type=jnp.float32
    ).reshape(pre_local, heads_q, head_dim)
    keyvalue_rows = jnp.dot(
        normalised_input,
        keyvalue_weight.reshape(model_width, heads_kv * 2 * head_dim),
        preferred_element_type=jnp.float32,
    ).reshape(pre_local, heads_kv, 2 * head_dim)
    before = span_tables(span_tenant)
    token_index = seq_index * pre_local + jnp.arange(pre_local, dtype=jnp.int32)
    tenant, token_positions = token_tables(token_index, span_tenant, before)
    query_matrix = (
        apply_rotary(query_matrix, token_positions)
        .astype(jnp.bfloat16)
        .reshape(pre_local, heads_kv, query_group_count, head_dim)
    )
    rotated_keys = apply_rotary(keyvalue_rows[..., :head_dim], token_positions).astype(jnp.bfloat16)
    local_keyvals = jnp.concatenate(
        [rotated_keys, keyvalue_rows[..., head_dim:].astype(jnp.bfloat16)], axis=-1
    )
    start_state = (
        jnp.full((pre_local, heads_kv, query_group_count), masked_score, jnp.float32),
        jnp.zeros((pre_local, heads_kv, query_group_count), jnp.float32),
        jnp.zeros((pre_local, heads_kv, query_group_count, head_dim), jnp.float32),
    )
    seq_near_first = [1 << j for j in range(seq_count.bit_length() - 1)]
    tp_near_first = [1 << j for j in range(tp_count.bit_length() - 1)]
    key_piece = gather_blocks(local_keyvals, "seq", seq_near_first[::-1])
    piece_rows = key_piece.shape[0]
    block_len = math.gcd(piece_rows, key_block)
    blocks = key_piece.reshape(piece_rows // block_len, block_len, heads_kv, 2 * head_dim)

    def one_block(run_state, block_item):
        block_number, block_vals = block_item
        key_index = block_number * block_len + jnp.arange(block_len, dtype=jnp.int32)
        key_tenant = token_tables(key_index, span_tenant, before)[0]
        visible = (tenant[:, None] == key_tenant[None, :]) & (
            token_index[:, None] >= key_index[None, :]
        )
        run_state = attend_keys(run_state, block_vals, visible, query_matrix, score_scale)
        return (run_state, None)

    run_max, run_total, run_acc = lax.scan(
        one_block, start_state, (jnp.arange(piece_rows // block_len, dtype=jnp.int32), blocks)
    )[0]
    attended = (
        (run_acc / run_total[..., None]).astype(jnp.bfloat16).reshape(pre_local, heads_q * head_dim)
    )
    prefill_part = jnp.dot(attended, output_weight, preferred_element_type=jnp.float32)
    prefill_sum = scatter_blocks(
        prefill_part, "tp", tp_near_first, add_parts, send_type=jnp.bfloat16
    )
    group_states = gather_blocks(decode_states, "tp", tp_near_first[::-1])
    group_rows = group_states.shape[0]
    group_lengths = lax.dynamic_slice_in_dim(cached_length, seq_index * group_rows, group_rows, 0)
    decode_normalised = rms_norm(group_states, attn_gain)
    group_queries = jnp.dot(
        decode_normalised, query_weight, preferred_element_type=jnp.float32
    ).reshape(group_rows, heads_q, head_dim)
    group_queries = (
        apply_rotary(group_queries, group_lengths)
        .astype(jnp.bfloat16)
        .reshape(group_rows, heads_kv, query_group_count, head_dim)
    )
    decode_keyvalues = jnp.dot(
        decode_normalised,
        keyvalue_weight.reshape(model_width, heads_kv * 2 * head_dim),
        preferred_element_type=jnp.float32,
    ).reshape(group_rows, heads_kv, 2 * head_dim)
    new_keys = apply_rotary(decode_keyvalues[..., :head_dim], group_lengths).astype(jnp.bfloat16)
    new_vals = decode_keyvalues[..., head_dim:].astype(jnp.bfloat16)
    decode_queries = gather_blocks(group_queries, "seq", seq_near_first[::-1])
    cache_local = cache_keyval.shape[1]
    cache_pos = seq_index * cache_local + jnp.arange(cache_local, dtype=jnp.int32)
    visible = (cache_pos[None, :] < cached_length[:, None])[:, None, None, :]
    scores = (
        jnp.einsum(
            "bhgd,bkhd->bhgk",
            decode_queries,
            cache_keyval[..., :head_dim],
            preferred_element_type=jnp.float32,
        )
        * score_scale
    )
    scores = jnp.where(visible, scores, masked_score)
    local_max = jnp.max(scores, axis=-1)
    weights_exp = jnp.where(visible, jnp.exp(scores - local_max[..., None]), 0.0)
    local_total = jnp.sum(weights_exp, axis=-1)
    local_acc = jnp.einsum(
        "bhgk,bkhd->bhgd",
        weights_exp.astype(jnp.bfloat16),
        cache_keyval[..., head_dim:],
        preferred_element_type=jnp.float32,
    )
    packed = jnp.concatenate([local_acc, local_total[..., None], local_max[..., None]], axis=-1)
    merged = scatter_blocks(packed, "seq", seq_near_first, merge_softmax)
    merged_acc = merged[..., :head_dim]
    merged_total = merged[..., head_dim]
    merged_max = merged[..., head_dim + 1]
    own_score = (
        jnp.sum(
            group_queries.astype(jnp.float32) * new_keys.astype(jnp.float32)[:, :, None, :],
            axis=-1,
        )
        * score_scale
    )
    final_max = jnp.maximum(merged_max, own_score)
    rescale = jnp.exp(merged_max - final_max)
    own_exp = jnp.exp(own_score - final_max)
    final_total = merged_total * rescale + own_exp
    own_rounded = lax.optimization_barrier(own_exp.astype(jnp.bfloat16)).astype(jnp.float32)
    final_acc = (
        merged_acc * rescale[..., None]
        + own_rounded[..., None] * new_vals.astype(jnp.float32)[:, :, None, :]
    )
    decode_attended = (
        (final_acc / final_total[..., None])
        .astype(jnp.bfloat16)
        .reshape(group_rows, heads_q * head_dim)
    )
    decode_part = jnp.dot(decode_attended, output_weight, preferred_element_type=jnp.float32)
    decode_sum = scatter_blocks(decode_part, "tp", tp_near_first, add_parts)
    own_states = lax.dynamic_slice_in_dim(prefill_states, tp_index * pre_share, pre_share, 0)
    prefill_h = (own_states.astype(jnp.float32) + prefill_sum).astype(jnp.bfloat16)
    decode_h = (decode_states.astype(jnp.float32) + decode_sum).astype(jnp.bfloat16)
    moe_in = jnp.concatenate([prefill_h, decode_h], axis=0)
    normed_moe = rms_norm(moe_in, ffn_gain)
    rows_dev, top_count = routes.shape
    capacity = 2 * ((rows_dev * top_count + EXPERTS - 1) // EXPERTS)
    flat_routes = routes.reshape(rows_dev * top_count)
    expert_ids = jnp.arange(EXPERTS, dtype=jnp.int32)
    onehot = (flat_routes[:, None] == expert_ids[None, :]).astype(jnp.int32)
    slot_rank = jnp.sum(jnp.cumsum(onehot, axis=0) * onehot, axis=1) - 1
    slot_index = flat_routes * capacity + slot_rank
    repeated = jnp.repeat(normed_moe, top_count, axis=0)
    buffer = jnp.zeros((EXPERTS * capacity, model_width), jnp.bfloat16).at[slot_index].set(repeated)
    outgoing = buffer.reshape(seq_count, EXPERTS // seq_count, capacity, model_width)
    hidden = jnp.einsum(
        "secd,edf->secf",
        lax.all_to_all(outgoing, "seq", split_axis=0, concat_axis=0, tiled=True),
        expert_in,
        preferred_element_type=jnp.float32,
    )
    ff_width = expert_out.shape[1]
    active = (jax.nn.silu(hidden[..., :ff_width]) * hidden[..., ff_width:]).astype(jnp.bfloat16)
    results = jnp.einsum(
        "secf,efd->secd", active, expert_out, preferred_element_type=jnp.float32
    ).astype(jnp.bfloat16)
    returned = lax.all_to_all(results, "seq", split_axis=0, concat_axis=0, tiled=True)
    fetched = (
        returned.reshape(EXPERTS * capacity, model_width)[slot_index]
        .astype(jnp.float32)
        .reshape(rows_dev, top_count, model_width)
    )
    combined = jnp.sum(fetched * gate_values[..., None], axis=1)
    layer_out = (moe_in.astype(jnp.float32) + combined).astype(jnp.bfloat16)
    return (layer_out[:pre_share], layer_out[pre_share:])


def solution(mesh):
    return jax.shard_map(
        shards,
        mesh=mesh,
        in_specs=(
            P("seq", None),
            P(("seq", "tp"), None),
            P(),
            P(None, "tp"),
            P(None, "tp", None),
            P("tp", None),
            P(None, "seq", "tp", None),
            P(),
            P(),
            P(),
            P("seq", None, None),
            P("seq", None, None),
            P(("seq", "tp"), None),
            P(("seq", "tp"), None),
        ),
        out_specs=(P(("seq", "tp"), None), P(("seq", "tp"), None)),
        check_vma=False,
    )
```

```python
import math

import jax
import jax.numpy as jnp
from jax import lax
from jax.sharding import PartitionSpec as P

EXPERTS = 32
SPAN = 2048


eps_norm = 1e-05
rope_base = 10000.0
masked_score = -1e30
key_block = 512


def rms_norm(values, scales):
    floats = values.astype(jnp.float32)
    factor = lax.rsqrt(jnp.mean(floats * floats, axis=-1, keepdims=True) + eps_norm)
    return (floats * factor * scales.astype(jnp.float32)).astype(jnp.bfloat16)


def apply_rotary(values, token_positions):
    half_dim = values.shape[-1] // 2
    frequency = rope_base ** (-2.0 * jnp.arange(half_dim, dtype=jnp.float32) / values.shape[-1])
    angles = token_positions.astype(jnp.float32)[:, None] * frequency[None, :]
    cosine = jnp.cos(angles)[:, None, :]
    sine_part = jnp.sin(angles)[:, None, :]
    first_half = values[..., :half_dim]
    second_half = values[..., half_dim:]
    return jnp.concatenate(
        [
            first_half * cosine - second_half * sine_part,
            second_half * cosine + first_half * sine_part,
        ],
        axis=-1,
    )


def span_tables(span_tenant):
    span_count = span_tenant.shape[0]
    ordinal = jnp.arange(span_count, dtype=jnp.int32)
    same_tenant = span_tenant[:, None] == span_tenant[None, :]
    earlier = ordinal[None, :] < ordinal[:, None]
    return jnp.sum(jnp.where(same_tenant & earlier, 1, 0), axis=1).astype(jnp.int32)


def token_tables(token_index, span_tenant, before):
    span_count = span_tenant.shape[0]
    span_index = token_index // SPAN
    onehot = span_index[:, None] == jnp.arange(span_count, dtype=jnp.int32)[None, :]
    tenant = jnp.sum(jnp.where(onehot, span_tenant[None, :], 0), axis=1)
    offset = jnp.sum(jnp.where(onehot, before[None, :], 0), axis=1)
    return (tenant, offset * SPAN + token_index % SPAN)


def attend_keys(fold_state, keyvalue_rows, visible, query_matrix, score_scale):
    run_max, run_total, run_acc = fold_state
    head_dim = keyvalue_rows.shape[-1] // 2
    scores = (
        jnp.einsum(
            "qhgd,khd->qhgk",
            query_matrix,
            keyvalue_rows[..., :head_dim],
            preferred_element_type=jnp.float32,
        )
        * score_scale
    )
    mask_full = visible[:, None, None, :]
    scores = jnp.where(mask_full, scores, masked_score)
    new_max = jnp.maximum(run_max, jnp.max(scores, axis=-1))
    weights_exp = jnp.where(mask_full, jnp.exp(scores - new_max[..., None]), 0.0)
    factor = jnp.exp(run_max - new_max)
    new_total = run_total * factor + jnp.sum(weights_exp, axis=-1)
    new_acc = run_acc * factor[..., None] + jnp.einsum(
        "qhgk,khd->qhgd",
        weights_exp.astype(jnp.bfloat16),
        keyvalue_rows[..., head_dim:],
        preferred_element_type=jnp.float32,
    )
    return (new_max, new_total, new_acc)


def swap_partner(values, axis_name, distance):
    count = lax.axis_size(axis_name)
    pairs = [(i, i ^ distance) for i in range(count)]
    return lax.ppermute(values, axis_name, pairs)


def gather_blocks(block, axis_name, distances):
    index = lax.axis_index(axis_name)
    stacked = block
    done = []
    for distance in distances:
        theirs = swap_partner(stacked, axis_name, distance)
        upper = (index // distance) % 2 == 1
        low = jnp.where(upper, theirs, stacked)
        high = jnp.where(upper, stacked, theirs)
        place = sum(1 for d in done if d > distance)
        stacked = jnp.stack([low, high], axis=place)
        done.append(distance)
    return stacked.reshape((-1,) + block.shape[1:])


def scatter_blocks(values, axis_name, distances, combine, send_type=None):
    count = lax.axis_size(axis_name)
    index = lax.axis_index(axis_name)
    levels = count.bit_length() - 1
    rows = values.shape[0] // count
    stacked = values.reshape((2,) * levels + (rows,) + values.shape[1:])
    remaining = [count >> (j + 1) for j in range(levels)]
    for distance in distances:
        place = remaining.index(distance)
        low = lax.index_in_dim(stacked, 0, place, keepdims=False)
        high = lax.index_in_dim(stacked, 1, place, keepdims=False)
        upper = (index // distance) % 2 == 1
        keep = jnp.where(upper, high, low)
        send = jnp.where(upper, low, high)
        if send_type is not None:
            send = send.astype(send_type)
        received = swap_partner(send, axis_name, distance).astype(keep.dtype)
        stacked = combine(keep, received)
        remaining.pop(place)
    return stacked


def exchange_all(chunks, axis_name):
    count = lax.axis_size(axis_name)
    index = lax.axis_index(axis_name)
    pieces = [lax.dynamic_index_in_dim(chunks, index, 0, keepdims=False)]
    for shift in range(1, count):
        outgoing = lax.dynamic_index_in_dim(chunks, (index - shift) % count, 0, keepdims=False)
        pairs = [(i, (i - shift) % count) for i in range(count)]
        pieces.append(lax.ppermute(outgoing, axis_name, pairs))
    return jnp.roll(jnp.stack(pieces), index, axis=0)


def gather_direct(block, axis_name):
    count = lax.axis_size(axis_name)
    index = lax.axis_index(axis_name)
    pieces = [block]
    for shift in range(1, count):
        pairs = [(i, (i - shift) % count) for i in range(count)]
        pieces.append(lax.ppermute(block, axis_name, pairs))
    gathered = jnp.roll(jnp.stack(pieces), index, axis=0)
    return gathered.reshape((-1,) + block.shape[1:])


def scatter_direct(values, axis_name, send_type=None):
    count = lax.axis_size(axis_name)
    chunks = values.reshape((count, values.shape[0] // count) + values.shape[1:])
    if send_type is not None:
        chunks = chunks.astype(send_type)
    return exchange_all(chunks, axis_name).astype(values.dtype)


def add_parts(first, second):
    return first + second


def merge_softmax(first, second):
    first_max, second_max = first[..., -1], second[..., -1]
    top = jnp.maximum(first_max, second_max)
    first_scale = jnp.exp(first_max - top)[..., None]
    second_scale = jnp.exp(second_max - top)[..., None]
    body = first[..., :-1] * first_scale + second[..., :-1] * second_scale
    return jnp.concatenate([body, top[..., None]], axis=-1)


def shards(
    prefill_states,
    decode_states,
    attn_gain,
    query_weight,
    keyvalue_weight,
    output_weight,
    cache_keyval,
    cached_length,
    span_tenant,
    ffn_gain,
    expert_in,
    expert_out,
    routes,
    gate_values,
):
    seq_count = lax.axis_size("seq")
    tp_count = lax.axis_size("tp")
    seq_index = lax.axis_index("seq")
    tp_index = lax.axis_index("tp")
    pre_local, model_width = prefill_states.shape
    dec_local = decode_states.shape[0]
    heads_kv = keyvalue_weight.shape[1]
    head_dim = keyvalue_weight.shape[2] // 2
    heads_q = query_weight.shape[1] // head_dim
    query_group_count = heads_q // heads_kv
    score_scale = head_dim ** (-0.5)
    pre_share = pre_local // tp_count
    normalised_input = rms_norm(prefill_states, attn_gain)
    query_matrix = jnp.dot(
        normalised_input, query_weight, preferred_element_type=jnp.float32
    ).reshape(pre_local, heads_q, head_dim)
    keyvalue_rows = jnp.dot(
        normalised_input,
        keyvalue_weight.reshape(model_width, heads_kv * 2 * head_dim),
        preferred_element_type=jnp.float32,
    ).reshape(pre_local, heads_kv, 2 * head_dim)
    before = span_tables(span_tenant)
    token_index = seq_index * pre_local + jnp.arange(pre_local, dtype=jnp.int32)
    tenant, token_positions = token_tables(token_index, span_tenant, before)
    query_matrix = (
        apply_rotary(query_matrix, token_positions)
        .astype(jnp.bfloat16)
        .reshape(pre_local, heads_kv, query_group_count, head_dim)
    )
    rotated_keys = apply_rotary(keyvalue_rows[..., :head_dim], token_positions).astype(jnp.bfloat16)
    local_keyvals = jnp.concatenate(
        [rotated_keys, keyvalue_rows[..., head_dim:].astype(jnp.bfloat16)], axis=-1
    )
    seq_near_first = [1 << j for j in range(seq_count.bit_length() - 1)]
    key_piece = gather_blocks(local_keyvals, "seq", seq_near_first[::-1])
    piece_rows = key_piece.shape[0]
    block_len = math.gcd(piece_rows, key_block)
    blocks = key_piece.reshape(piece_rows // block_len, block_len, heads_kv, 2 * head_dim)
    query_count = pre_local * query_group_count
    query_rows = query_matrix.transpose(1, 0, 2, 3).reshape(heads_kv, query_count, head_dim)
    row_token = jnp.repeat(token_index, query_group_count)
    row_tenant = jnp.repeat(tenant, query_group_count)
    start_state = (
        jnp.full((heads_kv, query_count), masked_score, jnp.float32),
        jnp.zeros((heads_kv, query_count), jnp.float32),
        jnp.zeros((heads_kv, query_count, head_dim), jnp.float32),
    )

    def one_block(run_state, block_item):
        block_number, block_vals = block_item
        key_index = block_number * block_len + jnp.arange(block_len, dtype=jnp.int32)
        key_tenant = token_tables(key_index, span_tenant, before)[0]
        token_visible = (tenant[:, None] == key_tenant[None, :]) & (
            token_index[:, None] >= key_index[None, :]
        )

        def attend(state):
            run_max, run_total, run_acc = state
            visible = (row_tenant[:, None] == key_tenant[None, :]) & (
                row_token[:, None] >= key_index[None, :]
            )
            scores = (
                jnp.einsum(
                    "hqd,khd->hqk",
                    query_rows,
                    block_vals[..., :head_dim],
                    preferred_element_type=jnp.float32,
                )
                * score_scale
            )
            scores = jnp.where(visible[None], scores, masked_score)
            new_max = jnp.maximum(run_max, jnp.max(scores, axis=-1))
            weights_exp = jnp.where(visible[None], jnp.exp(scores - new_max[..., None]), 0.0)
            factor = jnp.exp(run_max - new_max)
            new_total = run_total * factor + jnp.sum(weights_exp, axis=-1)
            new_acc = run_acc * factor[..., None] + jnp.einsum(
                "hqk,khd->hqd",
                weights_exp.astype(jnp.bfloat16),
                block_vals[..., head_dim:],
                preferred_element_type=jnp.float32,
            )
            return (new_max, new_total, new_acc)

        run_state = lax.cond(jnp.any(token_visible), attend, lambda state: state, run_state)
        return (run_state, None)

    run_max, run_total, run_acc = lax.scan(
        one_block, start_state, (jnp.arange(piece_rows // block_len, dtype=jnp.int32), blocks)
    )[0]
    attended = (
        (run_acc / run_total[..., None])
        .astype(jnp.bfloat16)
        .reshape(heads_kv, pre_local, query_group_count, head_dim)
        .transpose(1, 0, 2, 3)
        .reshape(pre_local, heads_q * head_dim)
    )
    prefill_part = jnp.dot(attended, output_weight, preferred_element_type=jnp.float32)
    prefill_sum = jnp.sum(scatter_direct(prefill_part, "tp", send_type=jnp.bfloat16), axis=0)
    group_states = gather_direct(decode_states, "tp")
    group_rows = group_states.shape[0]
    group_lengths = lax.dynamic_slice_in_dim(cached_length, seq_index * group_rows, group_rows, 0)
    decode_normalised = rms_norm(group_states, attn_gain)
    group_queries = jnp.dot(
        decode_normalised, query_weight, preferred_element_type=jnp.float32
    ).reshape(group_rows, heads_q, head_dim)
    group_queries = (
        apply_rotary(group_queries, group_lengths)
        .astype(jnp.bfloat16)
        .reshape(group_rows, heads_kv, query_group_count, head_dim)
    )
    decode_keyvalues = jnp.dot(
        decode_normalised,
        keyvalue_weight.reshape(model_width, heads_kv * 2 * head_dim),
        preferred_element_type=jnp.float32,
    ).reshape(group_rows, heads_kv, 2 * head_dim)
    new_keys = apply_rotary(decode_keyvalues[..., :head_dim], group_lengths).astype(jnp.bfloat16)
    new_vals = decode_keyvalues[..., head_dim:].astype(jnp.bfloat16)
    decode_queries = gather_direct(group_queries, "seq")
    cache_local = cache_keyval.shape[1]
    cache_pos = seq_index * cache_local + jnp.arange(cache_local, dtype=jnp.int32)
    visible = (cache_pos[None, :] < cached_length[:, None])[:, None, None, :]
    scores = (
        jnp.einsum(
            "bhgd,bkhd->bhgk",
            decode_queries,
            cache_keyval[..., :head_dim],
            preferred_element_type=jnp.float32,
        )
        * score_scale
    )
    scores = jnp.where(visible, scores, masked_score)
    local_max = jnp.max(scores, axis=-1)
    weights_exp = jnp.where(visible, jnp.exp(scores - local_max[..., None]), 0.0)
    local_total = jnp.sum(weights_exp, axis=-1)
    local_acc = jnp.einsum(
        "bhgk,bkhd->bhgd",
        weights_exp.astype(jnp.bfloat16),
        cache_keyval[..., head_dim:],
        preferred_element_type=jnp.float32,
    )
    packed = jnp.concatenate([local_acc, local_total[..., None], local_max[..., None]], axis=-1)
    parts = scatter_direct(packed, "seq")
    part_max = parts[..., -1]
    merged_max = jnp.max(part_max, axis=0)
    part_scale = jnp.exp(part_max - merged_max[None])
    merged = jnp.sum(parts[..., :-1] * part_scale[..., None], axis=0)
    merged_acc = merged[..., :head_dim]
    merged_total = merged[..., head_dim]
    own_score = (
        jnp.sum(
            group_queries.astype(jnp.float32) * new_keys.astype(jnp.float32)[:, :, None, :],
            axis=-1,
        )
        * score_scale
    )
    final_max = jnp.maximum(merged_max, own_score)
    rescale = jnp.exp(merged_max - final_max)
    own_exp = jnp.exp(own_score - final_max)
    final_total = merged_total * rescale + own_exp
    own_rounded = lax.optimization_barrier(own_exp.astype(jnp.bfloat16)).astype(jnp.float32)
    final_acc = (
        merged_acc * rescale[..., None]
        + own_rounded[..., None] * new_vals.astype(jnp.float32)[:, :, None, :]
    )
    decode_attended = (
        (final_acc / final_total[..., None])
        .astype(jnp.bfloat16)
        .reshape(group_rows, heads_q * head_dim)
    )
    decode_part = jnp.dot(decode_attended, output_weight, preferred_element_type=jnp.float32)
    decode_sum = jnp.sum(scatter_direct(decode_part, "tp"), axis=0)
    own_states = lax.dynamic_slice_in_dim(prefill_states, tp_index * pre_share, pre_share, 0)
    prefill_h = (own_states.astype(jnp.float32) + prefill_sum).astype(jnp.bfloat16)
    decode_h = (decode_states.astype(jnp.float32) + decode_sum).astype(jnp.bfloat16)
    moe_in = jnp.concatenate([prefill_h, decode_h], axis=0)
    normed_moe = rms_norm(moe_in, ffn_gain)
    rows_dev, top_count = routes.shape
    capacity = 2 * ((rows_dev * top_count + EXPERTS - 1) // EXPERTS)
    flat_routes = routes.reshape(rows_dev * top_count)
    expert_ids = jnp.arange(EXPERTS, dtype=jnp.int32)
    onehot = (flat_routes[:, None] == expert_ids[None, :]).astype(jnp.int32)
    slot_rank = jnp.sum(jnp.cumsum(onehot, axis=0) * onehot, axis=1) - 1
    slot_index = flat_routes * capacity + slot_rank
    repeated = jnp.repeat(normed_moe, top_count, axis=0)
    buffer = jnp.zeros((EXPERTS * capacity, model_width), jnp.bfloat16).at[slot_index].set(repeated)
    outgoing = buffer.reshape(seq_count, EXPERTS // seq_count, capacity, model_width)
    hidden = jnp.einsum(
        "secd,edf->secf",
        exchange_all(outgoing, "seq"),
        expert_in,
        preferred_element_type=jnp.float32,
    )
    ff_width = expert_out.shape[1]
    active = (jax.nn.silu(hidden[..., :ff_width]) * hidden[..., ff_width:]).astype(jnp.bfloat16)
    results = jnp.einsum(
        "secf,efd->secd", active, expert_out, preferred_element_type=jnp.float32
    ).astype(jnp.bfloat16)
    returned = exchange_all(results, "seq")
    fetched = (
        returned.reshape(EXPERTS * capacity, model_width)[slot_index]
        .astype(jnp.float32)
        .reshape(rows_dev, top_count, model_width)
    )
    combined = jnp.sum(fetched * gate_values[..., None], axis=1)
    layer_out = (moe_in.astype(jnp.float32) + combined).astype(jnp.bfloat16)
    return (layer_out[:pre_share], layer_out[pre_share:])


def solution(mesh):
    return jax.shard_map(
        shards,
        mesh=mesh,
        in_specs=(
            P("seq", None),
            P(("seq", "tp"), None),
            P(),
            P(None, "tp"),
            P(None, "tp", None),
            P("tp", None),
            P(None, "seq", "tp", None),
            P(),
            P(),
            P(),
            P("seq", None, None),
            P("seq", None, None),
            P(("seq", "tp"), None),
            P(("seq", "tp"), None),
        ),
        out_specs=(P(("seq", "tp"), None), P(("seq", "tp"), None)),
        check_vma=False,
    )
```

```python
import math

import jax
import jax.numpy as jnp
from jax import lax
from jax.sharding import PartitionSpec as P

EXPERTS = 32
SPAN = 2048


eps_norm = 1e-05
rope_base = 10000.0
masked_score = -1e30
key_block = 512


def rms_norm(values, scales):
    floats = values.astype(jnp.float32)
    factor = lax.rsqrt(jnp.mean(floats * floats, axis=-1, keepdims=True) + eps_norm)
    return (floats * factor * scales.astype(jnp.float32)).astype(jnp.bfloat16)


def apply_rotary(values, token_positions):
    half_dim = values.shape[-1] // 2
    frequency = rope_base ** (-2.0 * jnp.arange(half_dim, dtype=jnp.float32) / values.shape[-1])
    angles = token_positions.astype(jnp.float32)[:, None] * frequency[None, :]
    cosine = jnp.cos(angles)[:, None, :]
    sine_part = jnp.sin(angles)[:, None, :]
    first_half = values[..., :half_dim]
    second_half = values[..., half_dim:]
    return jnp.concatenate(
        [
            first_half * cosine - second_half * sine_part,
            second_half * cosine + first_half * sine_part,
        ],
        axis=-1,
    )


def span_tables(span_tenant):
    span_count = span_tenant.shape[0]
    ordinal = jnp.arange(span_count, dtype=jnp.int32)
    same_tenant = span_tenant[:, None] == span_tenant[None, :]
    earlier = ordinal[None, :] < ordinal[:, None]
    return jnp.sum(jnp.where(same_tenant & earlier, 1, 0), axis=1).astype(jnp.int32)


def token_tables(token_index, span_tenant, before):
    span_count = span_tenant.shape[0]
    span_index = token_index // SPAN
    onehot = span_index[:, None] == jnp.arange(span_count, dtype=jnp.int32)[None, :]
    tenant = jnp.sum(jnp.where(onehot, span_tenant[None, :], 0), axis=1)
    offset = jnp.sum(jnp.where(onehot, before[None, :], 0), axis=1)
    return (tenant, offset * SPAN + token_index % SPAN)


def attend_keys(fold_state, keyvalue_rows, visible, query_matrix, score_scale):
    run_max, run_total, run_acc = fold_state
    head_dim = keyvalue_rows.shape[-1] // 2
    scores = (
        jnp.einsum(
            "qhgd,khd->qhgk",
            query_matrix,
            keyvalue_rows[..., :head_dim],
            preferred_element_type=jnp.float32,
        )
        * score_scale
    )
    mask_full = visible[:, None, None, :]
    scores = jnp.where(mask_full, scores, masked_score)
    new_max = jnp.maximum(run_max, jnp.max(scores, axis=-1))
    weights_exp = jnp.where(mask_full, jnp.exp(scores - new_max[..., None]), 0.0)
    factor = jnp.exp(run_max - new_max)
    new_total = run_total * factor + jnp.sum(weights_exp, axis=-1)
    new_acc = run_acc * factor[..., None] + jnp.einsum(
        "qhgk,khd->qhgd",
        weights_exp.astype(jnp.bfloat16),
        keyvalue_rows[..., head_dim:],
        preferred_element_type=jnp.float32,
    )
    return (new_max, new_total, new_acc)


def swap_partner(values, axis_name, distance):
    count = lax.axis_size(axis_name)
    pairs = [(i, i ^ distance) for i in range(count)]
    return lax.ppermute(values, axis_name, pairs)


def gather_blocks(block, axis_name, distances):
    index = lax.axis_index(axis_name)
    stacked = block
    done = []
    for distance in distances:
        theirs = swap_partner(stacked, axis_name, distance)
        upper = (index // distance) % 2 == 1
        low = jnp.where(upper, theirs, stacked)
        high = jnp.where(upper, stacked, theirs)
        place = sum(1 for d in done if d > distance)
        stacked = jnp.stack([low, high], axis=place)
        done.append(distance)
    return stacked.reshape((-1,) + block.shape[1:])


def scatter_blocks(values, axis_name, distances, combine, send_type=None):
    count = lax.axis_size(axis_name)
    index = lax.axis_index(axis_name)
    levels = count.bit_length() - 1
    rows = values.shape[0] // count
    stacked = values.reshape((2,) * levels + (rows,) + values.shape[1:])
    remaining = [count >> (j + 1) for j in range(levels)]
    for distance in distances:
        place = remaining.index(distance)
        low = lax.index_in_dim(stacked, 0, place, keepdims=False)
        high = lax.index_in_dim(stacked, 1, place, keepdims=False)
        upper = (index // distance) % 2 == 1
        keep = jnp.where(upper, high, low)
        send = jnp.where(upper, low, high)
        if send_type is not None:
            send = send.astype(send_type)
        received = swap_partner(send, axis_name, distance).astype(keep.dtype)
        stacked = combine(keep, received)
        remaining.pop(place)
    return stacked


def add_parts(first, second):
    return first + second


def merge_softmax(first, second):
    first_max, second_max = first[..., -1], second[..., -1]
    top = jnp.maximum(first_max, second_max)
    first_scale = jnp.exp(first_max - top)[..., None]
    second_scale = jnp.exp(second_max - top)[..., None]
    body = first[..., :-1] * first_scale + second[..., :-1] * second_scale
    return jnp.concatenate([body, top[..., None]], axis=-1)


def shards(
    prefill_states,
    decode_states,
    attn_gain,
    query_weight,
    keyvalue_weight,
    output_weight,
    cache_keyval,
    cached_length,
    span_tenant,
    ffn_gain,
    expert_in,
    expert_out,
    routes,
    gate_values,
):
    seq_count = lax.axis_size("seq")
    tp_count = lax.axis_size("tp")
    seq_index = lax.axis_index("seq")
    tp_index = lax.axis_index("tp")
    pre_local, model_width = prefill_states.shape
    dec_local = decode_states.shape[0]
    heads_kv = keyvalue_weight.shape[1]
    head_dim = keyvalue_weight.shape[2] // 2
    heads_q = query_weight.shape[1] // head_dim
    query_group_count = heads_q // heads_kv
    score_scale = head_dim ** (-0.5)
    pre_share = pre_local // tp_count
    normalised_input = rms_norm(prefill_states, attn_gain)
    query_matrix = jnp.dot(
        normalised_input, query_weight, preferred_element_type=jnp.float32
    ).reshape(pre_local, heads_q, head_dim)
    keyvalue_rows = jnp.dot(
        normalised_input,
        keyvalue_weight.reshape(model_width, heads_kv * 2 * head_dim),
        preferred_element_type=jnp.float32,
    ).reshape(pre_local, heads_kv, 2 * head_dim)
    before = span_tables(span_tenant)
    token_index = seq_index * pre_local + jnp.arange(pre_local, dtype=jnp.int32)
    tenant, token_positions = token_tables(token_index, span_tenant, before)
    query_matrix = (
        apply_rotary(query_matrix, token_positions)
        .astype(jnp.bfloat16)
        .reshape(pre_local, heads_kv, query_group_count, head_dim)
    )
    rotated_keys = apply_rotary(keyvalue_rows[..., :head_dim], token_positions).astype(jnp.bfloat16)
    local_keyvals = jnp.concatenate(
        [rotated_keys, keyvalue_rows[..., head_dim:].astype(jnp.bfloat16)], axis=-1
    )
    seq_near_first = [1 << j for j in range(seq_count.bit_length() - 1)]
    key_piece = gather_blocks(local_keyvals, "seq", seq_near_first[::-1])
    piece_rows = key_piece.shape[0]
    block_len = math.gcd(piece_rows, key_block)
    blocks = key_piece.reshape(piece_rows // block_len, block_len, heads_kv, 2 * head_dim)
    query_count = pre_local * query_group_count
    query_rows = query_matrix.transpose(1, 0, 2, 3).reshape(heads_kv, query_count, head_dim)
    row_token = jnp.repeat(token_index, query_group_count)
    row_tenant = jnp.repeat(tenant, query_group_count)
    start_state = (
        jnp.full((heads_kv, query_count), masked_score, jnp.float32),
        jnp.zeros((heads_kv, query_count), jnp.float32),
        jnp.zeros((heads_kv, query_count, head_dim), jnp.float32),
    )

    def one_block(run_state, block_item):
        block_number, block_vals = block_item
        key_index = block_number * block_len + jnp.arange(block_len, dtype=jnp.int32)
        key_tenant = token_tables(key_index, span_tenant, before)[0]
        token_visible = (tenant[:, None] == key_tenant[None, :]) & (
            token_index[:, None] >= key_index[None, :]
        )

        def attend(state):
            run_max, run_total, run_acc = state
            visible = (row_tenant[:, None] == key_tenant[None, :]) & (
                row_token[:, None] >= key_index[None, :]
            )
            scores = (
                jnp.einsum(
                    "hqd,khd->hqk",
                    query_rows,
                    block_vals[..., :head_dim],
                    preferred_element_type=jnp.float32,
                )
                * score_scale
            )
            scores = jnp.where(visible[None], scores, masked_score)
            new_max = jnp.maximum(run_max, jnp.max(scores, axis=-1))
            weights_exp = jnp.where(visible[None], jnp.exp(scores - new_max[..., None]), 0.0)
            factor = jnp.exp(run_max - new_max)
            new_total = run_total * factor + jnp.sum(weights_exp, axis=-1)
            new_acc = run_acc * factor[..., None] + jnp.einsum(
                "hqk,khd->hqd",
                weights_exp.astype(jnp.bfloat16),
                block_vals[..., head_dim:],
                preferred_element_type=jnp.float32,
            )
            return (new_max, new_total, new_acc)

        run_state = lax.cond(jnp.any(token_visible), attend, lambda state: state, run_state)
        return (run_state, None)

    run_max, run_total, run_acc = lax.scan(
        one_block, start_state, (jnp.arange(piece_rows // block_len, dtype=jnp.int32), blocks)
    )[0]
    attended = (
        (run_acc / run_total[..., None])
        .astype(jnp.bfloat16)
        .reshape(heads_kv, pre_local, query_group_count, head_dim)
        .transpose(1, 0, 2, 3)
        .reshape(pre_local, heads_q * head_dim)
    )
    prefill_part = jnp.dot(attended, output_weight, preferred_element_type=jnp.float32)
    tp_near_first = [1 << j for j in range(tp_count.bit_length() - 1)]
    prefill_sum = scatter_blocks(
        prefill_part, "tp", tp_near_first, add_parts, send_type=jnp.bfloat16
    )
    group_states = gather_blocks(decode_states, "tp", tp_near_first[::-1])
    group_rows = group_states.shape[0]
    group_lengths = lax.dynamic_slice_in_dim(cached_length, seq_index * group_rows, group_rows, 0)
    decode_normalised = rms_norm(group_states, attn_gain)
    group_queries = jnp.dot(
        decode_normalised, query_weight, preferred_element_type=jnp.float32
    ).reshape(group_rows, heads_q, head_dim)
    group_queries = (
        apply_rotary(group_queries, group_lengths)
        .astype(jnp.bfloat16)
        .reshape(group_rows, heads_kv, query_group_count, head_dim)
    )
    decode_keyvalues = jnp.dot(
        decode_normalised,
        keyvalue_weight.reshape(model_width, heads_kv * 2 * head_dim),
        preferred_element_type=jnp.float32,
    ).reshape(group_rows, heads_kv, 2 * head_dim)
    new_keys = apply_rotary(decode_keyvalues[..., :head_dim], group_lengths).astype(jnp.bfloat16)
    new_vals = decode_keyvalues[..., head_dim:].astype(jnp.bfloat16)
    decode_queries = gather_blocks(group_queries, "seq", seq_near_first[::-1])
    cache_local = cache_keyval.shape[1]
    cache_pos = seq_index * cache_local + jnp.arange(cache_local, dtype=jnp.int32)
    visible = (cache_pos[None, :] < cached_length[:, None])[:, None, None, :]
    scores = (
        jnp.einsum(
            "bhgd,bkhd->bhgk",
            decode_queries,
            cache_keyval[..., :head_dim],
            preferred_element_type=jnp.float32,
        )
        * score_scale
    )
    scores = jnp.where(visible, scores, masked_score)
    local_max = jnp.max(scores, axis=-1)
    weights_exp = jnp.where(visible, jnp.exp(scores - local_max[..., None]), 0.0)
    local_total = jnp.sum(weights_exp, axis=-1)
    local_acc = jnp.einsum(
        "bhgk,bkhd->bhgd",
        weights_exp.astype(jnp.bfloat16),
        cache_keyval[..., head_dim:],
        preferred_element_type=jnp.float32,
    )
    packed = jnp.concatenate([local_acc, local_total[..., None], local_max[..., None]], axis=-1)
    merged = scatter_blocks(packed, "seq", seq_near_first, merge_softmax)
    merged_max = merged[..., head_dim + 1]
    merged_acc = merged[..., :head_dim]
    merged_total = merged[..., head_dim]
    own_score = (
        jnp.sum(
            group_queries.astype(jnp.float32) * new_keys.astype(jnp.float32)[:, :, None, :],
            axis=-1,
        )
        * score_scale
    )
    final_max = jnp.maximum(merged_max, own_score)
    rescale = jnp.exp(merged_max - final_max)
    own_exp = jnp.exp(own_score - final_max)
    final_total = merged_total * rescale + own_exp
    own_rounded = lax.optimization_barrier(own_exp.astype(jnp.bfloat16)).astype(jnp.float32)
    final_acc = (
        merged_acc * rescale[..., None]
        + own_rounded[..., None] * new_vals.astype(jnp.float32)[:, :, None, :]
    )
    decode_attended = (
        (final_acc / final_total[..., None])
        .astype(jnp.bfloat16)
        .reshape(group_rows, heads_q * head_dim)
    )
    decode_part = jnp.dot(decode_attended, output_weight, preferred_element_type=jnp.float32)
    decode_sum = scatter_blocks(decode_part, "tp", tp_near_first, add_parts)
    own_states = lax.dynamic_slice_in_dim(prefill_states, tp_index * pre_share, pre_share, 0)
    prefill_h = (own_states.astype(jnp.float32) + prefill_sum).astype(jnp.bfloat16)
    decode_h = (decode_states.astype(jnp.float32) + decode_sum).astype(jnp.bfloat16)
    moe_in = jnp.concatenate([prefill_h, decode_h], axis=0)
    normed_moe = rms_norm(moe_in, ffn_gain)
    rows_dev, top_count = routes.shape
    capacity = 2 * ((rows_dev * top_count + EXPERTS - 1) // EXPERTS)
    flat_routes = routes.reshape(rows_dev * top_count)
    expert_ids = jnp.arange(EXPERTS, dtype=jnp.int32)
    onehot = (flat_routes[:, None] == expert_ids[None, :]).astype(jnp.int32)
    slot_rank = jnp.sum(jnp.cumsum(onehot, axis=0) * onehot, axis=1) - 1
    slot_index = flat_routes * capacity + slot_rank
    repeated = jnp.repeat(normed_moe, top_count, axis=0)
    buffer = jnp.zeros((EXPERTS * capacity, model_width), jnp.bfloat16).at[slot_index].set(repeated)
    outgoing = buffer.reshape(seq_count, EXPERTS // seq_count, capacity, model_width)
    hidden = jnp.einsum(
        "secd,edf->secf",
        lax.all_to_all(outgoing, "seq", split_axis=0, concat_axis=0, tiled=True),
        expert_in,
        preferred_element_type=jnp.float32,
    )
    ff_width = expert_out.shape[1]
    active = (jax.nn.silu(hidden[..., :ff_width]) * hidden[..., ff_width:]).astype(jnp.bfloat16)
    results = jnp.einsum(
        "secf,efd->secd", active, expert_out, preferred_element_type=jnp.float32
    ).astype(jnp.bfloat16)
    returned = lax.all_to_all(results, "seq", split_axis=0, concat_axis=0, tiled=True)
    fetched = (
        returned.reshape(EXPERTS * capacity, model_width)[slot_index]
        .astype(jnp.float32)
        .reshape(rows_dev, top_count, model_width)
    )
    combined = jnp.sum(fetched * gate_values[..., None], axis=1)
    layer_out = (moe_in.astype(jnp.float32) + combined).astype(jnp.bfloat16)
    return (layer_out[:pre_share], layer_out[pre_share:])


def solution(mesh):
    return jax.shard_map(
        shards,
        mesh=mesh,
        in_specs=(
            P("seq", None),
            P(("seq", "tp"), None),
            P(),
            P(None, "tp"),
            P(None, "tp", None),
            P("tp", None),
            P(None, "seq", "tp", None),
            P(),
            P(),
            P(),
            P("seq", None, None),
            P("seq", None, None),
            P(("seq", "tp"), None),
            P(("seq", "tp"), None),
        ),
        out_specs=(P(("seq", "tp"), None), P(("seq", "tp"), None)),
        check_vma=False,
    )
```

```python
import math

import jax
import jax.numpy as jnp
from jax import lax
from jax.sharding import PartitionSpec as P

EXPERTS = 32
SPAN = 2048


eps_norm = 1e-05
rope_base = 10000.0
masked_score = -1e30
key_block = 512


def rms_norm(values, scales):
    floats = values.astype(jnp.float32)
    factor = lax.rsqrt(jnp.mean(floats * floats, axis=-1, keepdims=True) + eps_norm)
    return (floats * factor * scales.astype(jnp.float32)).astype(jnp.bfloat16)


def apply_rotary(values, token_positions):
    half_dim = values.shape[-1] // 2
    frequency = rope_base ** (-2.0 * jnp.arange(half_dim, dtype=jnp.float32) / values.shape[-1])
    angles = token_positions.astype(jnp.float32)[:, None] * frequency[None, :]
    cosine = jnp.cos(angles)[:, None, :]
    sine_part = jnp.sin(angles)[:, None, :]
    first_half = values[..., :half_dim]
    second_half = values[..., half_dim:]
    return jnp.concatenate(
        [
            first_half * cosine - second_half * sine_part,
            second_half * cosine + first_half * sine_part,
        ],
        axis=-1,
    )


def span_tables(span_tenant):
    span_count = span_tenant.shape[0]
    ordinal = jnp.arange(span_count, dtype=jnp.int32)
    same_tenant = span_tenant[:, None] == span_tenant[None, :]
    earlier = ordinal[None, :] < ordinal[:, None]
    return jnp.sum(jnp.where(same_tenant & earlier, 1, 0), axis=1).astype(jnp.int32)


def token_tables(token_index, span_tenant, before):
    span_count = span_tenant.shape[0]
    span_index = token_index // SPAN
    onehot = span_index[:, None] == jnp.arange(span_count, dtype=jnp.int32)[None, :]
    tenant = jnp.sum(jnp.where(onehot, span_tenant[None, :], 0), axis=1)
    offset = jnp.sum(jnp.where(onehot, before[None, :], 0), axis=1)
    return (tenant, offset * SPAN + token_index % SPAN)


def attend_keys(fold_state, keyvalue_rows, visible, query_matrix, score_scale):
    run_max, run_total, run_acc = fold_state
    head_dim = keyvalue_rows.shape[-1] // 2
    scores = (
        jnp.einsum(
            "qhgd,khd->qhgk",
            query_matrix,
            keyvalue_rows[..., :head_dim],
            preferred_element_type=jnp.float32,
        )
        * score_scale
    )
    mask_full = visible[:, None, None, :]
    scores = jnp.where(mask_full, scores, masked_score)
    new_max = jnp.maximum(run_max, jnp.max(scores, axis=-1))
    weights_exp = jnp.where(mask_full, jnp.exp(scores - new_max[..., None]), 0.0)
    factor = jnp.exp(run_max - new_max)
    new_total = run_total * factor + jnp.sum(weights_exp, axis=-1)
    new_acc = run_acc * factor[..., None] + jnp.einsum(
        "qhgk,khd->qhgd",
        weights_exp.astype(jnp.bfloat16),
        keyvalue_rows[..., head_dim:],
        preferred_element_type=jnp.float32,
    )
    return (new_max, new_total, new_acc)


def swap_partner(values, axis_name, distance):
    count = lax.axis_size(axis_name)
    pairs = [(i, i ^ distance) for i in range(count)]
    return lax.ppermute(values, axis_name, pairs)


def gather_blocks(block, axis_name, distances, hook=None):
    index = lax.axis_index(axis_name)
    stacked = block
    done = []
    for distance in distances:
        theirs = swap_partner(stacked, axis_name, distance)
        upper = (index // distance) % 2 == 1
        low = jnp.where(upper, theirs, stacked)
        high = jnp.where(upper, stacked, theirs)
        place = sum(1 for d in done if d > distance)
        stacked = jnp.stack([low, high], axis=place)
        done.append(distance)
        if hook is not None:
            stacked = hook(stacked)
    return stacked.reshape((-1,) + block.shape[1:])


def scatter_blocks(values, axis_name, distances, combine, send_type=None, hook=None):
    count = lax.axis_size(axis_name)
    index = lax.axis_index(axis_name)
    levels = count.bit_length() - 1
    rows = values.shape[0] // count
    stacked = values.reshape((2,) * levels + (rows,) + values.shape[1:])
    remaining = [count >> (j + 1) for j in range(levels)]
    for distance in distances:
        place = remaining.index(distance)
        low = lax.index_in_dim(stacked, 0, place, keepdims=False)
        high = lax.index_in_dim(stacked, 1, place, keepdims=False)
        upper = (index // distance) % 2 == 1
        keep = jnp.where(upper, high, low)
        send = jnp.where(upper, low, high)
        if send_type is not None:
            send = send.astype(send_type)
        received = swap_partner(send, axis_name, distance).astype(keep.dtype)
        stacked = combine(keep, received)
        remaining.pop(place)
        if hook is not None:
            stacked = hook(stacked)
    return stacked


def add_parts(first, second):
    return first + second


def merge_softmax(first, second):
    first_max, second_max = first[..., -1], second[..., -1]
    top = jnp.maximum(first_max, second_max)
    first_scale = jnp.exp(first_max - top)[..., None]
    second_scale = jnp.exp(second_max - top)[..., None]
    body = first[..., :-1] * first_scale + second[..., :-1] * second_scale
    return jnp.concatenate([body, top[..., None]], axis=-1)


def shards(
    prefill_states,
    decode_states,
    attn_gain,
    query_weight,
    keyvalue_weight,
    output_weight,
    cache_keyval,
    cached_length,
    span_tenant,
    ffn_gain,
    expert_in,
    expert_out,
    routes,
    gate_values,
):
    seq_count = lax.axis_size("seq")
    tp_count = lax.axis_size("tp")
    seq_index = lax.axis_index("seq")
    tp_index = lax.axis_index("tp")
    pre_local, model_width = prefill_states.shape
    dec_local = decode_states.shape[0]
    heads_kv = keyvalue_weight.shape[1]
    head_dim = keyvalue_weight.shape[2] // 2
    heads_q = query_weight.shape[1] // head_dim
    query_group_count = heads_q // heads_kv
    score_scale = head_dim ** (-0.5)
    pre_share = pre_local // tp_count
    normalised_input = rms_norm(prefill_states, attn_gain)
    query_matrix = jnp.dot(
        normalised_input, query_weight, preferred_element_type=jnp.float32
    ).reshape(pre_local, heads_q, head_dim)
    keyvalue_rows = jnp.dot(
        normalised_input,
        keyvalue_weight.reshape(model_width, heads_kv * 2 * head_dim),
        preferred_element_type=jnp.float32,
    ).reshape(pre_local, heads_kv, 2 * head_dim)
    before = span_tables(span_tenant)
    token_index = seq_index * pre_local + jnp.arange(pre_local, dtype=jnp.int32)
    tenant, token_positions = token_tables(token_index, span_tenant, before)
    query_matrix = (
        apply_rotary(query_matrix, token_positions)
        .astype(jnp.bfloat16)
        .reshape(pre_local, heads_kv, query_group_count, head_dim)
    )
    rotated_keys = apply_rotary(keyvalue_rows[..., :head_dim], token_positions).astype(jnp.bfloat16)
    local_keyvals = jnp.concatenate(
        [rotated_keys, keyvalue_rows[..., head_dim:].astype(jnp.bfloat16)], axis=-1
    )
    seq_near_first = [1 << j for j in range(seq_count.bit_length() - 1)]
    key_piece = gather_blocks(local_keyvals, "seq", seq_near_first[::-1])
    piece_rows = key_piece.shape[0]
    block_len = math.gcd(piece_rows, key_block)
    blocks = key_piece.reshape(piece_rows // block_len, block_len, heads_kv, 2 * head_dim)
    query_count = pre_local * query_group_count
    query_rows = query_matrix.transpose(1, 0, 2, 3).reshape(heads_kv, query_count, head_dim)
    row_token = jnp.repeat(token_index, query_group_count)
    row_tenant = jnp.repeat(tenant, query_group_count)
    start_state = (
        jnp.full((heads_kv, query_count), masked_score, jnp.float32),
        jnp.zeros((heads_kv, query_count), jnp.float32),
        jnp.zeros((heads_kv, query_count, head_dim), jnp.float32),
    )

    def one_block(run_state, block_item):
        block_number, block_vals = block_item
        key_index = block_number * block_len + jnp.arange(block_len, dtype=jnp.int32)
        key_tenant = token_tables(key_index, span_tenant, before)[0]
        token_visible = (tenant[:, None] == key_tenant[None, :]) & (
            token_index[:, None] >= key_index[None, :]
        )

        def attend(state):
            run_max, run_total, run_acc = state
            visible = (row_tenant[:, None] == key_tenant[None, :]) & (
                row_token[:, None] >= key_index[None, :]
            )
            scores = (
                jnp.einsum(
                    "hqd,khd->hqk",
                    query_rows,
                    block_vals[..., :head_dim],
                    preferred_element_type=jnp.float32,
                )
                * score_scale
            )
            scores = jnp.where(visible[None], scores, masked_score)
            new_max = jnp.maximum(run_max, jnp.max(scores, axis=-1))
            weights_exp = jnp.where(visible[None], jnp.exp(scores - new_max[..., None]), 0.0)
            factor = jnp.exp(run_max - new_max)
            new_total = run_total * factor + jnp.sum(weights_exp, axis=-1)
            new_acc = run_acc * factor[..., None] + jnp.einsum(
                "hqk,khd->hqd",
                weights_exp.astype(jnp.bfloat16),
                block_vals[..., head_dim:],
                preferred_element_type=jnp.float32,
            )
            return (new_max, new_total, new_acc)

        run_state = lax.cond(jnp.any(token_visible), attend, lambda state: state, run_state)
        return (run_state, None)

    block_total = piece_rows // block_len
    progress = {"next": 0, "state": start_state}

    def advance(count):
        def hook(value):
            for _ in range(count):
                number = progress["next"]
                if number < block_total:
                    progress["state"] = one_block(
                        progress["state"], (jnp.int32(number), blocks[number])
                    )[0]
                    progress["next"] = number + 1
            value, progress["state"] = lax.optimization_barrier((value, progress["state"]))
            return value

        return hook

    hook_counts = iter([1, 1, 1, 1, 2, 2, 2, 2, 2, 2])

    def next_hook(value):
        count = next(hook_counts, 0)
        return advance(count)(value) if count else value

    tp_near_first = [1 << j for j in range(tp_count.bit_length() - 1)]
    group_states = gather_blocks(decode_states, "tp", tp_near_first[::-1])
    group_rows = group_states.shape[0]
    group_lengths = lax.dynamic_slice_in_dim(cached_length, seq_index * group_rows, group_rows, 0)
    decode_normalised = rms_norm(group_states, attn_gain)
    group_queries = jnp.dot(
        decode_normalised, query_weight, preferred_element_type=jnp.float32
    ).reshape(group_rows, heads_q, head_dim)
    group_queries = (
        apply_rotary(group_queries, group_lengths)
        .astype(jnp.bfloat16)
        .reshape(group_rows, heads_kv, query_group_count, head_dim)
    )
    decode_keyvalues = jnp.dot(
        decode_normalised,
        keyvalue_weight.reshape(model_width, heads_kv * 2 * head_dim),
        preferred_element_type=jnp.float32,
    ).reshape(group_rows, heads_kv, 2 * head_dim)
    new_keys = apply_rotary(decode_keyvalues[..., :head_dim], group_lengths).astype(jnp.bfloat16)
    new_vals = decode_keyvalues[..., head_dim:].astype(jnp.bfloat16)
    decode_queries = gather_blocks(group_queries, "seq", seq_near_first[::-1], hook=next_hook)
    cache_local = cache_keyval.shape[1]
    cache_pos = seq_index * cache_local + jnp.arange(cache_local, dtype=jnp.int32)
    visible = (cache_pos[None, :] < cached_length[:, None])[:, None, None, :]
    scores = (
        jnp.einsum(
            "bhgd,bkhd->bhgk",
            decode_queries,
            cache_keyval[..., :head_dim],
            preferred_element_type=jnp.float32,
        )
        * score_scale
    )
    scores = jnp.where(visible, scores, masked_score)
    local_max = jnp.max(scores, axis=-1)
    weights_exp = jnp.where(visible, jnp.exp(scores - local_max[..., None]), 0.0)
    local_total = jnp.sum(weights_exp, axis=-1)
    local_acc = jnp.einsum(
        "bhgk,bkhd->bhgd",
        weights_exp.astype(jnp.bfloat16),
        cache_keyval[..., head_dim:],
        preferred_element_type=jnp.float32,
    )
    packed = jnp.concatenate([local_acc, local_total[..., None], local_max[..., None]], axis=-1)
    merged = scatter_blocks(packed, "seq", seq_near_first, merge_softmax, hook=next_hook)
    merged_max = merged[..., head_dim + 1]
    merged_acc = merged[..., :head_dim]
    merged_total = merged[..., head_dim]
    own_score = (
        jnp.sum(
            group_queries.astype(jnp.float32) * new_keys.astype(jnp.float32)[:, :, None, :],
            axis=-1,
        )
        * score_scale
    )
    final_max = jnp.maximum(merged_max, own_score)
    rescale = jnp.exp(merged_max - final_max)
    own_exp = jnp.exp(own_score - final_max)
    final_total = merged_total * rescale + own_exp
    own_rounded = lax.optimization_barrier(own_exp.astype(jnp.bfloat16)).astype(jnp.float32)
    final_acc = (
        merged_acc * rescale[..., None]
        + own_rounded[..., None] * new_vals.astype(jnp.float32)[:, :, None, :]
    )
    decode_attended = (
        (final_acc / final_total[..., None])
        .astype(jnp.bfloat16)
        .reshape(group_rows, heads_q * head_dim)
    )
    decode_part = jnp.dot(decode_attended, output_weight, preferred_element_type=jnp.float32)
    decode_sum = scatter_blocks(decode_part, "tp", tp_near_first, add_parts, hook=next_hook)
    advance(block_total)(jnp.zeros((), jnp.float32))
    run_max, run_total, run_acc = progress["state"]
    attended = (
        (run_acc / run_total[..., None])
        .astype(jnp.bfloat16)
        .reshape(heads_kv, pre_local, query_group_count, head_dim)
        .transpose(1, 0, 2, 3)
        .reshape(pre_local, heads_q * head_dim)
    )
    prefill_part = jnp.dot(attended, output_weight, preferred_element_type=jnp.float32)
    prefill_sum = scatter_blocks(
        prefill_part, "tp", tp_near_first, add_parts, send_type=jnp.bfloat16
    )
    own_states = lax.dynamic_slice_in_dim(prefill_states, tp_index * pre_share, pre_share, 0)
    prefill_h = (own_states.astype(jnp.float32) + prefill_sum).astype(jnp.bfloat16)
    decode_h = (decode_states.astype(jnp.float32) + decode_sum).astype(jnp.bfloat16)
    moe_in = jnp.concatenate([prefill_h, decode_h], axis=0)
    normed_moe = rms_norm(moe_in, ffn_gain)
    rows_dev, top_count = routes.shape
    capacity = 2 * ((rows_dev * top_count + EXPERTS - 1) // EXPERTS)
    flat_routes = routes.reshape(rows_dev * top_count)
    expert_ids = jnp.arange(EXPERTS, dtype=jnp.int32)
    onehot = (flat_routes[:, None] == expert_ids[None, :]).astype(jnp.int32)
    slot_rank = jnp.sum(jnp.cumsum(onehot, axis=0) * onehot, axis=1) - 1
    slot_index = flat_routes * capacity + slot_rank
    repeated = jnp.repeat(normed_moe, top_count, axis=0)
    buffer = jnp.zeros((EXPERTS * capacity, model_width), jnp.bfloat16).at[slot_index].set(repeated)
    outgoing = buffer.reshape(seq_count, EXPERTS // seq_count, capacity, model_width)
    hidden = jnp.einsum(
        "secd,edf->secf",
        lax.all_to_all(outgoing, "seq", split_axis=0, concat_axis=0, tiled=True),
        expert_in,
        preferred_element_type=jnp.float32,
    )
    ff_width = expert_out.shape[1]
    active = (jax.nn.silu(hidden[..., :ff_width]) * hidden[..., ff_width:]).astype(jnp.bfloat16)
    results = jnp.einsum(
        "secf,efd->secd", active, expert_out, preferred_element_type=jnp.float32
    ).astype(jnp.bfloat16)
    returned = lax.all_to_all(results, "seq", split_axis=0, concat_axis=0, tiled=True)
    fetched = (
        returned.reshape(EXPERTS * capacity, model_width)[slot_index]
        .astype(jnp.float32)
        .reshape(rows_dev, top_count, model_width)
    )
    combined = jnp.sum(fetched * gate_values[..., None], axis=1)
    layer_out = (moe_in.astype(jnp.float32) + combined).astype(jnp.bfloat16)
    return (layer_out[:pre_share], layer_out[pre_share:])


def solution(mesh):
    return jax.shard_map(
        shards,
        mesh=mesh,
        in_specs=(
            P("seq", None),
            P(("seq", "tp"), None),
            P(),
            P(None, "tp"),
            P(None, "tp", None),
            P("tp", None),
            P(None, "seq", "tp", None),
            P(),
            P(),
            P(),
            P("seq", None, None),
            P("seq", None, None),
            P(("seq", "tp"), None),
            P(("seq", "tp"), None),
        ),
        out_specs=(P(("seq", "tp"), None), P(("seq", "tp"), None)),
        check_vma=False,
    )
```

```python
import math

import jax
import jax.numpy as jnp
from jax import lax
from jax.sharding import PartitionSpec as P
from jax.experimental import pallas as pl
from jax.experimental.pallas import tpu as pltpu

EXPERTS = 32
SPAN = 2048


eps_norm = 1e-05
rope_base = 10000.0
masked_score = -1e30
key_block = 512


def rms_norm(values, scales):
    floats = values.astype(jnp.float32)
    factor = lax.rsqrt(jnp.mean(floats * floats, axis=-1, keepdims=True) + eps_norm)
    return (floats * factor * scales.astype(jnp.float32)).astype(jnp.bfloat16)


def apply_rotary(values, token_positions):
    half_dim = values.shape[-1] // 2
    frequency = rope_base ** (-2.0 * jnp.arange(half_dim, dtype=jnp.float32) / values.shape[-1])
    angles = token_positions.astype(jnp.float32)[:, None] * frequency[None, :]
    cosine = jnp.cos(angles)[:, None, :]
    sine_part = jnp.sin(angles)[:, None, :]
    first_half = values[..., :half_dim]
    second_half = values[..., half_dim:]
    return jnp.concatenate(
        [
            first_half * cosine - second_half * sine_part,
            second_half * cosine + first_half * sine_part,
        ],
        axis=-1,
    )


def span_tables(span_tenant):
    span_count = span_tenant.shape[0]
    ordinal = jnp.arange(span_count, dtype=jnp.int32)
    same_tenant = span_tenant[:, None] == span_tenant[None, :]
    earlier = ordinal[None, :] < ordinal[:, None]
    return jnp.sum(jnp.where(same_tenant & earlier, 1, 0), axis=1).astype(jnp.int32)


def token_tables(token_index, span_tenant, before):
    span_count = span_tenant.shape[0]
    span_index = token_index // SPAN
    onehot = span_index[:, None] == jnp.arange(span_count, dtype=jnp.int32)[None, :]
    tenant = jnp.sum(jnp.where(onehot, span_tenant[None, :], 0), axis=1)
    offset = jnp.sum(jnp.where(onehot, before[None, :], 0), axis=1)
    return (tenant, offset * SPAN + token_index % SPAN)


def attend_keys(fold_state, keyvalue_rows, visible, query_matrix, score_scale):
    run_max, run_total, run_acc = fold_state
    head_dim = keyvalue_rows.shape[-1] // 2
    scores = (
        jnp.einsum(
            "qhgd,khd->qhgk",
            query_matrix,
            keyvalue_rows[..., :head_dim],
            preferred_element_type=jnp.float32,
        )
        * score_scale
    )
    mask_full = visible[:, None, None, :]
    scores = jnp.where(mask_full, scores, masked_score)
    new_max = jnp.maximum(run_max, jnp.max(scores, axis=-1))
    weights_exp = jnp.where(mask_full, jnp.exp(scores - new_max[..., None]), 0.0)
    factor = jnp.exp(run_max - new_max)
    new_total = run_total * factor + jnp.sum(weights_exp, axis=-1)
    new_acc = run_acc * factor[..., None] + jnp.einsum(
        "qhgk,khd->qhgd",
        weights_exp.astype(jnp.bfloat16),
        keyvalue_rows[..., head_dim:],
        preferred_element_type=jnp.float32,
    )
    return (new_max, new_total, new_acc)


def flash_kernel(
    flags_ref, q_ref, k_ref, v_ref, row_token_ref, row_tenant_ref, key_tenant_ref,
    o_ref, max_ref, total_ref, acc_ref, *, score_scale, block_len
):
    step = pl.program_id(0)

    @pl.when(step == 0)
    def _():
        max_ref[...] = jnp.full(max_ref.shape, masked_score, jnp.float32)
        total_ref[...] = jnp.zeros(total_ref.shape, jnp.float32)
        acc_ref[...] = jnp.zeros(acc_ref.shape, jnp.float32)

    @pl.when(flags_ref[step] != 0)
    def _():
        scores = (
            lax.dot_general(
                q_ref[...], k_ref[...], (((1,), (1,)), ((), ())),
                preferred_element_type=jnp.float32,
            )
            * score_scale
        )
        key_index = step * block_len + lax.broadcasted_iota(jnp.int32, (1, block_len), 1)
        visible = (row_tenant_ref[...] == key_tenant_ref[...]) & (
            row_token_ref[...] >= key_index
        )
        scores = jnp.where(visible, scores, masked_score)
        run_max = max_ref[...]
        new_max = jnp.maximum(run_max, jnp.max(scores, axis=-1, keepdims=True))
        weights_exp = jnp.where(visible, jnp.exp(scores - new_max), 0.0)
        factor = jnp.exp(run_max - new_max)
        total_ref[...] = total_ref[...] * factor + jnp.sum(weights_exp, axis=-1, keepdims=True)
        acc_ref[...] = acc_ref[...] * factor + jnp.dot(
            weights_exp.astype(jnp.bfloat16), v_ref[...], preferred_element_type=jnp.float32
        )
        max_ref[...] = new_max

    @pl.when(step == pl.num_programs(0) - 1)
    def _():
        o_ref[...] = (acc_ref[...] / total_ref[...]).astype(o_ref.dtype)


def flash_attend(flags, queries, keys, values, row_token, row_tenant, key_tenant, score_scale, block_len, interpret=False):
    query_count, head_dim = queries.shape
    key_count = keys.shape[0]
    full = lambda step, flags_ref: (0, 0)
    grid_spec = pltpu.PrefetchScalarGridSpec(
        num_scalar_prefetch=1,
        grid=(key_count // block_len,),
        in_specs=[
            pl.BlockSpec((query_count, head_dim), full),
            pl.BlockSpec((block_len, head_dim), lambda step, flags_ref: (step, 0)),
            pl.BlockSpec((block_len, head_dim), lambda step, flags_ref: (step, 0)),
            pl.BlockSpec((query_count, 1), full),
            pl.BlockSpec((query_count, 1), full),
            pl.BlockSpec((1, block_len), lambda step, flags_ref: (0, step)),
        ],
        out_specs=pl.BlockSpec((query_count, head_dim), full),
        scratch_shapes=[
            pltpu.VMEM((query_count, 1), jnp.float32),
            pltpu.VMEM((query_count, 1), jnp.float32),
            pltpu.VMEM((query_count, head_dim), jnp.float32),
        ],
    )
    body = lambda *refs: flash_kernel(*refs, score_scale=score_scale, block_len=block_len)
    return pl.pallas_call(
        body,
        grid_spec=grid_spec,
        out_shape=jax.ShapeDtypeStruct((query_count, head_dim), jnp.bfloat16),
        interpret=interpret,
    )(flags, queries, keys, values, row_token[:, None], row_tenant[:, None], key_tenant[None, :])


def swap_partner(values, axis_name, distance):
    count = lax.axis_size(axis_name)
    pairs = [(i, i ^ distance) for i in range(count)]
    return lax.ppermute(values, axis_name, pairs)


def gather_blocks(block, axis_name, distances):
    index = lax.axis_index(axis_name)
    stacked = block
    done = []
    for distance in distances:
        theirs = swap_partner(stacked, axis_name, distance)
        upper = (index // distance) % 2 == 1
        low = jnp.where(upper, theirs, stacked)
        high = jnp.where(upper, stacked, theirs)
        place = sum(1 for d in done if d > distance)
        stacked = jnp.stack([low, high], axis=place)
        done.append(distance)
    return stacked.reshape((-1,) + block.shape[1:])


def scatter_blocks(values, axis_name, distances, combine, send_type=None):
    count = lax.axis_size(axis_name)
    index = lax.axis_index(axis_name)
    levels = count.bit_length() - 1
    rows = values.shape[0] // count
    stacked = values.reshape((2,) * levels + (rows,) + values.shape[1:])
    remaining = [count >> (j + 1) for j in range(levels)]
    for distance in distances:
        place = remaining.index(distance)
        low = lax.index_in_dim(stacked, 0, place, keepdims=False)
        high = lax.index_in_dim(stacked, 1, place, keepdims=False)
        upper = (index // distance) % 2 == 1
        keep = jnp.where(upper, high, low)
        send = jnp.where(upper, low, high)
        if send_type is not None:
            send = send.astype(send_type)
        received = swap_partner(send, axis_name, distance).astype(keep.dtype)
        stacked = combine(keep, received)
        remaining.pop(place)
    return stacked


def add_parts(first, second):
    return first + second


def merge_softmax(first, second):
    first_max, second_max = first[..., -1], second[..., -1]
    top = jnp.maximum(first_max, second_max)
    first_scale = jnp.exp(first_max - top)[..., None]
    second_scale = jnp.exp(second_max - top)[..., None]
    body = first[..., :-1] * first_scale + second[..., :-1] * second_scale
    return jnp.concatenate([body, top[..., None]], axis=-1)


def shards(
    prefill_states,
    decode_states,
    attn_gain,
    query_weight,
    keyvalue_weight,
    output_weight,
    cache_keyval,
    cached_length,
    span_tenant,
    ffn_gain,
    expert_in,
    expert_out,
    routes,
    gate_values,
):
    seq_count = lax.axis_size("seq")
    tp_count = lax.axis_size("tp")
    seq_index = lax.axis_index("seq")
    tp_index = lax.axis_index("tp")
    pre_local, model_width = prefill_states.shape
    dec_local = decode_states.shape[0]
    heads_kv = keyvalue_weight.shape[1]
    head_dim = keyvalue_weight.shape[2] // 2
    heads_q = query_weight.shape[1] // head_dim
    query_group_count = heads_q // heads_kv
    score_scale = head_dim ** (-0.5)
    pre_share = pre_local // tp_count
    normalised_input = rms_norm(prefill_states, attn_gain)
    query_matrix = jnp.dot(
        normalised_input, query_weight, preferred_element_type=jnp.float32
    ).reshape(pre_local, heads_q, head_dim)
    keyvalue_rows = jnp.dot(
        normalised_input,
        keyvalue_weight.reshape(model_width, heads_kv * 2 * head_dim),
        preferred_element_type=jnp.float32,
    ).reshape(pre_local, heads_kv, 2 * head_dim)
    before = span_tables(span_tenant)
    token_index = seq_index * pre_local + jnp.arange(pre_local, dtype=jnp.int32)
    tenant, token_positions = token_tables(token_index, span_tenant, before)
    query_matrix = (
        apply_rotary(query_matrix, token_positions)
        .astype(jnp.bfloat16)
        .reshape(pre_local, heads_kv, query_group_count, head_dim)
    )
    rotated_keys = apply_rotary(keyvalue_rows[..., :head_dim], token_positions).astype(jnp.bfloat16)
    local_keyvals = jnp.concatenate(
        [rotated_keys, keyvalue_rows[..., head_dim:].astype(jnp.bfloat16)], axis=-1
    )
    seq_near_first = [1 << j for j in range(seq_count.bit_length() - 1)]
    key_piece = gather_blocks(local_keyvals, "seq", seq_near_first[::-1])
    piece_rows = key_piece.shape[0]
    block_len = math.gcd(piece_rows, key_block)
    blocks = key_piece.reshape(piece_rows // block_len, block_len, heads_kv, 2 * head_dim)
    query_count = pre_local * query_group_count
    query_rows = query_matrix.transpose(1, 0, 2, 3).reshape(heads_kv, query_count, head_dim)
    row_token = jnp.repeat(token_index, query_group_count)
    row_tenant = jnp.repeat(tenant, query_group_count)
    key_positions = jnp.arange(piece_rows, dtype=jnp.int32)
    key_tenant = token_tables(key_positions, span_tenant, before)[0]
    token_visible = (tenant[:, None] == key_tenant[None, :]) & (
        token_index[:, None] >= key_positions[None, :]
    )
    block_flags = jnp.any(
        token_visible.reshape(pre_local, piece_rows // block_len, block_len), axis=(0, 2)
    ).astype(jnp.int32)
    head_outputs = [
        flash_attend(
            block_flags,
            query_rows[head],
            key_piece[:, head, :head_dim],
            key_piece[:, head, head_dim:],
            row_token,
            row_tenant,
            key_tenant,
            score_scale,
            block_len,
        )
        for head in range(heads_kv)
    ]
    attended = (
        jnp.stack(head_outputs)
        .reshape(heads_kv, pre_local, query_group_count, head_dim)
        .transpose(1, 0, 2, 3)
        .reshape(pre_local, heads_q * head_dim)
    )
    prefill_part = jnp.dot(attended, output_weight, preferred_element_type=jnp.float32)
    tp_near_first = [1 << j for j in range(tp_count.bit_length() - 1)]
    prefill_sum = scatter_blocks(
        prefill_part, "tp", tp_near_first, add_parts, send_type=jnp.bfloat16
    )
    group_states = gather_blocks(decode_states, "tp", tp_near_first[::-1])
    group_rows = group_states.shape[0]
    group_lengths = lax.dynamic_slice_in_dim(cached_length, seq_index * group_rows, group_rows, 0)
    decode_normalised = rms_norm(group_states, attn_gain)
    group_queries = jnp.dot(
        decode_normalised, query_weight, preferred_element_type=jnp.float32
    ).reshape(group_rows, heads_q, head_dim)
    group_queries = (
        apply_rotary(group_queries, group_lengths)
        .astype(jnp.bfloat16)
        .reshape(group_rows, heads_kv, query_group_count, head_dim)
    )
    decode_keyvalues = jnp.dot(
        decode_normalised,
        keyvalue_weight.reshape(model_width, heads_kv * 2 * head_dim),
        preferred_element_type=jnp.float32,
    ).reshape(group_rows, heads_kv, 2 * head_dim)
    new_keys = apply_rotary(decode_keyvalues[..., :head_dim], group_lengths).astype(jnp.bfloat16)
    new_vals = decode_keyvalues[..., head_dim:].astype(jnp.bfloat16)
    decode_queries = gather_blocks(group_queries, "seq", seq_near_first[::-1])
    cache_local = cache_keyval.shape[1]
    cache_pos = seq_index * cache_local + jnp.arange(cache_local, dtype=jnp.int32)
    visible = (cache_pos[None, :] < cached_length[:, None])[:, None, None, :]
    scores = (
        jnp.einsum(
            "bhgd,bkhd->bhgk",
            decode_queries,
            cache_keyval[..., :head_dim],
            preferred_element_type=jnp.float32,
        )
        * score_scale
    )
    scores = jnp.where(visible, scores, masked_score)
    local_max = jnp.max(scores, axis=-1)
    weights_exp = jnp.where(visible, jnp.exp(scores - local_max[..., None]), 0.0)
    local_total = jnp.sum(weights_exp, axis=-1)
    local_acc = jnp.einsum(
        "bhgk,bkhd->bhgd",
        weights_exp.astype(jnp.bfloat16),
        cache_keyval[..., head_dim:],
        preferred_element_type=jnp.float32,
    )
    packed = jnp.concatenate([local_acc, local_total[..., None], local_max[..., None]], axis=-1)
    merged = scatter_blocks(packed, "seq", seq_near_first, merge_softmax)
    merged_max = merged[..., head_dim + 1]
    merged_acc = merged[..., :head_dim]
    merged_total = merged[..., head_dim]
    own_score = (
        jnp.sum(
            group_queries.astype(jnp.float32) * new_keys.astype(jnp.float32)[:, :, None, :],
            axis=-1,
        )
        * score_scale
    )
    final_max = jnp.maximum(merged_max, own_score)
    rescale = jnp.exp(merged_max - final_max)
    own_exp = jnp.exp(own_score - final_max)
    final_total = merged_total * rescale + own_exp
    own_rounded = lax.optimization_barrier(own_exp.astype(jnp.bfloat16)).astype(jnp.float32)
    final_acc = (
        merged_acc * rescale[..., None]
        + own_rounded[..., None] * new_vals.astype(jnp.float32)[:, :, None, :]
    )
    decode_attended = (
        (final_acc / final_total[..., None])
        .astype(jnp.bfloat16)
        .reshape(group_rows, heads_q * head_dim)
    )
    decode_part = jnp.dot(decode_attended, output_weight, preferred_element_type=jnp.float32)
    decode_sum = scatter_blocks(decode_part, "tp", tp_near_first, add_parts)
    own_states = lax.dynamic_slice_in_dim(prefill_states, tp_index * pre_share, pre_share, 0)
    prefill_h = (own_states.astype(jnp.float32) + prefill_sum).astype(jnp.bfloat16)
    decode_h = (decode_states.astype(jnp.float32) + decode_sum).astype(jnp.bfloat16)
    moe_in = jnp.concatenate([prefill_h, decode_h], axis=0)
    normed_moe = rms_norm(moe_in, ffn_gain)
    rows_dev, top_count = routes.shape
    capacity = 2 * ((rows_dev * top_count + EXPERTS - 1) // EXPERTS)
    flat_routes = routes.reshape(rows_dev * top_count)
    expert_ids = jnp.arange(EXPERTS, dtype=jnp.int32)
    onehot = (flat_routes[:, None] == expert_ids[None, :]).astype(jnp.int32)
    slot_rank = jnp.sum(jnp.cumsum(onehot, axis=0) * onehot, axis=1) - 1
    slot_index = flat_routes * capacity + slot_rank
    repeated = jnp.repeat(normed_moe, top_count, axis=0)
    buffer = jnp.zeros((EXPERTS * capacity, model_width), jnp.bfloat16).at[slot_index].set(repeated)
    outgoing = buffer.reshape(seq_count, EXPERTS // seq_count, capacity, model_width)
    hidden = jnp.einsum(
        "secd,edf->secf",
        lax.all_to_all(outgoing, "seq", split_axis=0, concat_axis=0, tiled=True),
        expert_in,
        preferred_element_type=jnp.float32,
    )
    ff_width = expert_out.shape[1]
    active = (jax.nn.silu(hidden[..., :ff_width]) * hidden[..., ff_width:]).astype(jnp.bfloat16)
    results = jnp.einsum(
        "secf,efd->secd", active, expert_out, preferred_element_type=jnp.float32
    ).astype(jnp.bfloat16)
    returned = lax.all_to_all(results, "seq", split_axis=0, concat_axis=0, tiled=True)
    fetched = (
        returned.reshape(EXPERTS * capacity, model_width)[slot_index]
        .astype(jnp.float32)
        .reshape(rows_dev, top_count, model_width)
    )
    combined = jnp.sum(fetched * gate_values[..., None], axis=1)
    layer_out = (moe_in.astype(jnp.float32) + combined).astype(jnp.bfloat16)
    return (layer_out[:pre_share], layer_out[pre_share:])


def solution(mesh):
    return jax.shard_map(
        shards,
        mesh=mesh,
        in_specs=(
            P("seq", None),
            P(("seq", "tp"), None),
            P(),
            P(None, "tp"),
            P(None, "tp", None),
            P("tp", None),
            P(None, "seq", "tp", None),
            P(),
            P(),
            P(),
            P("seq", None, None),
            P("seq", None, None),
            P(("seq", "tp"), None),
            P(("seq", "tp"), None),
        ),
        out_specs=(P(("seq", "tp"), None), P(("seq", "tp"), None)),
        check_vma=False,
    )
```

```python
import math

import jax
import jax.numpy as jnp
from jax import lax
from jax.sharding import PartitionSpec as P
from jax.experimental import pallas as pl
from jax.experimental.pallas import tpu as pltpu

EXPERTS = 32
SPAN = 2048


eps_norm = 1e-05
rope_base = 10000.0
masked_score = -1e30
key_block = 512


def rms_norm(values, scales):
    floats = values.astype(jnp.float32)
    factor = lax.rsqrt(jnp.mean(floats * floats, axis=-1, keepdims=True) + eps_norm)
    return (floats * factor * scales.astype(jnp.float32)).astype(jnp.bfloat16)


def apply_rotary(values, token_positions):
    half_dim = values.shape[-1] // 2
    frequency = rope_base ** (-2.0 * jnp.arange(half_dim, dtype=jnp.float32) / values.shape[-1])
    angles = token_positions.astype(jnp.float32)[:, None] * frequency[None, :]
    cosine = jnp.cos(angles)[:, None, :]
    sine_part = jnp.sin(angles)[:, None, :]
    first_half = values[..., :half_dim]
    second_half = values[..., half_dim:]
    return jnp.concatenate(
        [
            first_half * cosine - second_half * sine_part,
            second_half * cosine + first_half * sine_part,
        ],
        axis=-1,
    )


def span_tables(span_tenant):
    span_count = span_tenant.shape[0]
    ordinal = jnp.arange(span_count, dtype=jnp.int32)
    same_tenant = span_tenant[:, None] == span_tenant[None, :]
    earlier = ordinal[None, :] < ordinal[:, None]
    return jnp.sum(jnp.where(same_tenant & earlier, 1, 0), axis=1).astype(jnp.int32)


def token_tables(token_index, span_tenant, before):
    span_count = span_tenant.shape[0]
    span_index = token_index // SPAN
    onehot = span_index[:, None] == jnp.arange(span_count, dtype=jnp.int32)[None, :]
    tenant = jnp.sum(jnp.where(onehot, span_tenant[None, :], 0), axis=1)
    offset = jnp.sum(jnp.where(onehot, before[None, :], 0), axis=1)
    return (tenant, offset * SPAN + token_index % SPAN)


def attend_keys(fold_state, keyvalue_rows, visible, query_matrix, score_scale):
    run_max, run_total, run_acc = fold_state
    head_dim = keyvalue_rows.shape[-1] // 2
    scores = (
        jnp.einsum(
            "qhgd,khd->qhgk",
            query_matrix,
            keyvalue_rows[..., :head_dim],
            preferred_element_type=jnp.float32,
        )
        * score_scale
    )
    mask_full = visible[:, None, None, :]
    scores = jnp.where(mask_full, scores, masked_score)
    new_max = jnp.maximum(run_max, jnp.max(scores, axis=-1))
    weights_exp = jnp.where(mask_full, jnp.exp(scores - new_max[..., None]), 0.0)
    factor = jnp.exp(run_max - new_max)
    new_total = run_total * factor + jnp.sum(weights_exp, axis=-1)
    new_acc = run_acc * factor[..., None] + jnp.einsum(
        "qhgk,khd->qhgd",
        weights_exp.astype(jnp.bfloat16),
        keyvalue_rows[..., head_dim:],
        preferred_element_type=jnp.float32,
    )
    return (new_max, new_total, new_acc)


def flash_kernel(
    flags_ref, q_ref, k_ref, v_ref, row_token_ref, row_tenant_ref, key_tenant_ref,
    o_ref, max_ref, total_ref, acc_ref, *, score_scale, block_len
):
    step = pl.program_id(0)

    @pl.when(step == 0)
    def _():
        max_ref[...] = jnp.full(max_ref.shape, masked_score, jnp.float32)
        total_ref[...] = jnp.zeros(total_ref.shape, jnp.float32)
        acc_ref[...] = jnp.zeros(acc_ref.shape, jnp.float32)

    @pl.when(flags_ref[step] != 0)
    def _():
        scores = (
            lax.dot_general(
                q_ref[...], k_ref[...], (((1,), (1,)), ((), ())),
                preferred_element_type=jnp.float32,
            )
            * score_scale
        )
        key_index = step * block_len + lax.broadcasted_iota(jnp.int32, (1, block_len), 1)
        visible = (row_tenant_ref[...] == key_tenant_ref[...]) & (
            row_token_ref[...] >= key_index
        )
        scores = jnp.where(visible, scores, masked_score)
        run_max = max_ref[...]
        new_max = jnp.maximum(run_max, jnp.max(scores, axis=-1, keepdims=True))
        weights_exp = jnp.where(visible, jnp.exp(scores - new_max), 0.0)
        factor = jnp.exp(run_max - new_max)
        total_ref[...] = total_ref[...] * factor + jnp.sum(weights_exp, axis=-1, keepdims=True)
        acc_ref[...] = acc_ref[...] * factor + jnp.dot(
            weights_exp.astype(jnp.bfloat16), v_ref[...], preferred_element_type=jnp.float32
        )
        max_ref[...] = new_max

    @pl.when(step == pl.num_programs(0) - 1)
    def _():
        o_ref[...] = (acc_ref[...] / total_ref[...]).astype(o_ref.dtype)


def flash_attend(flags, queries, keys, values, row_token, row_tenant, key_tenant, score_scale, block_len, interpret=False):
    query_count, head_dim = queries.shape
    key_count = keys.shape[0]
    full = lambda step, flags_ref: (0, 0)
    grid_spec = pltpu.PrefetchScalarGridSpec(
        num_scalar_prefetch=1,
        grid=(key_count // block_len,),
        in_specs=[
            pl.BlockSpec((query_count, head_dim), full),
            pl.BlockSpec((block_len, head_dim), lambda step, flags_ref: (step, 0)),
            pl.BlockSpec((block_len, head_dim), lambda step, flags_ref: (step, 0)),
            pl.BlockSpec((query_count, 1), full),
            pl.BlockSpec((query_count, 1), full),
            pl.BlockSpec((1, block_len), lambda step, flags_ref: (0, step)),
        ],
        out_specs=pl.BlockSpec((query_count, head_dim), full),
        scratch_shapes=[
            pltpu.VMEM((query_count, 1), jnp.float32),
            pltpu.VMEM((query_count, 1), jnp.float32),
            pltpu.VMEM((query_count, head_dim), jnp.float32),
        ],
    )
    body = lambda *refs: flash_kernel(*refs, score_scale=score_scale, block_len=block_len)
    return pl.pallas_call(
        body,
        grid_spec=grid_spec,
        out_shape=jax.ShapeDtypeStruct((query_count, head_dim), jnp.bfloat16),
        interpret=interpret,
    )(flags, queries, keys, values, row_token[:, None], row_tenant[:, None], key_tenant[None, :])


def swap_partner(values, axis_name, distance):
    count = lax.axis_size(axis_name)
    pairs = [(i, i ^ distance) for i in range(count)]
    return lax.ppermute(values, axis_name, pairs)


def lane_dense(values):
    flat = values.reshape(-1)
    return flat.reshape(-1, 128) if flat.shape[0] % 128 == 0 else flat.reshape(1, -1)


def gather_blocks(block, axis_name, distances):
    index = lax.axis_index(axis_name)
    shape = block.shape
    block = lane_dense(block)[None]
    stacked = block
    done = []
    for distance in distances:
        theirs = swap_partner(stacked, axis_name, distance)
        upper = (index // distance) % 2 == 1
        low = jnp.where(upper, theirs, stacked)
        high = jnp.where(upper, stacked, theirs)
        place = sum(1 for d in done if d > distance)
        stacked = jnp.stack([low, high], axis=place)
        done.append(distance)
    return stacked.reshape((-1,) + shape[1:])


def scatter_blocks(values, axis_name, distances, combine, send_type=None, dense=False):
    count = lax.axis_size(axis_name)
    index = lax.axis_index(axis_name)
    levels = count.bit_length() - 1
    rows = values.shape[0] // count
    part_shape = (rows,) + values.shape[1:]
    if dense:
        flat = math.prod(part_shape)
        part_shape = (flat // 128, 128) if flat % 128 == 0 else (1, flat)
    stacked = values.reshape((2,) * levels + part_shape)
    remaining = [count >> (j + 1) for j in range(levels)]
    for distance in distances:
        place = remaining.index(distance)
        low = lax.index_in_dim(stacked, 0, place, keepdims=False)
        high = lax.index_in_dim(stacked, 1, place, keepdims=False)
        upper = (index // distance) % 2 == 1
        keep = jnp.where(upper, high, low)
        send = jnp.where(upper, low, high)
        if send_type is not None:
            send = send.astype(send_type)
        received = swap_partner(send, axis_name, distance).astype(keep.dtype)
        stacked = combine(keep, received)
        remaining.pop(place)
    return stacked.reshape((rows,) + values.shape[1:])


def add_parts(first, second):
    return first + second


def merge_softmax(first, second, groups, head_dim):
    width = groups * head_dim
    first_max, second_max = first[..., width + groups:], second[..., width + groups:]
    top = jnp.maximum(first_max, second_max)
    first_scale = jnp.exp(first_max - top)
    second_scale = jnp.exp(second_max - top)
    acc = first[..., :width] * jnp.repeat(first_scale, head_dim, axis=-1) + second[
        ..., :width
    ] * jnp.repeat(second_scale, head_dim, axis=-1)
    total = first[..., width:width + groups] * first_scale + second[..., width:width + groups] * second_scale
    return jnp.concatenate([acc, total, top], axis=-1)

def shards(
    prefill_states,
    decode_states,
    attn_gain,
    query_weight,
    keyvalue_weight,
    output_weight,
    cache_keyval,
    cached_length,
    span_tenant,
    ffn_gain,
    expert_in,
    expert_out,
    routes,
    gate_values,
):
    seq_count = lax.axis_size("seq")
    tp_count = lax.axis_size("tp")
    seq_index = lax.axis_index("seq")
    tp_index = lax.axis_index("tp")
    pre_local, model_width = prefill_states.shape
    dec_local = decode_states.shape[0]
    heads_kv = keyvalue_weight.shape[1]
    head_dim = keyvalue_weight.shape[2] // 2
    heads_q = query_weight.shape[1] // head_dim
    query_group_count = heads_q // heads_kv
    score_scale = head_dim ** (-0.5)
    pre_share = pre_local // tp_count
    normalised_input = rms_norm(prefill_states, attn_gain)
    query_matrix = jnp.dot(
        normalised_input, query_weight, preferred_element_type=jnp.float32
    ).reshape(pre_local, heads_q, head_dim)
    keyvalue_rows = jnp.dot(
        normalised_input,
        keyvalue_weight.reshape(model_width, heads_kv * 2 * head_dim),
        preferred_element_type=jnp.float32,
    ).reshape(pre_local, heads_kv, 2 * head_dim)
    before = span_tables(span_tenant)
    token_index = seq_index * pre_local + jnp.arange(pre_local, dtype=jnp.int32)
    tenant, token_positions = token_tables(token_index, span_tenant, before)
    query_matrix = (
        apply_rotary(query_matrix, token_positions)
        .astype(jnp.bfloat16)
        .reshape(pre_local, heads_kv, query_group_count, head_dim)
    )
    rotated_keys = apply_rotary(keyvalue_rows[..., :head_dim], token_positions).astype(jnp.bfloat16)
    local_keyvals = jnp.concatenate(
        [rotated_keys, keyvalue_rows[..., head_dim:].astype(jnp.bfloat16)], axis=-1
    )
    seq_near_first = [1 << j for j in range(seq_count.bit_length() - 1)]
    key_piece = lax.all_gather(
        local_keyvals.reshape(pre_local, heads_kv * 2 * head_dim), "seq", axis=0, tiled=True
    ).reshape(-1, heads_kv, 2 * head_dim)
    piece_rows = key_piece.shape[0]
    block_len = math.gcd(piece_rows, key_block)
    blocks = key_piece.reshape(piece_rows // block_len, block_len, heads_kv, 2 * head_dim)
    query_count = pre_local * query_group_count
    query_rows = query_matrix.transpose(1, 0, 2, 3).reshape(heads_kv, query_count, head_dim)
    row_token = jnp.repeat(token_index, query_group_count)
    row_tenant = jnp.repeat(tenant, query_group_count)
    key_positions = jnp.arange(piece_rows, dtype=jnp.int32)
    key_tenant = token_tables(key_positions, span_tenant, before)[0]
    token_visible = (tenant[:, None] == key_tenant[None, :]) & (
        token_index[:, None] >= key_positions[None, :]
    )
    block_flags = jnp.any(
        token_visible.reshape(pre_local, piece_rows // block_len, block_len), axis=(0, 2)
    ).astype(jnp.int32)
    head_outputs = [
        flash_attend(
            block_flags,
            query_rows[head],
            key_piece[:, head, :head_dim],
            key_piece[:, head, head_dim:],
            row_token,
            row_tenant,
            key_tenant,
            score_scale,
            block_len,
        )
        for head in range(heads_kv)
    ]
    attended = (
        jnp.stack(head_outputs)
        .reshape(heads_kv, pre_local, query_group_count, head_dim)
        .transpose(1, 0, 2, 3)
        .reshape(pre_local, heads_q * head_dim)
    )
    prefill_part = jnp.dot(attended, output_weight, preferred_element_type=jnp.float32)
    tp_near_first = [1 << j for j in range(tp_count.bit_length() - 1)]
    prefill_sum = scatter_blocks(
        prefill_part, "tp", tp_near_first, add_parts, send_type=jnp.bfloat16, dense=True
    )
    group_states = gather_blocks(decode_states, "tp", tp_near_first[::-1])
    group_rows = group_states.shape[0]
    group_lengths = lax.dynamic_slice_in_dim(cached_length, seq_index * group_rows, group_rows, 0)
    decode_normalised = rms_norm(group_states, attn_gain)
    group_queries = jnp.dot(
        decode_normalised, query_weight, preferred_element_type=jnp.float32
    ).reshape(group_rows, heads_q, head_dim)
    group_queries = (
        apply_rotary(group_queries, group_lengths)
        .astype(jnp.bfloat16)
        .reshape(group_rows, heads_kv, query_group_count, head_dim)
    )
    decode_keyvalues = jnp.dot(
        decode_normalised,
        keyvalue_weight.reshape(model_width, heads_kv * 2 * head_dim),
        preferred_element_type=jnp.float32,
    ).reshape(group_rows, heads_kv, 2 * head_dim)
    new_keys = apply_rotary(decode_keyvalues[..., :head_dim], group_lengths).astype(jnp.bfloat16)
    new_vals = decode_keyvalues[..., head_dim:].astype(jnp.bfloat16)
    decode_queries = gather_blocks(group_queries, "seq", seq_near_first[::-1])
    cache_local = cache_keyval.shape[1]
    cache_pos = seq_index * cache_local + jnp.arange(cache_local, dtype=jnp.int32)
    visible = (cache_pos[None, :] < cached_length[:, None])[:, None, None, :]
    scores = (
        jnp.einsum(
            "bhgd,bkhd->bhgk",
            decode_queries,
            cache_keyval[..., :head_dim],
            preferred_element_type=jnp.float32,
        )
        * score_scale
    )
    scores = jnp.where(visible, scores, masked_score)
    local_max = jnp.max(scores, axis=-1)
    weights_exp = jnp.where(visible, jnp.exp(scores - local_max[..., None]), 0.0)
    local_total = jnp.sum(weights_exp, axis=-1)
    local_acc = jnp.einsum(
        "bhgk,bkhd->bhgd",
        weights_exp.astype(jnp.bfloat16),
        cache_keyval[..., head_dim:],
        preferred_element_type=jnp.float32,
    )
    dec_total = local_acc.shape[0]
    groups = heads_kv * query_group_count
    packed = jnp.concatenate(
        [
            local_acc.reshape(dec_total, groups * head_dim),
            local_total.reshape(dec_total, groups),
            local_max.reshape(dec_total, groups),
        ],
        axis=-1,
    )
    merged = scatter_blocks(
        packed, "seq", seq_near_first, lambda a, b: merge_softmax(a, b, groups, head_dim)
    )
    merged_acc = merged[:, : groups * head_dim].reshape(group_rows, heads_kv, query_group_count, head_dim)
    merged_total = merged[:, groups * head_dim : groups * (head_dim + 1)].reshape(
        group_rows, heads_kv, query_group_count
    )
    merged_max = merged[:, groups * (head_dim + 1) :].reshape(group_rows, heads_kv, query_group_count)
    own_score = (
        jnp.sum(
            group_queries.astype(jnp.float32) * new_keys.astype(jnp.float32)[:, :, None, :],
            axis=-1,
        )
        * score_scale
    )
    final_max = jnp.maximum(merged_max, own_score)
    rescale = jnp.exp(merged_max - final_max)
    own_exp = jnp.exp(own_score - final_max)
    final_total = merged_total * rescale + own_exp
    own_rounded = lax.optimization_barrier(own_exp.astype(jnp.bfloat16)).astype(jnp.float32)
    final_acc = (
        merged_acc * rescale[..., None]
        + own_rounded[..., None] * new_vals.astype(jnp.float32)[:, :, None, :]
    )
    decode_attended = (
        (final_acc / final_total[..., None])
        .astype(jnp.bfloat16)
        .reshape(group_rows, heads_q * head_dim)
    )
    decode_part = jnp.dot(decode_attended, output_weight, preferred_element_type=jnp.float32)
    decode_sum = scatter_blocks(decode_part, "tp", tp_near_first, add_parts, dense=True)
    own_states = lax.dynamic_slice_in_dim(prefill_states, tp_index * pre_share, pre_share, 0)
    prefill_h = (own_states.astype(jnp.float32) + prefill_sum).astype(jnp.bfloat16)
    decode_h = (decode_states.astype(jnp.float32) + decode_sum).astype(jnp.bfloat16)
    moe_in = jnp.concatenate([prefill_h, decode_h], axis=0)
    normed_moe = rms_norm(moe_in, ffn_gain)
    rows_dev, top_count = routes.shape
    capacity = 2 * ((rows_dev * top_count + EXPERTS - 1) // EXPERTS)
    flat_routes = routes.reshape(rows_dev * top_count)
    expert_ids = jnp.arange(EXPERTS, dtype=jnp.int32)
    onehot = (flat_routes[:, None] == expert_ids[None, :]).astype(jnp.int32)
    slot_rank = jnp.sum(jnp.cumsum(onehot, axis=0) * onehot, axis=1) - 1
    slot_index = flat_routes * capacity + slot_rank
    repeated = jnp.repeat(normed_moe, top_count, axis=0)
    buffer = jnp.zeros((EXPERTS * capacity, model_width), jnp.bfloat16).at[slot_index].set(repeated)
    outgoing = buffer.reshape(seq_count, EXPERTS // seq_count, capacity, model_width)
    hidden = jnp.einsum(
        "secd,edf->secf",
        lax.all_to_all(outgoing, "seq", split_axis=0, concat_axis=0, tiled=True),
        expert_in,
        preferred_element_type=jnp.float32,
    )
    ff_width = expert_out.shape[1]
    active = (jax.nn.silu(hidden[..., :ff_width]) * hidden[..., ff_width:]).astype(jnp.bfloat16)
    results = jnp.einsum(
        "secf,efd->secd", active, expert_out, preferred_element_type=jnp.float32
    ).astype(jnp.bfloat16)
    returned = lax.all_to_all(results, "seq", split_axis=0, concat_axis=0, tiled=True)
    fetched = (
        returned.reshape(EXPERTS * capacity, model_width)[slot_index]
        .astype(jnp.float32)
        .reshape(rows_dev, top_count, model_width)
    )
    combined = jnp.sum(fetched * gate_values[..., None], axis=1)
    layer_out = (moe_in.astype(jnp.float32) + combined).astype(jnp.bfloat16)
    return (layer_out[:pre_share], layer_out[pre_share:])


def solution(mesh):
    return jax.shard_map(
        shards,
        mesh=mesh,
        in_specs=(
            P("seq", None),
            P(("seq", "tp"), None),
            P(),
            P(None, "tp"),
            P(None, "tp", None),
            P("tp", None),
            P(None, "seq", "tp", None),
            P(),
            P(),
            P(),
            P("seq", None, None),
            P("seq", None, None),
            P(("seq", "tp"), None),
            P(("seq", "tp"), None),
        ),
        out_specs=(P(("seq", "tp"), None), P(("seq", "tp"), None)),
        check_vma=False,
    )
```

```python
import math

import jax
import jax.numpy as jnp
from jax import lax
from jax.sharding import PartitionSpec as P
from jax.experimental import pallas as pl
from jax.experimental.pallas import tpu as pltpu

EXPERTS = 32
SPAN = 2048


eps_norm = 1e-05
rope_base = 10000.0
masked_score = -1e30
key_block = 512


def rms_norm(values, scales):
    floats = values.astype(jnp.float32)
    factor = lax.rsqrt(jnp.mean(floats * floats, axis=-1, keepdims=True) + eps_norm)
    return (floats * factor * scales.astype(jnp.float32)).astype(jnp.bfloat16)


def apply_rotary(values, token_positions):
    half_dim = values.shape[-1] // 2
    frequency = rope_base ** (-2.0 * jnp.arange(half_dim, dtype=jnp.float32) / values.shape[-1])
    angles = token_positions.astype(jnp.float32)[:, None] * frequency[None, :]
    cosine = jnp.cos(angles)[:, None, :]
    sine_part = jnp.sin(angles)[:, None, :]
    first_half = values[..., :half_dim]
    second_half = values[..., half_dim:]
    return jnp.concatenate(
        [
            first_half * cosine - second_half * sine_part,
            second_half * cosine + first_half * sine_part,
        ],
        axis=-1,
    )


def span_tables(span_tenant):
    span_count = span_tenant.shape[0]
    ordinal = jnp.arange(span_count, dtype=jnp.int32)
    same_tenant = span_tenant[:, None] == span_tenant[None, :]
    earlier = ordinal[None, :] < ordinal[:, None]
    return jnp.sum(jnp.where(same_tenant & earlier, 1, 0), axis=1).astype(jnp.int32)


def token_tables(token_index, span_tenant, before):
    span_count = span_tenant.shape[0]
    span_index = token_index // SPAN
    onehot = span_index[:, None] == jnp.arange(span_count, dtype=jnp.int32)[None, :]
    tenant = jnp.sum(jnp.where(onehot, span_tenant[None, :], 0), axis=1)
    offset = jnp.sum(jnp.where(onehot, before[None, :], 0), axis=1)
    return (tenant, offset * SPAN + token_index % SPAN)


def attend_keys(fold_state, keyvalue_rows, visible, query_matrix, score_scale):
    run_max, run_total, run_acc = fold_state
    head_dim = keyvalue_rows.shape[-1] // 2
    scores = (
        jnp.einsum(
            "qhgd,khd->qhgk",
            query_matrix,
            keyvalue_rows[..., :head_dim],
            preferred_element_type=jnp.float32,
        )
        * score_scale
    )
    mask_full = visible[:, None, None, :]
    scores = jnp.where(mask_full, scores, masked_score)
    new_max = jnp.maximum(run_max, jnp.max(scores, axis=-1))
    weights_exp = jnp.where(mask_full, jnp.exp(scores - new_max[..., None]), 0.0)
    factor = jnp.exp(run_max - new_max)
    new_total = run_total * factor + jnp.sum(weights_exp, axis=-1)
    new_acc = run_acc * factor[..., None] + jnp.einsum(
        "qhgk,khd->qhgd",
        weights_exp.astype(jnp.bfloat16),
        keyvalue_rows[..., head_dim:],
        preferred_element_type=jnp.float32,
    )
    return (new_max, new_total, new_acc)


def flash_kernel(
    flags_ref, q_ref, k_ref, v_ref, row_token_ref, row_tenant_ref, key_tenant_ref,
    o_ref, max_ref, total_ref, acc_ref, *, score_scale, block_len
):
    step = pl.program_id(0)

    @pl.when(step == 0)
    def _():
        max_ref[...] = jnp.full(max_ref.shape, masked_score, jnp.float32)
        total_ref[...] = jnp.zeros(total_ref.shape, jnp.float32)
        acc_ref[...] = jnp.zeros(acc_ref.shape, jnp.float32)

    @pl.when(flags_ref[step] != 0)
    def _():
        scores = (
            lax.dot_general(
                q_ref[...], v_ref[...], (((1,), (1,)), ((), ())),
                preferred_element_type=jnp.float32,
            )
            * score_scale
        )
        key_index = step * block_len + lax.broadcasted_iota(jnp.int32, (1, block_len), 1)
        visible = (row_tenant_ref[...] == key_tenant_ref[...]) & (
            row_token_ref[...] >= key_index
        )
        scores = jnp.where(visible, scores, masked_score)
        run_max = max_ref[...]
        new_max = jnp.maximum(run_max, jnp.max(scores, axis=-1, keepdims=True))
        weights_exp = jnp.where(visible, jnp.exp(scores - new_max), 0.0)
        factor = jnp.exp(run_max - new_max)
        total_ref[...] = total_ref[...] * factor + jnp.sum(weights_exp, axis=-1, keepdims=True)
        acc_ref[...] = acc_ref[...] * factor + jnp.dot(
            weights_exp.astype(jnp.bfloat16), v_ref[...], preferred_element_type=jnp.float32
        )
        max_ref[...] = new_max

    @pl.when(step == pl.num_programs(0) - 1)
    def _():
        o_ref[...] = (acc_ref[...] / total_ref[...]).astype(o_ref.dtype)


def flash_attend(flags, queries, keyvals, head, row_token, row_tenant, key_tenant, score_scale, block_len, interpret=False):
    query_count, head_dim = queries.shape
    key_count = keyvals.shape[0]
    full = lambda step, flags_ref: (0, 0)
    grid_spec = pltpu.PrefetchScalarGridSpec(
        num_scalar_prefetch=1,
        grid=(key_count // block_len,),
        in_specs=[
            pl.BlockSpec((query_count, head_dim), full),
            pl.BlockSpec((block_len, head_dim), lambda step, flags_ref: (step, head)),
            pl.BlockSpec((block_len, head_dim), lambda step, flags_ref: (step, head)),
            pl.BlockSpec((query_count, 1), full),
            pl.BlockSpec((query_count, 1), full),
            pl.BlockSpec((1, block_len), lambda step, flags_ref: (0, step)),
        ],
        out_specs=pl.BlockSpec((query_count, head_dim), full),
        scratch_shapes=[
            pltpu.VMEM((query_count, 1), jnp.float32),
            pltpu.VMEM((query_count, 1), jnp.float32),
            pltpu.VMEM((query_count, head_dim), jnp.float32),
        ],
    )
    body = lambda *refs: flash_kernel(*refs, score_scale=score_scale, block_len=block_len)
    return pl.pallas_call(
        body,
        grid_spec=grid_spec,
        out_shape=jax.ShapeDtypeStruct((query_count, head_dim), jnp.bfloat16),
        interpret=interpret,
    )(flags, queries, keyvals, keyvals, row_token[:, None], row_tenant[:, None], key_tenant[None, :])


def swap_partner(values, axis_name, distance):
    count = lax.axis_size(axis_name)
    pairs = [(i, i ^ distance) for i in range(count)]
    return lax.ppermute(values, axis_name, pairs)


def lane_dense(values):
    flat = values.reshape(-1)
    return flat.reshape(-1, 128) if flat.shape[0] % 128 == 0 else flat.reshape(1, -1)


def gather_blocks(block, axis_name, distances):
    index = lax.axis_index(axis_name)
    shape = block.shape
    block = lane_dense(block)[None]
    stacked = block
    done = []
    for distance in distances:
        theirs = swap_partner(stacked, axis_name, distance)
        upper = (index // distance) % 2 == 1
        low = jnp.where(upper, theirs, stacked)
        high = jnp.where(upper, stacked, theirs)
        place = sum(1 for d in done if d > distance)
        stacked = jnp.stack([low, high], axis=place)
        done.append(distance)
    return stacked.reshape((-1,) + shape[1:])


def scatter_blocks(values, axis_name, distances, combine, send_type=None, dense=False):
    count = lax.axis_size(axis_name)
    index = lax.axis_index(axis_name)
    levels = count.bit_length() - 1
    rows = values.shape[0] // count
    part_shape = (rows,) + values.shape[1:]
    if dense:
        flat = math.prod(part_shape)
        part_shape = (flat // 128, 128) if flat % 128 == 0 else (1, flat)
    stacked = values.reshape((2,) * levels + part_shape)
    remaining = [count >> (j + 1) for j in range(levels)]
    for distance in distances:
        place = remaining.index(distance)
        low = lax.index_in_dim(stacked, 0, place, keepdims=False)
        high = lax.index_in_dim(stacked, 1, place, keepdims=False)
        upper = (index // distance) % 2 == 1
        keep = jnp.where(upper, high, low)
        send = jnp.where(upper, low, high)
        if send_type is not None:
            send = send.astype(send_type)
        received = swap_partner(send, axis_name, distance).astype(keep.dtype)
        stacked = combine(keep, received)
        remaining.pop(place)
    return stacked.reshape((rows,) + values.shape[1:])


def add_parts(first, second):
    return first + second


def merge_softmax(first, second, groups, head_dim):
    width = groups * head_dim
    first_max, second_max = first[..., width + groups:], second[..., width + groups:]
    top = jnp.maximum(first_max, second_max)
    first_scale = jnp.exp(first_max - top)
    second_scale = jnp.exp(second_max - top)
    acc = first[..., :width] * jnp.repeat(first_scale, head_dim, axis=-1) + second[
        ..., :width
    ] * jnp.repeat(second_scale, head_dim, axis=-1)
    total = first[..., width:width + groups] * first_scale + second[..., width:width + groups] * second_scale
    return jnp.concatenate([acc, total, top], axis=-1)

def shards(
    prefill_states,
    decode_states,
    attn_gain,
    query_weight,
    keyvalue_weight,
    output_weight,
    cache_keyval,
    cached_length,
    span_tenant,
    ffn_gain,
    expert_in,
    expert_out,
    routes,
    gate_values,
):
    seq_count = lax.axis_size("seq")
    tp_count = lax.axis_size("tp")
    seq_index = lax.axis_index("seq")
    tp_index = lax.axis_index("tp")
    pre_local, model_width = prefill_states.shape
    dec_local = decode_states.shape[0]
    heads_kv = keyvalue_weight.shape[1]
    head_dim = keyvalue_weight.shape[2] // 2
    heads_q = query_weight.shape[1] // head_dim
    query_group_count = heads_q // heads_kv
    score_scale = head_dim ** (-0.5)
    pre_share = pre_local // tp_count
    normalised_input = rms_norm(prefill_states, attn_gain)
    query_matrix = jnp.dot(
        normalised_input, query_weight, preferred_element_type=jnp.float32
    ).reshape(pre_local, heads_q, head_dim)
    keyvalue_rows = jnp.dot(
        normalised_input,
        keyvalue_weight.reshape(model_width, heads_kv * 2 * head_dim),
        preferred_element_type=jnp.float32,
    ).reshape(pre_local, heads_kv, 2 * head_dim)
    before = span_tables(span_tenant)
    token_index = seq_index * pre_local + jnp.arange(pre_local, dtype=jnp.int32)
    tenant, token_positions = token_tables(token_index, span_tenant, before)
    query_matrix = (
        apply_rotary(query_matrix, token_positions)
        .astype(jnp.bfloat16)
        .reshape(pre_local, heads_kv, query_group_count, head_dim)
    )
    rotated_keys = apply_rotary(keyvalue_rows[..., :head_dim], token_positions).astype(jnp.bfloat16)
    local_keyvals = jnp.concatenate(
        [rotated_keys, keyvalue_rows[..., head_dim:].astype(jnp.bfloat16)], axis=-1
    )
    seq_near_first = [1 << j for j in range(seq_count.bit_length() - 1)]
    key_piece = lax.all_gather(
        local_keyvals.reshape(pre_local, heads_kv * 2 * head_dim), "seq", axis=0, tiled=True
    ).reshape(-1, heads_kv, 2 * head_dim)
    piece_rows = key_piece.shape[0]
    block_len = math.gcd(piece_rows, key_block)
    blocks = key_piece.reshape(piece_rows // block_len, block_len, heads_kv, 2 * head_dim)
    query_count = pre_local * query_group_count
    query_rows = query_matrix.transpose(1, 0, 2, 3).reshape(heads_kv, query_count, head_dim)
    row_token = jnp.repeat(token_index, query_group_count)
    row_tenant = jnp.repeat(tenant, query_group_count)
    key_positions = jnp.arange(piece_rows, dtype=jnp.int32)
    key_tenant = token_tables(key_positions, span_tenant, before)[0]
    token_visible = (tenant[:, None] == key_tenant[None, :]) & (
        token_index[:, None] >= key_positions[None, :]
    )
    block_flags = jnp.any(
        token_visible.reshape(pre_local, piece_rows // block_len, block_len), axis=(0, 2)
    ).astype(jnp.int32)
    padded_queries = jnp.pad(query_rows, ((0, 0), (0, 0), (0, head_dim)))
    flat_keyvals = key_piece.reshape(piece_rows, heads_kv * 2 * head_dim)
    head_outputs = [
        flash_attend(
            block_flags,
            padded_queries[head],
            flat_keyvals,
            head,
            row_token,
            row_tenant,
            key_tenant,
            score_scale,
            block_len,
        )[:, head_dim:]
        for head in range(heads_kv)
    ]
    attended = (
        jnp.stack(head_outputs)
        .reshape(heads_kv, pre_local, query_group_count, head_dim)
        .transpose(1, 0, 2, 3)
        .reshape(pre_local, heads_q * head_dim)
    )
    prefill_part = jnp.dot(attended, output_weight, preferred_element_type=jnp.float32)
    tp_near_first = [1 << j for j in range(tp_count.bit_length() - 1)]
    prefill_sum = scatter_blocks(
        prefill_part, "tp", tp_near_first, add_parts, send_type=jnp.bfloat16, dense=True
    )
    group_states = gather_blocks(decode_states, "tp", tp_near_first[::-1])
    group_rows = group_states.shape[0]
    group_lengths = lax.dynamic_slice_in_dim(cached_length, seq_index * group_rows, group_rows, 0)
    decode_normalised = rms_norm(group_states, attn_gain)
    group_queries = jnp.dot(
        decode_normalised, query_weight, preferred_element_type=jnp.float32
    ).reshape(group_rows, heads_q, head_dim)
    group_queries = (
        apply_rotary(group_queries, group_lengths)
        .astype(jnp.bfloat16)
        .reshape(group_rows, heads_kv, query_group_count, head_dim)
    )
    decode_keyvalues = jnp.dot(
        decode_normalised,
        keyvalue_weight.reshape(model_width, heads_kv * 2 * head_dim),
        preferred_element_type=jnp.float32,
    ).reshape(group_rows, heads_kv, 2 * head_dim)
    new_keys = apply_rotary(decode_keyvalues[..., :head_dim], group_lengths).astype(jnp.bfloat16)
    new_vals = decode_keyvalues[..., head_dim:].astype(jnp.bfloat16)
    decode_queries = gather_blocks(group_queries, "seq", seq_near_first[::-1])
    cache_local = cache_keyval.shape[1]
    cache_pos = seq_index * cache_local + jnp.arange(cache_local, dtype=jnp.int32)
    visible = (cache_pos[None, :] < cached_length[:, None])[:, None, None, :]
    scores = (
        jnp.einsum(
            "bhgd,bkhd->bhgk",
            decode_queries,
            cache_keyval[..., :head_dim],
            preferred_element_type=jnp.float32,
        )
        * score_scale
    )
    scores = jnp.where(visible, scores, masked_score)
    local_max = jnp.max(scores, axis=-1)
    weights_exp = jnp.where(visible, jnp.exp(scores - local_max[..., None]), 0.0)
    local_total = jnp.sum(weights_exp, axis=-1)
    local_acc = jnp.einsum(
        "bhgk,bkhd->bhgd",
        weights_exp.astype(jnp.bfloat16),
        cache_keyval[..., head_dim:],
        preferred_element_type=jnp.float32,
    )
    dec_total = local_acc.shape[0]
    groups = heads_kv * query_group_count
    packed = jnp.concatenate(
        [
            local_acc.reshape(dec_total, groups * head_dim),
            local_total.reshape(dec_total, groups),
            local_max.reshape(dec_total, groups),
        ],
        axis=-1,
    )
    merged = scatter_blocks(
        packed, "seq", seq_near_first, lambda a, b: merge_softmax(a, b, groups, head_dim)
    )
    merged_acc = merged[:, : groups * head_dim].reshape(group_rows, heads_kv, query_group_count, head_dim)
    merged_total = merged[:, groups * head_dim : groups * (head_dim + 1)].reshape(
        group_rows, heads_kv, query_group_count
    )
    merged_max = merged[:, groups * (head_dim + 1) :].reshape(group_rows, heads_kv, query_group_count)
    own_score = (
        jnp.sum(
            group_queries.astype(jnp.float32) * new_keys.astype(jnp.float32)[:, :, None, :],
            axis=-1,
        )
        * score_scale
    )
    final_max = jnp.maximum(merged_max, own_score)
    rescale = jnp.exp(merged_max - final_max)
    own_exp = jnp.exp(own_score - final_max)
    final_total = merged_total * rescale + own_exp
    own_rounded = lax.optimization_barrier(own_exp.astype(jnp.bfloat16)).astype(jnp.float32)
    final_acc = (
        merged_acc * rescale[..., None]
        + own_rounded[..., None] * new_vals.astype(jnp.float32)[:, :, None, :]
    )
    decode_attended = (
        (final_acc / final_total[..., None])
        .astype(jnp.bfloat16)
        .reshape(group_rows, heads_q * head_dim)
    )
    decode_part = jnp.dot(decode_attended, output_weight, preferred_element_type=jnp.float32)
    decode_sum = scatter_blocks(decode_part, "tp", tp_near_first, add_parts, dense=True)
    own_states = lax.dynamic_slice_in_dim(prefill_states, tp_index * pre_share, pre_share, 0)
    prefill_h = (own_states.astype(jnp.float32) + prefill_sum).astype(jnp.bfloat16)
    decode_h = (decode_states.astype(jnp.float32) + decode_sum).astype(jnp.bfloat16)
    moe_in = jnp.concatenate([prefill_h, decode_h], axis=0)
    normed_moe = rms_norm(moe_in, ffn_gain)
    rows_dev, top_count = routes.shape
    capacity = 2 * ((rows_dev * top_count + EXPERTS - 1) // EXPERTS)
    flat_routes = routes.reshape(rows_dev * top_count)
    expert_ids = jnp.arange(EXPERTS, dtype=jnp.int32)
    onehot = (flat_routes[:, None] == expert_ids[None, :]).astype(jnp.int32)
    slot_rank = jnp.sum(jnp.cumsum(onehot, axis=0) * onehot, axis=1) - 1
    slot_index = flat_routes * capacity + slot_rank
    repeated = jnp.repeat(normed_moe, top_count, axis=0)
    buffer = jnp.zeros((EXPERTS * capacity, model_width), jnp.bfloat16).at[slot_index].set(repeated)
    outgoing = buffer.reshape(seq_count, EXPERTS // seq_count, capacity, model_width)
    hidden = jnp.einsum(
        "secd,edf->secf",
        lax.all_to_all(outgoing, "seq", split_axis=0, concat_axis=0, tiled=True),
        expert_in,
        preferred_element_type=jnp.float32,
    )
    ff_width = expert_out.shape[1]
    active = (jax.nn.silu(hidden[..., :ff_width]) * hidden[..., ff_width:]).astype(jnp.bfloat16)
    results = jnp.einsum(
        "secf,efd->secd", active, expert_out, preferred_element_type=jnp.float32
    ).astype(jnp.bfloat16)
    returned = lax.all_to_all(results, "seq", split_axis=0, concat_axis=0, tiled=True)
    fetched = (
        returned.reshape(EXPERTS * capacity, model_width)[slot_index]
        .astype(jnp.float32)
        .reshape(rows_dev, top_count, model_width)
    )
    combined = jnp.sum(fetched * gate_values[..., None], axis=1)
    layer_out = (moe_in.astype(jnp.float32) + combined).astype(jnp.bfloat16)
    return (layer_out[:pre_share], layer_out[pre_share:])


def solution(mesh):
    return jax.shard_map(
        shards,
        mesh=mesh,
        in_specs=(
            P("seq", None),
            P(("seq", "tp"), None),
            P(),
            P(None, "tp"),
            P(None, "tp", None),
            P("tp", None),
            P(None, "seq", "tp", None),
            P(),
            P(),
            P(),
            P("seq", None, None),
            P("seq", None, None),
            P(("seq", "tp"), None),
            P(("seq", "tp"), None),
        ),
        out_specs=(P(("seq", "tp"), None), P(("seq", "tp"), None)),
        check_vma=False,
    )
```

```python
import math

import jax
import jax.numpy as jnp
from jax import lax
from jax.sharding import PartitionSpec as P
from jax.experimental import pallas as pl
from jax.experimental.pallas import tpu as pltpu

EXPERTS = 32
SPAN = 2048


eps_norm = 1e-05
rope_base = 10000.0
masked_score = -1e30
key_block = 512


def rms_norm(values, scales):
    floats = values.astype(jnp.float32)
    factor = lax.rsqrt(jnp.mean(floats * floats, axis=-1, keepdims=True) + eps_norm)
    return (floats * factor * scales.astype(jnp.float32)).astype(jnp.bfloat16)


def apply_rotary(values, token_positions):
    half_dim = values.shape[-1] // 2
    frequency = rope_base ** (-2.0 * jnp.arange(half_dim, dtype=jnp.float32) / values.shape[-1])
    angles = token_positions.astype(jnp.float32)[:, None] * frequency[None, :]
    cosine = jnp.cos(angles)[:, None, :]
    sine_part = jnp.sin(angles)[:, None, :]
    first_half = values[..., :half_dim]
    second_half = values[..., half_dim:]
    return jnp.concatenate(
        [
            first_half * cosine - second_half * sine_part,
            second_half * cosine + first_half * sine_part,
        ],
        axis=-1,
    )


def span_tables(span_tenant):
    span_count = span_tenant.shape[0]
    ordinal = jnp.arange(span_count, dtype=jnp.int32)
    same_tenant = span_tenant[:, None] == span_tenant[None, :]
    earlier = ordinal[None, :] < ordinal[:, None]
    return jnp.sum(jnp.where(same_tenant & earlier, 1, 0), axis=1).astype(jnp.int32)


def token_tables(token_index, span_tenant, before):
    span_count = span_tenant.shape[0]
    span_index = token_index // SPAN
    onehot = span_index[:, None] == jnp.arange(span_count, dtype=jnp.int32)[None, :]
    tenant = jnp.sum(jnp.where(onehot, span_tenant[None, :], 0), axis=1)
    offset = jnp.sum(jnp.where(onehot, before[None, :], 0), axis=1)
    return (tenant, offset * SPAN + token_index % SPAN)


def attend_keys(fold_state, keyvalue_rows, visible, query_matrix, score_scale):
    run_max, run_total, run_acc = fold_state
    head_dim = keyvalue_rows.shape[-1] // 2
    scores = (
        jnp.einsum(
            "qhgd,khd->qhgk",
            query_matrix,
            keyvalue_rows[..., :head_dim],
            preferred_element_type=jnp.float32,
        )
        * score_scale
    )
    mask_full = visible[:, None, None, :]
    scores = jnp.where(mask_full, scores, masked_score)
    new_max = jnp.maximum(run_max, jnp.max(scores, axis=-1))
    weights_exp = jnp.where(mask_full, jnp.exp(scores - new_max[..., None]), 0.0)
    factor = jnp.exp(run_max - new_max)
    new_total = run_total * factor + jnp.sum(weights_exp, axis=-1)
    new_acc = run_acc * factor[..., None] + jnp.einsum(
        "qhgk,khd->qhgd",
        weights_exp.astype(jnp.bfloat16),
        keyvalue_rows[..., head_dim:],
        preferred_element_type=jnp.float32,
    )
    return (new_max, new_total, new_acc)


def flash_kernel(
    flags_ref, q_ref, k_ref, v_ref, row_token_ref, row_tenant_ref, key_tenant_ref,
    o_ref, max_ref, total_ref, acc_ref, *, score_scale, block_len
):
    step = pl.program_id(0)

    @pl.when(step == 0)
    def _():
        max_ref[...] = jnp.full(max_ref.shape, masked_score, jnp.float32)
        total_ref[...] = jnp.zeros(total_ref.shape, jnp.float32)
        acc_ref[...] = jnp.zeros(acc_ref.shape, jnp.float32)

    @pl.when(flags_ref[step] != 0)
    def _():
        scores = (
            lax.dot_general(
                q_ref[...], v_ref[...], (((1,), (1,)), ((), ())),
                preferred_element_type=jnp.float32,
            )
            * score_scale
        )
        key_index = step * block_len + lax.broadcasted_iota(jnp.int32, (1, block_len), 1)
        visible = (row_tenant_ref[...] == key_tenant_ref[...]) & (
            row_token_ref[...] >= key_index
        )
        scores = jnp.where(visible, scores, masked_score)
        run_max = max_ref[...]
        new_max = jnp.maximum(run_max, jnp.max(scores, axis=-1, keepdims=True))
        weights_exp = jnp.where(visible, jnp.exp(scores - new_max), 0.0)
        factor = jnp.exp(run_max - new_max)
        total_ref[...] = total_ref[...] * factor + jnp.sum(weights_exp, axis=-1, keepdims=True)
        acc_ref[...] = acc_ref[...] * factor + jnp.dot(
            weights_exp.astype(jnp.bfloat16), v_ref[...], preferred_element_type=jnp.float32
        )
        max_ref[...] = new_max

    @pl.when(step == pl.num_programs(0) - 1)
    def _():
        o_ref[...] = (acc_ref[...] / total_ref[...]).astype(o_ref.dtype)


def flash_attend(flags, queries, keyvals, head, row_token, row_tenant, key_tenant, score_scale, block_len, interpret=False):
    query_count, head_dim = queries.shape
    key_count = keyvals.shape[0]
    full = lambda step, flags_ref: (0, 0)
    grid_spec = pltpu.PrefetchScalarGridSpec(
        num_scalar_prefetch=1,
        grid=(key_count // block_len,),
        in_specs=[
            pl.BlockSpec((query_count, head_dim), full),
            pl.BlockSpec((block_len, head_dim), lambda step, flags_ref: (step, head)),
            pl.BlockSpec((block_len, head_dim), lambda step, flags_ref: (step, head)),
            pl.BlockSpec((query_count, 1), full),
            pl.BlockSpec((query_count, 1), full),
            pl.BlockSpec((1, block_len), lambda step, flags_ref: (0, step)),
        ],
        out_specs=pl.BlockSpec((query_count, head_dim), full),
        scratch_shapes=[
            pltpu.VMEM((query_count, 1), jnp.float32),
            pltpu.VMEM((query_count, 1), jnp.float32),
            pltpu.VMEM((query_count, head_dim), jnp.float32),
        ],
    )
    body = lambda *refs: flash_kernel(*refs, score_scale=score_scale, block_len=block_len)
    return pl.pallas_call(
        body,
        grid_spec=grid_spec,
        out_shape=jax.ShapeDtypeStruct((query_count, head_dim), jnp.bfloat16),
        interpret=interpret,
    )(flags, queries, keyvals, keyvals, row_token[:, None], row_tenant[:, None], key_tenant[None, :])


def swap_partner(values, axis_name, distance):
    count = lax.axis_size(axis_name)
    pairs = [(i, i ^ distance) for i in range(count)]
    return lax.ppermute(values, axis_name, pairs)


def lane_dense(values):
    flat = values.reshape(-1)
    return flat.reshape(-1, 128) if flat.shape[0] % 128 == 0 else flat.reshape(1, -1)


def gather_blocks(block, axis_name, distances):
    index = lax.axis_index(axis_name)
    shape = block.shape
    block = lane_dense(block)[None]
    stacked = block
    done = []
    for distance in distances:
        theirs = swap_partner(stacked, axis_name, distance)
        upper = (index // distance) % 2 == 1
        low = jnp.where(upper, theirs, stacked)
        high = jnp.where(upper, stacked, theirs)
        place = sum(1 for d in done if d > distance)
        stacked = jnp.stack([low, high], axis=place)
        done.append(distance)
    return stacked.reshape((-1,) + shape[1:])


def scatter_blocks(values, axis_name, distances, combine, send_type=None, dense=False):
    count = lax.axis_size(axis_name)
    index = lax.axis_index(axis_name)
    levels = count.bit_length() - 1
    rows = values.shape[0] // count
    part_shape = (rows,) + values.shape[1:]
    if dense:
        flat = math.prod(part_shape)
        part_shape = (flat // 128, 128) if flat % 128 == 0 else (1, flat)
    stacked = values.reshape((2,) * levels + part_shape)
    remaining = [count >> (j + 1) for j in range(levels)]
    for distance in distances:
        place = remaining.index(distance)
        low = lax.index_in_dim(stacked, 0, place, keepdims=False)
        high = lax.index_in_dim(stacked, 1, place, keepdims=False)
        upper = (index // distance) % 2 == 1
        keep = jnp.where(upper, high, low)
        send = jnp.where(upper, low, high)
        if send_type is not None:
            send = send.astype(send_type)
        received = swap_partner(send, axis_name, distance).astype(keep.dtype)
        stacked = combine(keep, received)
        remaining.pop(place)
    return stacked.reshape((rows,) + values.shape[1:])


def add_parts(first, second):
    return first + second


def merge_softmax(first, second, groups, head_dim):
    width = groups * head_dim
    first_max, second_max = first[..., width + groups:], second[..., width + groups:]
    top = jnp.maximum(first_max, second_max)
    first_scale = jnp.exp(first_max - top)
    second_scale = jnp.exp(second_max - top)
    acc = first[..., :width] * jnp.repeat(first_scale, head_dim, axis=-1) + second[
        ..., :width
    ] * jnp.repeat(second_scale, head_dim, axis=-1)
    total = first[..., width:width + groups] * first_scale + second[..., width:width + groups] * second_scale
    return jnp.concatenate([acc, total, top], axis=-1)

def shards(
    prefill_states,
    decode_states,
    attn_gain,
    query_weight,
    keyvalue_weight,
    output_weight,
    cache_keyval,
    cached_length,
    span_tenant,
    ffn_gain,
    expert_in,
    expert_out,
    routes,
    gate_values,
):
    seq_count = lax.axis_size("seq")
    tp_count = lax.axis_size("tp")
    seq_index = lax.axis_index("seq")
    tp_index = lax.axis_index("tp")
    pre_local, model_width = prefill_states.shape
    dec_local = decode_states.shape[0]
    heads_kv = keyvalue_weight.shape[1]
    head_dim = keyvalue_weight.shape[2] // 2
    heads_q = query_weight.shape[1] // head_dim
    query_group_count = heads_q // heads_kv
    score_scale = head_dim ** (-0.5)
    pre_share = pre_local // tp_count
    normalised_input = rms_norm(prefill_states, attn_gain)
    query_matrix = jnp.dot(
        normalised_input, query_weight, preferred_element_type=jnp.float32
    ).reshape(pre_local, heads_q, head_dim)
    keyvalue_rows = jnp.dot(
        normalised_input,
        keyvalue_weight.reshape(model_width, heads_kv * 2 * head_dim),
        preferred_element_type=jnp.float32,
    ).reshape(pre_local, heads_kv, 2 * head_dim)
    before = span_tables(span_tenant)
    token_index = seq_index * pre_local + jnp.arange(pre_local, dtype=jnp.int32)
    tenant, token_positions = token_tables(token_index, span_tenant, before)
    query_matrix = (
        apply_rotary(query_matrix, token_positions)
        .astype(jnp.bfloat16)
        .reshape(pre_local, heads_kv, query_group_count, head_dim)
    )
    rotated_keys = apply_rotary(keyvalue_rows[..., :head_dim], token_positions).astype(jnp.bfloat16)
    local_keyvals = jnp.concatenate(
        [rotated_keys, keyvalue_rows[..., head_dim:].astype(jnp.bfloat16)], axis=-1
    )
    seq_near_first = [1 << j for j in range(seq_count.bit_length() - 1)]
    key_piece = lax.all_gather(
        local_keyvals.reshape(pre_local, heads_kv * 2 * head_dim), "seq", axis=0, tiled=True
    ).reshape(-1, heads_kv, 2 * head_dim)
    piece_rows = key_piece.shape[0]
    block_len = math.gcd(piece_rows, key_block)
    blocks = key_piece.reshape(piece_rows // block_len, block_len, heads_kv, 2 * head_dim)
    query_count = pre_local * query_group_count
    query_rows = query_matrix.transpose(1, 0, 2, 3).reshape(heads_kv, query_count, head_dim)
    row_token = jnp.repeat(token_index, query_group_count)
    row_tenant = jnp.repeat(tenant, query_group_count)
    key_positions = jnp.arange(piece_rows, dtype=jnp.int32)
    key_tenant = token_tables(key_positions, span_tenant, before)[0]
    token_visible = (tenant[:, None] == key_tenant[None, :]) & (
        token_index[:, None] >= key_positions[None, :]
    )
    block_flags = jnp.any(
        token_visible.reshape(pre_local, piece_rows // block_len, block_len), axis=(0, 2)
    ).astype(jnp.int32)
    padded_queries = jnp.pad(query_rows, ((0, 0), (0, 0), (0, head_dim)))
    flat_keyvals = key_piece.reshape(piece_rows, heads_kv * 2 * head_dim)
    head_outputs = [
        flash_attend(
            block_flags,
            padded_queries[head],
            flat_keyvals,
            head,
            row_token,
            row_tenant,
            key_tenant,
            score_scale,
            block_len,
        )[:, head_dim:]
        for head in range(heads_kv)
    ]
    attended = (
        jnp.stack(head_outputs)
        .reshape(heads_kv, pre_local, query_group_count, head_dim)
        .transpose(1, 0, 2, 3)
        .reshape(pre_local, heads_q * head_dim)
    )
    prefill_part = jnp.dot(attended, output_weight, preferred_element_type=jnp.float32)
    tp_near_first = [1 << j for j in range(tp_count.bit_length() - 1)]
    prefill_sum = scatter_blocks(
        prefill_part, "tp", tp_near_first, add_parts, send_type=jnp.bfloat16, dense=True
    )
    group_states = gather_blocks(decode_states, "tp", tp_near_first[::-1])
    group_rows = group_states.shape[0]
    group_lengths = lax.dynamic_slice_in_dim(cached_length, seq_index * group_rows, group_rows, 0)
    decode_normalised = rms_norm(group_states, attn_gain)
    group_queries = jnp.dot(
        decode_normalised, query_weight, preferred_element_type=jnp.float32
    ).reshape(group_rows, heads_q, head_dim)
    group_queries = (
        apply_rotary(group_queries, group_lengths)
        .astype(jnp.bfloat16)
        .reshape(group_rows, heads_kv, query_group_count, head_dim)
    )
    decode_keyvalues = jnp.dot(
        decode_normalised,
        keyvalue_weight.reshape(model_width, heads_kv * 2 * head_dim),
        preferred_element_type=jnp.float32,
    ).reshape(group_rows, heads_kv, 2 * head_dim)
    new_keys = apply_rotary(decode_keyvalues[..., :head_dim], group_lengths).astype(jnp.bfloat16)
    new_vals = decode_keyvalues[..., head_dim:].astype(jnp.bfloat16)
    decode_queries = gather_blocks(group_queries, "seq", seq_near_first[::-1])
    cache_local = cache_keyval.shape[1]
    cache_pos = seq_index * cache_local + jnp.arange(cache_local, dtype=jnp.int32)
    visible = (cache_pos[None, :] < cached_length[:, None])[:, None, None, :]
    scores = (
        jnp.einsum(
            "bhgd,bkhd->bhgk",
            decode_queries,
            cache_keyval[..., :head_dim],
            preferred_element_type=jnp.float32,
        )
        * score_scale
    )
    scores = jnp.where(visible, scores, masked_score)
    local_max = jnp.max(scores, axis=-1)
    weights_exp = jnp.where(visible, jnp.exp(scores - local_max[..., None]), 0.0)
    local_total = jnp.sum(weights_exp, axis=-1)
    local_acc = jnp.einsum(
        "bhgk,bkhd->bhgd",
        weights_exp.astype(jnp.bfloat16),
        cache_keyval[..., head_dim:],
        preferred_element_type=jnp.float32,
    )
    dec_total = local_acc.shape[0]
    groups = heads_kv * query_group_count
    packed = jnp.concatenate(
        [
            local_acc.reshape(dec_total, groups * head_dim),
            local_total.reshape(dec_total, groups),
            local_max.reshape(dec_total, groups),
        ],
        axis=-1,
    )
    merged = scatter_blocks(
        packed, "seq", seq_near_first, lambda a, b: merge_softmax(a, b, groups, head_dim)
    )
    merged_acc = merged[:, : groups * head_dim].reshape(group_rows, heads_kv, query_group_count, head_dim)
    merged_total = merged[:, groups * head_dim : groups * (head_dim + 1)].reshape(
        group_rows, heads_kv, query_group_count
    )
    merged_max = merged[:, groups * (head_dim + 1) :].reshape(group_rows, heads_kv, query_group_count)
    own_score = (
        jnp.sum(
            group_queries.astype(jnp.float32) * new_keys.astype(jnp.float32)[:, :, None, :],
            axis=-1,
        )
        * score_scale
    )
    final_max = jnp.maximum(merged_max, own_score)
    rescale = jnp.exp(merged_max - final_max)
    own_exp = jnp.exp(own_score - final_max)
    final_total = merged_total * rescale + own_exp
    own_rounded = lax.optimization_barrier(own_exp.astype(jnp.bfloat16)).astype(jnp.float32)
    final_acc = (
        merged_acc * rescale[..., None]
        + own_rounded[..., None] * new_vals.astype(jnp.float32)[:, :, None, :]
    )
    decode_attended = (
        (final_acc / final_total[..., None])
        .astype(jnp.bfloat16)
        .reshape(group_rows, heads_q * head_dim)
    )
    decode_part = jnp.dot(decode_attended, output_weight, preferred_element_type=jnp.float32)
    decode_sum = scatter_blocks(decode_part, "tp", tp_near_first, add_parts, dense=True)
    own_states = lax.dynamic_slice_in_dim(prefill_states, tp_index * pre_share, pre_share, 0)
    prefill_h = (own_states.astype(jnp.float32) + prefill_sum).astype(jnp.bfloat16)
    decode_h = (decode_states.astype(jnp.float32) + decode_sum).astype(jnp.bfloat16)
    moe_in = jnp.concatenate([prefill_h, decode_h], axis=0)
    normed_moe = rms_norm(moe_in, ffn_gain)
    rows_dev, top_count = routes.shape
    capacity = 2 * ((rows_dev * top_count + EXPERTS - 1) // EXPERTS)
    capacity = -(-capacity // 8) * 8
    flat_routes = routes.reshape(rows_dev * top_count)
    expert_ids = jnp.arange(EXPERTS, dtype=jnp.int32)
    onehot = (flat_routes[:, None] == expert_ids[None, :]).astype(jnp.int32)
    slot_rank = jnp.sum(jnp.cumsum(onehot, axis=0) * onehot, axis=1) - 1
    slot_index = flat_routes * capacity + slot_rank
    repeated = jnp.repeat(normed_moe, top_count, axis=0)
    buffer = jnp.zeros((EXPERTS * capacity, model_width), jnp.bfloat16).at[slot_index].set(repeated)
    outgoing = buffer.reshape(seq_count, EXPERTS // seq_count, capacity, model_width)
    hidden = jnp.einsum(
        "secd,edf->secf",
        lax.all_to_all(outgoing, "seq", split_axis=0, concat_axis=0, tiled=True),
        expert_in,
        preferred_element_type=jnp.float32,
    )
    ff_width = expert_out.shape[1]
    active = (jax.nn.silu(hidden[..., :ff_width]) * hidden[..., ff_width:]).astype(jnp.bfloat16)
    results = jnp.einsum(
        "secf,efd->secd", active, expert_out, preferred_element_type=jnp.float32
    ).astype(jnp.bfloat16)
    returned = lax.all_to_all(results, "seq", split_axis=0, concat_axis=0, tiled=True)
    fetched = (
        returned.reshape(EXPERTS * capacity, model_width)[slot_index]
        .astype(jnp.float32)
        .reshape(rows_dev, top_count, model_width)
    )
    combined = jnp.sum(fetched * gate_values[..., None], axis=1)
    layer_out = (moe_in.astype(jnp.float32) + combined).astype(jnp.bfloat16)
    return (layer_out[:pre_share], layer_out[pre_share:])


def solution(mesh):
    return jax.shard_map(
        shards,
        mesh=mesh,
        in_specs=(
            P("seq", None),
            P(("seq", "tp"), None),
            P(),
            P(None, "tp"),
            P(None, "tp", None),
            P("tp", None),
            P(None, "seq", "tp", None),
            P(),
            P(),
            P(),
            P("seq", None, None),
            P("seq", None, None),
            P(("seq", "tp"), None),
            P(("seq", "tp"), None),
        ),
        out_specs=(P(("seq", "tp"), None), P(("seq", "tp"), None)),
        check_vma=False,
    )
```

```python
import math

import jax
import jax.numpy as jnp
from jax import lax
from jax.sharding import PartitionSpec as P
from jax.experimental import pallas as pl
from jax.experimental.pallas import tpu as pltpu

EXPERTS = 32
SPAN = 2048


eps_norm = 1e-05
rope_base = 10000.0
masked_score = -1e30
key_block = 512


def rms_norm(values, scales):
    floats = values.astype(jnp.float32)
    factor = lax.rsqrt(jnp.mean(floats * floats, axis=-1, keepdims=True) + eps_norm)
    return (floats * factor * scales.astype(jnp.float32)).astype(jnp.bfloat16)


def apply_rotary(values, token_positions):
    half_dim = values.shape[-1] // 2
    frequency = rope_base ** (-2.0 * jnp.arange(half_dim, dtype=jnp.float32) / values.shape[-1])
    angles = token_positions.astype(jnp.float32)[:, None] * frequency[None, :]
    cosine = jnp.cos(angles)[:, None, :]
    sine_part = jnp.sin(angles)[:, None, :]
    first_half = values[..., :half_dim]
    second_half = values[..., half_dim:]
    return jnp.concatenate(
        [
            first_half * cosine - second_half * sine_part,
            second_half * cosine + first_half * sine_part,
        ],
        axis=-1,
    )


def span_tables(span_tenant):
    span_count = span_tenant.shape[0]
    ordinal = jnp.arange(span_count, dtype=jnp.int32)
    same_tenant = span_tenant[:, None] == span_tenant[None, :]
    earlier = ordinal[None, :] < ordinal[:, None]
    return jnp.sum(jnp.where(same_tenant & earlier, 1, 0), axis=1).astype(jnp.int32)


def token_tables(token_index, span_tenant, before):
    span_count = span_tenant.shape[0]
    span_index = token_index // SPAN
    onehot = span_index[:, None] == jnp.arange(span_count, dtype=jnp.int32)[None, :]
    tenant = jnp.sum(jnp.where(onehot, span_tenant[None, :], 0), axis=1)
    offset = jnp.sum(jnp.where(onehot, before[None, :], 0), axis=1)
    return (tenant, offset * SPAN + token_index % SPAN)


def attend_keys(fold_state, keyvalue_rows, visible, query_matrix, score_scale):
    run_max, run_total, run_acc = fold_state
    head_dim = keyvalue_rows.shape[-1] // 2
    scores = (
        jnp.einsum(
            "qhgd,khd->qhgk",
            query_matrix,
            keyvalue_rows[..., :head_dim],
            preferred_element_type=jnp.float32,
        )
        * score_scale
    )
    mask_full = visible[:, None, None, :]
    scores = jnp.where(mask_full, scores, masked_score)
    new_max = jnp.maximum(run_max, jnp.max(scores, axis=-1))
    weights_exp = jnp.where(mask_full, jnp.exp(scores - new_max[..., None]), 0.0)
    factor = jnp.exp(run_max - new_max)
    new_total = run_total * factor + jnp.sum(weights_exp, axis=-1)
    new_acc = run_acc * factor[..., None] + jnp.einsum(
        "qhgk,khd->qhgd",
        weights_exp.astype(jnp.bfloat16),
        keyvalue_rows[..., head_dim:],
        preferred_element_type=jnp.float32,
    )
    return (new_max, new_total, new_acc)


def flash_kernel(
    flags_ref, q_ref, k_ref, v_ref, row_token_ref, row_tenant_ref, key_tenant_ref,
    o_ref, max_ref, total_ref, acc_ref, *, score_scale, block_len
):
    step = pl.program_id(0)

    @pl.when(step == 0)
    def _():
        max_ref[...] = jnp.full(max_ref.shape, masked_score, jnp.float32)
        total_ref[...] = jnp.zeros(total_ref.shape, jnp.float32)
        acc_ref[...] = jnp.zeros(acc_ref.shape, jnp.float32)

    @pl.when(flags_ref[step] != 0)
    def _():
        scores = (
            lax.dot_general(
                q_ref[...], v_ref[...], (((1,), (1,)), ((), ())),
                preferred_element_type=jnp.float32,
            )
            * score_scale
        )
        key_index = step * block_len + lax.broadcasted_iota(jnp.int32, (1, block_len), 1)
        visible = (row_tenant_ref[...] == key_tenant_ref[...]) & (
            row_token_ref[...] >= key_index
        )
        scores = jnp.where(visible, scores, masked_score)
        run_max = max_ref[...]
        new_max = jnp.maximum(run_max, jnp.max(scores, axis=-1, keepdims=True))
        weights_exp = jnp.where(visible, jnp.exp(scores - new_max), 0.0)
        factor = jnp.exp(run_max - new_max)
        total_ref[...] = total_ref[...] * factor + jnp.sum(weights_exp, axis=-1, keepdims=True)
        acc_ref[...] = acc_ref[...] * factor + jnp.dot(
            weights_exp.astype(jnp.bfloat16), v_ref[...], preferred_element_type=jnp.float32
        )
        max_ref[...] = new_max

    @pl.when(step == pl.num_programs(0) - 1)
    def _():
        o_ref[...] = (acc_ref[...] / total_ref[...]).astype(o_ref.dtype)


def flash_attend(flags, queries, keyvals, head, row_token, row_tenant, key_tenant, score_scale, block_len, interpret=False):
    query_count, head_dim = queries.shape
    key_count = keyvals.shape[0]
    full = lambda step, flags_ref: (0, 0)
    grid_spec = pltpu.PrefetchScalarGridSpec(
        num_scalar_prefetch=1,
        grid=(key_count // block_len,),
        in_specs=[
            pl.BlockSpec((query_count, head_dim), full),
            pl.BlockSpec((block_len, head_dim), lambda step, flags_ref: (step, head)),
            pl.BlockSpec((block_len, head_dim), lambda step, flags_ref: (step, head)),
            pl.BlockSpec((query_count, 1), full),
            pl.BlockSpec((query_count, 1), full),
            pl.BlockSpec((1, block_len), lambda step, flags_ref: (0, step)),
        ],
        out_specs=pl.BlockSpec((query_count, head_dim), full),
        scratch_shapes=[
            pltpu.VMEM((query_count, 1), jnp.float32),
            pltpu.VMEM((query_count, 1), jnp.float32),
            pltpu.VMEM((query_count, head_dim), jnp.float32),
        ],
    )
    body = lambda *refs: flash_kernel(*refs, score_scale=score_scale, block_len=block_len)
    return pl.pallas_call(
        body,
        grid_spec=grid_spec,
        out_shape=jax.ShapeDtypeStruct((query_count, head_dim), jnp.bfloat16),
        interpret=interpret,
    )(flags, queries, keyvals, keyvals, row_token[:, None], row_tenant[:, None], key_tenant[None, :])


def swap_partner(values, axis_name, distance):
    count = lax.axis_size(axis_name)
    pairs = [(i, i ^ distance) for i in range(count)]
    return lax.ppermute(values, axis_name, pairs)


def lane_dense(values):
    flat = values.reshape(-1)
    return flat.reshape(-1, 128) if flat.shape[0] % 128 == 0 else flat.reshape(1, -1)


def gather_blocks(block, axis_name, distances):
    index = lax.axis_index(axis_name)
    shape = block.shape
    block = lane_dense(block)[None]
    stacked = block
    done = []
    for distance in distances:
        theirs = swap_partner(stacked, axis_name, distance)
        upper = (index // distance) % 2 == 1
        low = jnp.where(upper, theirs, stacked)
        high = jnp.where(upper, stacked, theirs)
        place = sum(1 for d in done if d > distance)
        stacked = jnp.stack([low, high], axis=place)
        done.append(distance)
    return stacked.reshape((-1,) + shape[1:])


def scatter_blocks(values, axis_name, distances, combine, send_type=None, dense=False):
    count = lax.axis_size(axis_name)
    index = lax.axis_index(axis_name)
    levels = count.bit_length() - 1
    rows = values.shape[0] // count
    part_shape = (rows,) + values.shape[1:]
    if dense:
        flat = math.prod(part_shape)
        part_shape = (flat // 128, 128) if flat % 128 == 0 else (1, flat)
    stacked = values.reshape((2,) * levels + part_shape)
    remaining = [count >> (j + 1) for j in range(levels)]
    for distance in distances:
        place = remaining.index(distance)
        low = lax.index_in_dim(stacked, 0, place, keepdims=False)
        high = lax.index_in_dim(stacked, 1, place, keepdims=False)
        upper = (index // distance) % 2 == 1
        keep = jnp.where(upper, high, low)
        send = jnp.where(upper, low, high)
        if send_type is not None:
            send = send.astype(send_type)
        received = swap_partner(send, axis_name, distance).astype(keep.dtype)
        stacked = combine(keep, received)
        remaining.pop(place)
    return stacked.reshape((rows,) + values.shape[1:])


def add_parts(first, second):
    return first + second


def merge_softmax(first, second, groups, head_dim):
    width = groups * head_dim
    first_max, second_max = first[..., width + groups:], second[..., width + groups:]
    top = jnp.maximum(first_max, second_max)
    first_scale = jnp.exp(first_max - top)
    second_scale = jnp.exp(second_max - top)
    acc = first[..., :width] * jnp.repeat(first_scale, head_dim, axis=-1) + second[
        ..., :width
    ] * jnp.repeat(second_scale, head_dim, axis=-1)
    total = first[..., width:width + groups] * first_scale + second[..., width:width + groups] * second_scale
    return jnp.concatenate([acc, total, top], axis=-1)

def shards(
    prefill_states,
    decode_states,
    attn_gain,
    query_weight,
    keyvalue_weight,
    output_weight,
    cache_keyval,
    cached_length,
    span_tenant,
    ffn_gain,
    expert_in,
    expert_out,
    routes,
    gate_values,
):
    seq_count = lax.axis_size("seq")
    tp_count = lax.axis_size("tp")
    seq_index = lax.axis_index("seq")
    tp_index = lax.axis_index("tp")
    pre_local, model_width = prefill_states.shape
    dec_local = decode_states.shape[0]
    heads_kv = keyvalue_weight.shape[1]
    head_dim = keyvalue_weight.shape[2] // 2
    heads_q = query_weight.shape[1] // head_dim
    query_group_count = heads_q // heads_kv
    score_scale = head_dim ** (-0.5)
    pre_share = pre_local // tp_count
    normalised_input = rms_norm(prefill_states, attn_gain)
    query_matrix = jnp.dot(
        normalised_input, query_weight, preferred_element_type=jnp.float32
    ).reshape(pre_local, heads_q, head_dim)
    keyvalue_rows = jnp.dot(
        normalised_input,
        keyvalue_weight.reshape(model_width, heads_kv * 2 * head_dim),
        preferred_element_type=jnp.float32,
    ).reshape(pre_local, heads_kv, 2 * head_dim)
    before = span_tables(span_tenant)
    token_index = seq_index * pre_local + jnp.arange(pre_local, dtype=jnp.int32)
    tenant, token_positions = token_tables(token_index, span_tenant, before)
    query_matrix = (
        apply_rotary(query_matrix, token_positions)
        .astype(jnp.bfloat16)
        .reshape(pre_local, heads_kv, query_group_count, head_dim)
    )
    rotated_keys = apply_rotary(keyvalue_rows[..., :head_dim], token_positions).astype(jnp.bfloat16)
    local_keyvals = jnp.concatenate(
        [rotated_keys, keyvalue_rows[..., head_dim:].astype(jnp.bfloat16)], axis=-1
    )
    seq_near_first = [1 << j for j in range(seq_count.bit_length() - 1)]
    key_piece = lax.all_gather(
        local_keyvals.reshape(pre_local, heads_kv * 2 * head_dim), "seq", axis=0, tiled=True
    ).reshape(-1, heads_kv, 2 * head_dim)
    piece_rows = key_piece.shape[0]
    block_len = math.gcd(piece_rows, key_block)
    blocks = key_piece.reshape(piece_rows // block_len, block_len, heads_kv, 2 * head_dim)
    query_count = pre_local * query_group_count
    query_rows = query_matrix.transpose(1, 0, 2, 3).reshape(heads_kv, query_count, head_dim)
    row_token = jnp.repeat(token_index, query_group_count)
    row_tenant = jnp.repeat(tenant, query_group_count)
    key_positions = jnp.arange(piece_rows, dtype=jnp.int32)
    key_tenant = token_tables(key_positions, span_tenant, before)[0]
    token_visible = (tenant[:, None] == key_tenant[None, :]) & (
        token_index[:, None] >= key_positions[None, :]
    )
    block_flags = jnp.any(
        token_visible.reshape(pre_local, piece_rows // block_len, block_len), axis=(0, 2)
    ).astype(jnp.int32)
    padded_queries = jnp.pad(query_rows, ((0, 0), (0, 0), (0, head_dim)))
    flat_keyvals = key_piece.reshape(piece_rows, heads_kv * 2 * head_dim)
    head_outputs = [
        flash_attend(
            block_flags,
            padded_queries[head],
            flat_keyvals,
            head,
            row_token,
            row_tenant,
            key_tenant,
            score_scale,
            block_len,
        )[:, head_dim:]
        for head in range(heads_kv)
    ]
    attended = (
        jnp.stack(head_outputs)
        .reshape(heads_kv, pre_local, query_group_count, head_dim)
        .transpose(1, 0, 2, 3)
        .reshape(pre_local, heads_q * head_dim)
    )
    prefill_part = jnp.dot(attended, output_weight, preferred_element_type=jnp.float32)
    tp_near_first = [1 << j for j in range(tp_count.bit_length() - 1)]
    prefill_sum = scatter_blocks(
        prefill_part, "tp", tp_near_first, add_parts, send_type=jnp.bfloat16, dense=True
    )
    group_states = gather_blocks(decode_states, "tp", tp_near_first[::-1])
    group_rows = group_states.shape[0]
    group_lengths = lax.dynamic_slice_in_dim(cached_length, seq_index * group_rows, group_rows, 0)
    decode_normalised = rms_norm(group_states, attn_gain)
    group_queries = jnp.dot(
        decode_normalised, query_weight, preferred_element_type=jnp.float32
    ).reshape(group_rows, heads_q, head_dim)
    group_queries = (
        apply_rotary(group_queries, group_lengths)
        .astype(jnp.bfloat16)
        .reshape(group_rows, heads_kv, query_group_count, head_dim)
    )
    decode_keyvalues = jnp.dot(
        decode_normalised,
        keyvalue_weight.reshape(model_width, heads_kv * 2 * head_dim),
        preferred_element_type=jnp.float32,
    ).reshape(group_rows, heads_kv, 2 * head_dim)
    new_keys = apply_rotary(decode_keyvalues[..., :head_dim], group_lengths).astype(jnp.bfloat16)
    new_vals = decode_keyvalues[..., head_dim:].astype(jnp.bfloat16)
    decode_queries = gather_blocks(group_queries, "seq", seq_near_first[::-1])
    cache_local = cache_keyval.shape[1]
    cache_pos = seq_index * cache_local + jnp.arange(cache_local, dtype=jnp.int32)
    visible = (cache_pos[None, :] < cached_length[:, None])[:, None, None, :]
    scores = (
        jnp.einsum(
            "bhgd,bkhd->bhgk",
            decode_queries,
            cache_keyval[..., :head_dim],
            preferred_element_type=jnp.float32,
        )
        * score_scale
    )
    scores = jnp.where(visible, scores, masked_score)
    local_max = jnp.max(scores, axis=-1)
    weights_exp = jnp.where(visible, jnp.exp(scores - local_max[..., None]), 0.0)
    local_total = jnp.sum(weights_exp, axis=-1)
    local_acc = jnp.einsum(
        "bhgk,bkhd->bhgd",
        weights_exp.astype(jnp.bfloat16),
        cache_keyval[..., head_dim:],
        preferred_element_type=jnp.float32,
    )
    dec_total = local_acc.shape[0]
    groups = heads_kv * query_group_count
    packed = jnp.concatenate(
        [
            local_acc.reshape(dec_total, groups * head_dim),
            local_total.reshape(dec_total, groups),
            local_max.reshape(dec_total, groups),
        ],
        axis=-1,
    )
    merged = scatter_blocks(
        packed, "seq", seq_near_first, lambda a, b: merge_softmax(a, b, groups, head_dim)
    )
    merged_acc = merged[:, : groups * head_dim].reshape(group_rows, heads_kv, query_group_count, head_dim)
    merged_total = merged[:, groups * head_dim : groups * (head_dim + 1)].reshape(
        group_rows, heads_kv, query_group_count
    )
    merged_max = merged[:, groups * (head_dim + 1) :].reshape(group_rows, heads_kv, query_group_count)
    own_score = (
        jnp.sum(
            group_queries.astype(jnp.float32) * new_keys.astype(jnp.float32)[:, :, None, :],
            axis=-1,
        )
        * score_scale
    )
    final_max = jnp.maximum(merged_max, own_score)
    rescale = jnp.exp(merged_max - final_max)
    own_exp = jnp.exp(own_score - final_max)
    final_total = merged_total * rescale + own_exp
    own_rounded = lax.optimization_barrier(own_exp.astype(jnp.bfloat16)).astype(jnp.float32)
    final_acc = (
        merged_acc * rescale[..., None]
        + own_rounded[..., None] * new_vals.astype(jnp.float32)[:, :, None, :]
    )
    decode_attended = (
        (final_acc / final_total[..., None])
        .astype(jnp.bfloat16)
        .reshape(group_rows, heads_q * head_dim)
    )
    decode_part = jnp.dot(decode_attended, output_weight, preferred_element_type=jnp.float32)
    decode_sum = scatter_blocks(decode_part, "tp", tp_near_first, add_parts, dense=True)
    own_states = lax.dynamic_slice_in_dim(prefill_states, tp_index * pre_share, pre_share, 0)
    prefill_h = (own_states.astype(jnp.float32) + prefill_sum).astype(jnp.bfloat16)
    decode_h = (decode_states.astype(jnp.float32) + decode_sum).astype(jnp.bfloat16)
    moe_in = jnp.concatenate([prefill_h, decode_h], axis=0)
    normed_moe = rms_norm(moe_in, ffn_gain)
    rows_dev, top_count = routes.shape
    capacity = 2 * ((rows_dev * top_count + EXPERTS - 1) // EXPERTS)
    capacity = -(-capacity // 8) * 8
    flat_routes = routes.reshape(rows_dev * top_count)
    expert_ids = jnp.arange(EXPERTS, dtype=jnp.int32)
    onehot = (flat_routes[:, None] == expert_ids[None, :]).astype(jnp.int32)
    slot_rank = jnp.sum(jnp.cumsum(onehot, axis=0) * onehot, axis=1) - 1
    slot_index = flat_routes * capacity + slot_rank
    slot_ids = jnp.arange(EXPERTS * capacity, dtype=jnp.int32)
    slot_onehot = (slot_index[:, None] == slot_ids[None, :]).astype(jnp.bfloat16)
    row_onehot = jnp.max(slot_onehot.reshape(rows_dev, top_count, -1), axis=1)
    buffer = jnp.dot(
        row_onehot.T, normed_moe, preferred_element_type=jnp.float32
    ).astype(jnp.bfloat16)
    outgoing = buffer.reshape(seq_count, EXPERTS // seq_count, capacity, model_width)
    hidden = jnp.einsum(
        "secd,edf->secf",
        lax.all_to_all(outgoing, "seq", split_axis=0, concat_axis=0, tiled=True),
        expert_in,
        preferred_element_type=jnp.float32,
    )
    ff_width = expert_out.shape[1]
    active = (jax.nn.silu(hidden[..., :ff_width]) * hidden[..., ff_width:]).astype(jnp.bfloat16)
    results = jnp.einsum(
        "secf,efd->secd", active, expert_out, preferred_element_type=jnp.float32
    ).astype(jnp.bfloat16)
    returned = lax.all_to_all(results, "seq", split_axis=0, concat_axis=0, tiled=True)
    fetched = jnp.dot(
        slot_onehot,
        returned.reshape(EXPERTS * capacity, model_width),
        preferred_element_type=jnp.float32,
    ).reshape(rows_dev, top_count, model_width)
    combined = jnp.sum(fetched * gate_values[..., None], axis=1)
    layer_out = (moe_in.astype(jnp.float32) + combined).astype(jnp.bfloat16)
    return (layer_out[:pre_share], layer_out[pre_share:])


def solution(mesh):
    return jax.shard_map(
        shards,
        mesh=mesh,
        in_specs=(
            P("seq", None),
            P(("seq", "tp"), None),
            P(),
            P(None, "tp"),
            P(None, "tp", None),
            P("tp", None),
            P(None, "seq", "tp", None),
            P(),
            P(),
            P(),
            P("seq", None, None),
            P("seq", None, None),
            P(("seq", "tp"), None),
            P(("seq", "tp"), None),
        ),
        out_specs=(P(("seq", "tp"), None), P(("seq", "tp"), None)),
        check_vma=False,
    )
```

```python
import math

import jax
import jax.numpy as jnp
from jax import lax
from jax.sharding import PartitionSpec as P
from jax.experimental import pallas as pl
from jax.experimental.pallas import tpu as pltpu

EXPERTS = 32
SPAN = 2048


eps_norm = 1e-05
rope_base = 10000.0
masked_score = -1e30
key_block = 512


def rms_norm(values, scales):
    floats = values.astype(jnp.float32)
    factor = lax.rsqrt(jnp.mean(floats * floats, axis=-1, keepdims=True) + eps_norm)
    return (floats * factor * scales.astype(jnp.float32)).astype(jnp.bfloat16)


def apply_rotary(values, token_positions):
    half_dim = values.shape[-1] // 2
    frequency = rope_base ** (-2.0 * jnp.arange(half_dim, dtype=jnp.float32) / values.shape[-1])
    angles = token_positions.astype(jnp.float32)[:, None] * frequency[None, :]
    cosine = jnp.cos(angles)[:, None, :]
    sine_part = jnp.sin(angles)[:, None, :]
    first_half = values[..., :half_dim]
    second_half = values[..., half_dim:]
    return jnp.concatenate(
        [
            first_half * cosine - second_half * sine_part,
            second_half * cosine + first_half * sine_part,
        ],
        axis=-1,
    )


def span_tables(span_tenant):
    span_count = span_tenant.shape[0]
    ordinal = jnp.arange(span_count, dtype=jnp.int32)
    same_tenant = span_tenant[:, None] == span_tenant[None, :]
    earlier = ordinal[None, :] < ordinal[:, None]
    return jnp.sum(jnp.where(same_tenant & earlier, 1, 0), axis=1).astype(jnp.int32)


def token_tables(token_index, span_tenant, before):
    span_count = span_tenant.shape[0]
    span_index = token_index // SPAN
    onehot = span_index[:, None] == jnp.arange(span_count, dtype=jnp.int32)[None, :]
    tenant = jnp.sum(jnp.where(onehot, span_tenant[None, :], 0), axis=1)
    offset = jnp.sum(jnp.where(onehot, before[None, :], 0), axis=1)
    return (tenant, offset * SPAN + token_index % SPAN)


def attend_keys(fold_state, keyvalue_rows, visible, query_matrix, score_scale):
    run_max, run_total, run_acc = fold_state
    head_dim = keyvalue_rows.shape[-1] // 2
    scores = (
        jnp.einsum(
            "qhgd,khd->qhgk",
            query_matrix,
            keyvalue_rows[..., :head_dim],
            preferred_element_type=jnp.float32,
        )
        * score_scale
    )
    mask_full = visible[:, None, None, :]
    scores = jnp.where(mask_full, scores, masked_score)
    new_max = jnp.maximum(run_max, jnp.max(scores, axis=-1))
    weights_exp = jnp.where(mask_full, jnp.exp(scores - new_max[..., None]), 0.0)
    factor = jnp.exp(run_max - new_max)
    new_total = run_total * factor + jnp.sum(weights_exp, axis=-1)
    new_acc = run_acc * factor[..., None] + jnp.einsum(
        "qhgk,khd->qhgd",
        weights_exp.astype(jnp.bfloat16),
        keyvalue_rows[..., head_dim:],
        preferred_element_type=jnp.float32,
    )
    return (new_max, new_total, new_acc)


def flash_kernel(
    flags_ref, q_ref, k_ref, v_ref, row_token_ref, row_tenant_ref, key_tenant_ref,
    o_ref, max_ref, total_ref, acc_ref, *, score_scale, block_len
):
    step = pl.program_id(0)

    @pl.when(step == 0)
    def _():
        max_ref[...] = jnp.full(max_ref.shape, masked_score, jnp.float32)
        total_ref[...] = jnp.zeros(total_ref.shape, jnp.float32)
        acc_ref[...] = jnp.zeros(acc_ref.shape, jnp.float32)

    @pl.when(flags_ref[step] != 0)
    def _():
        scores = (
            lax.dot_general(
                q_ref[...], v_ref[...], (((1,), (1,)), ((), ())),
                preferred_element_type=jnp.float32,
            )
            * score_scale
        )
        key_index = step * block_len + lax.broadcasted_iota(jnp.int32, (1, block_len), 1)
        visible = (row_tenant_ref[...] == key_tenant_ref[...]) & (
            row_token_ref[...] >= key_index
        )
        scores = jnp.where(visible, scores, masked_score)
        run_max = max_ref[...]
        new_max = jnp.maximum(run_max, jnp.max(scores, axis=-1, keepdims=True))
        weights_exp = jnp.where(visible, jnp.exp(scores - new_max), 0.0)
        factor = jnp.exp(run_max - new_max)
        total_ref[...] = total_ref[...] * factor + jnp.sum(weights_exp, axis=-1, keepdims=True)
        acc_ref[...] = acc_ref[...] * factor + jnp.dot(
            weights_exp.astype(jnp.bfloat16), v_ref[...], preferred_element_type=jnp.float32
        )
        max_ref[...] = new_max

    @pl.when(step == pl.num_programs(0) - 1)
    def _():
        o_ref[...] = (acc_ref[...] / total_ref[...]).astype(o_ref.dtype)


def flash_attend(flags, queries, keyvals, head, row_token, row_tenant, key_tenant, score_scale, block_len, interpret=False):
    query_count, head_dim = queries.shape
    key_count = keyvals.shape[0]
    full = lambda step, flags_ref: (0, 0)
    grid_spec = pltpu.PrefetchScalarGridSpec(
        num_scalar_prefetch=1,
        grid=(key_count // block_len,),
        in_specs=[
            pl.BlockSpec((query_count, head_dim), full),
            pl.BlockSpec((block_len, head_dim), lambda step, flags_ref: (step, head)),
            pl.BlockSpec((block_len, head_dim), lambda step, flags_ref: (step, head)),
            pl.BlockSpec((query_count, 1), full),
            pl.BlockSpec((query_count, 1), full),
            pl.BlockSpec((1, block_len), lambda step, flags_ref: (0, step)),
        ],
        out_specs=pl.BlockSpec((query_count, head_dim), full),
        scratch_shapes=[
            pltpu.VMEM((query_count, 1), jnp.float32),
            pltpu.VMEM((query_count, 1), jnp.float32),
            pltpu.VMEM((query_count, head_dim), jnp.float32),
        ],
    )
    body = lambda *refs: flash_kernel(*refs, score_scale=score_scale, block_len=block_len)
    return pl.pallas_call(
        body,
        grid_spec=grid_spec,
        out_shape=jax.ShapeDtypeStruct((query_count, head_dim), jnp.bfloat16),
        interpret=interpret,
    )(flags, queries, keyvals, keyvals, row_token[:, None], row_tenant[:, None], key_tenant[None, :])


def swap_partner(values, axis_name, distance):
    count = lax.axis_size(axis_name)
    pairs = [(i, i ^ distance) for i in range(count)]
    return lax.ppermute(values, axis_name, pairs)


def lane_dense(values):
    flat = values.reshape(-1)
    return flat.reshape(-1, 128) if flat.shape[0] % 128 == 0 else flat.reshape(1, -1)


def gather_blocks(block, axis_name, distances):
    index = lax.axis_index(axis_name)
    shape = block.shape
    block = lane_dense(block)[None]
    stacked = block
    done = []
    for distance in distances:
        theirs = swap_partner(stacked, axis_name, distance)
        upper = (index // distance) % 2 == 1
        low = jnp.where(upper, theirs, stacked)
        high = jnp.where(upper, stacked, theirs)
        place = sum(1 for d in done if d > distance)
        stacked = jnp.stack([low, high], axis=place)
        done.append(distance)
    return stacked.reshape((-1,) + shape[1:])


def scatter_blocks(values, axis_name, distances, combine, send_type=None, dense=False):
    count = lax.axis_size(axis_name)
    index = lax.axis_index(axis_name)
    levels = count.bit_length() - 1
    rows = values.shape[0] // count
    part_shape = (rows,) + values.shape[1:]
    if dense:
        flat = math.prod(part_shape)
        part_shape = (flat // 128, 128) if flat % 128 == 0 else (1, flat)
    stacked = values.reshape((2,) * levels + part_shape)
    remaining = [count >> (j + 1) for j in range(levels)]
    for distance in distances:
        place = remaining.index(distance)
        low = lax.index_in_dim(stacked, 0, place, keepdims=False)
        high = lax.index_in_dim(stacked, 1, place, keepdims=False)
        upper = (index // distance) % 2 == 1
        keep = jnp.where(upper, high, low)
        send = jnp.where(upper, low, high)
        if send_type is not None:
            send = send.astype(send_type)
        received = swap_partner(send, axis_name, distance).astype(keep.dtype)
        stacked = combine(keep, received)
        remaining.pop(place)
    return stacked.reshape((rows,) + values.shape[1:])


def add_parts(first, second):
    return first + second


def merge_softmax(first, second, groups, head_dim):
    width = groups * head_dim
    first_max, second_max = first[..., width + groups:], second[..., width + groups:]
    top = jnp.maximum(first_max, second_max)
    first_scale = jnp.exp(first_max - top)
    second_scale = jnp.exp(second_max - top)
    acc = first[..., :width] * jnp.repeat(first_scale, head_dim, axis=-1) + second[
        ..., :width
    ] * jnp.repeat(second_scale, head_dim, axis=-1)
    total = first[..., width:width + groups] * first_scale + second[..., width:width + groups] * second_scale
    return jnp.concatenate([acc, total, top], axis=-1)

def shards(
    prefill_states,
    decode_states,
    attn_gain,
    query_weight,
    keyvalue_weight,
    output_weight,
    cache_keyval,
    cached_length,
    span_tenant,
    ffn_gain,
    expert_in,
    expert_out,
    routes,
    gate_values,
):
    seq_count = lax.axis_size("seq")
    tp_count = lax.axis_size("tp")
    seq_index = lax.axis_index("seq")
    tp_index = lax.axis_index("tp")
    pre_local, model_width = prefill_states.shape
    dec_local = decode_states.shape[0]
    heads_kv = keyvalue_weight.shape[1]
    head_dim = keyvalue_weight.shape[2] // 2
    heads_q = query_weight.shape[1] // head_dim
    query_group_count = heads_q // heads_kv
    score_scale = head_dim ** (-0.5)
    pre_share = pre_local // tp_count
    normalised_input = rms_norm(prefill_states, attn_gain)
    query_matrix = jnp.dot(
        normalised_input, query_weight, preferred_element_type=jnp.float32
    ).reshape(pre_local, heads_q, head_dim)
    keyvalue_rows = jnp.dot(
        normalised_input,
        keyvalue_weight.reshape(model_width, heads_kv * 2 * head_dim),
        preferred_element_type=jnp.float32,
    ).reshape(pre_local, heads_kv, 2 * head_dim)
    before = span_tables(span_tenant)
    token_index = seq_index * pre_local + jnp.arange(pre_local, dtype=jnp.int32)
    tenant, token_positions = token_tables(token_index, span_tenant, before)
    query_matrix = (
        apply_rotary(query_matrix, token_positions)
        .astype(jnp.bfloat16)
        .reshape(pre_local, heads_kv, query_group_count, head_dim)
    )
    rotated_keys = apply_rotary(keyvalue_rows[..., :head_dim], token_positions).astype(jnp.bfloat16)
    local_keyvals = jnp.concatenate(
        [rotated_keys, keyvalue_rows[..., head_dim:].astype(jnp.bfloat16)], axis=-1
    )
    seq_near_first = [1 << j for j in range(seq_count.bit_length() - 1)]
    key_piece = lax.all_gather(
        local_keyvals.reshape(pre_local, heads_kv * 2 * head_dim), "seq", axis=0, tiled=True
    ).reshape(-1, heads_kv, 2 * head_dim)
    piece_rows = key_piece.shape[0]
    block_len = math.gcd(piece_rows, key_block)
    blocks = key_piece.reshape(piece_rows // block_len, block_len, heads_kv, 2 * head_dim)
    query_count = pre_local * query_group_count
    query_rows = query_matrix.transpose(1, 0, 2, 3).reshape(heads_kv, query_count, head_dim)
    row_token = jnp.repeat(token_index, query_group_count)
    row_tenant = jnp.repeat(tenant, query_group_count)
    key_positions = jnp.arange(piece_rows, dtype=jnp.int32)
    key_tenant = token_tables(key_positions, span_tenant, before)[0]
    token_visible = (tenant[:, None] == key_tenant[None, :]) & (
        token_index[:, None] >= key_positions[None, :]
    )
    block_flags = jnp.any(
        token_visible.reshape(pre_local, piece_rows // block_len, block_len), axis=(0, 2)
    ).astype(jnp.int32)
    padded_queries = jnp.pad(query_rows, ((0, 0), (0, 0), (0, head_dim)))
    flat_keyvals = key_piece.reshape(piece_rows, heads_kv * 2 * head_dim)
    head_outputs = [
        flash_attend(
            block_flags,
            padded_queries[head],
            flat_keyvals,
            head,
            row_token,
            row_tenant,
            key_tenant,
            score_scale,
            block_len,
        )[:, head_dim:]
        for head in range(heads_kv)
    ]
    attended = (
        jnp.stack(head_outputs)
        .reshape(heads_kv, pre_local, query_group_count, head_dim)
        .transpose(1, 0, 2, 3)
        .reshape(pre_local, heads_q * head_dim)
    )
    prefill_part = jnp.dot(attended, output_weight, preferred_element_type=jnp.float32)
    tp_near_first = [1 << j for j in range(tp_count.bit_length() - 1)]
    prefill_sum = scatter_blocks(
        prefill_part, "tp", tp_near_first, add_parts, send_type=jnp.bfloat16, dense=True
    )
    group_states = gather_blocks(decode_states, "tp", tp_near_first[::-1])
    group_rows = group_states.shape[0]
    group_lengths = lax.dynamic_slice_in_dim(cached_length, seq_index * group_rows, group_rows, 0)
    decode_normalised = rms_norm(group_states, attn_gain)
    group_queries = jnp.dot(
        decode_normalised, query_weight, preferred_element_type=jnp.float32
    ).reshape(group_rows, heads_q, head_dim)
    group_queries = (
        apply_rotary(group_queries, group_lengths)
        .astype(jnp.bfloat16)
        .reshape(group_rows, heads_kv, query_group_count, head_dim)
    )
    decode_keyvalues = jnp.dot(
        decode_normalised,
        keyvalue_weight.reshape(model_width, heads_kv * 2 * head_dim),
        preferred_element_type=jnp.float32,
    ).reshape(group_rows, heads_kv, 2 * head_dim)
    new_keys = apply_rotary(decode_keyvalues[..., :head_dim], group_lengths).astype(jnp.bfloat16)
    new_vals = decode_keyvalues[..., head_dim:].astype(jnp.bfloat16)
    decode_queries = gather_blocks(group_queries, "seq", seq_near_first[::-1])
    cache_local = cache_keyval.shape[1]
    cache_pos = seq_index * cache_local + jnp.arange(cache_local, dtype=jnp.int32)
    visible = (cache_pos[None, :] < cached_length[:, None])[:, None, None, :]
    padded_decode = jnp.pad(decode_queries, ((0, 0), (0, 0), (0, 0), (0, head_dim)))
    scores = (
        jnp.einsum(
            "bhgd,bkhd->bhgk",
            padded_decode,
            cache_keyval,
            preferred_element_type=jnp.float32,
        )
        * score_scale
    )
    scores = jnp.where(visible, scores, masked_score)
    local_max = jnp.max(scores, axis=-1)
    weights_exp = jnp.where(visible, jnp.exp(scores - local_max[..., None]), 0.0)
    local_total = jnp.sum(weights_exp, axis=-1)
    local_acc = jnp.einsum(
        "bhgk,bkhd->bhgd",
        weights_exp.astype(jnp.bfloat16),
        cache_keyval,
        preferred_element_type=jnp.float32,
    )[..., head_dim:]
    dec_total = local_acc.shape[0]
    groups = heads_kv * query_group_count
    packed = jnp.concatenate(
        [
            local_acc.reshape(dec_total, groups * head_dim),
            local_total.reshape(dec_total, groups),
            local_max.reshape(dec_total, groups),
        ],
        axis=-1,
    )
    merged = scatter_blocks(
        packed, "seq", seq_near_first, lambda a, b: merge_softmax(a, b, groups, head_dim)
    )
    merged_acc = merged[:, : groups * head_dim].reshape(group_rows, heads_kv, query_group_count, head_dim)
    merged_total = merged[:, groups * head_dim : groups * (head_dim + 1)].reshape(
        group_rows, heads_kv, query_group_count
    )
    merged_max = merged[:, groups * (head_dim + 1) :].reshape(group_rows, heads_kv, query_group_count)
    own_score = (
        jnp.sum(
            group_queries.astype(jnp.float32) * new_keys.astype(jnp.float32)[:, :, None, :],
            axis=-1,
        )
        * score_scale
    )
    final_max = jnp.maximum(merged_max, own_score)
    rescale = jnp.exp(merged_max - final_max)
    own_exp = jnp.exp(own_score - final_max)
    final_total = merged_total * rescale + own_exp
    own_rounded = lax.optimization_barrier(own_exp.astype(jnp.bfloat16)).astype(jnp.float32)
    final_acc = (
        merged_acc * rescale[..., None]
        + own_rounded[..., None] * new_vals.astype(jnp.float32)[:, :, None, :]
    )
    decode_attended = (
        (final_acc / final_total[..., None])
        .astype(jnp.bfloat16)
        .reshape(group_rows, heads_q * head_dim)
    )
    decode_part = jnp.dot(decode_attended, output_weight, preferred_element_type=jnp.float32)
    decode_sum = scatter_blocks(decode_part, "tp", tp_near_first, add_parts, dense=True)
    own_states = lax.dynamic_slice_in_dim(prefill_states, tp_index * pre_share, pre_share, 0)
    prefill_h = (own_states.astype(jnp.float32) + prefill_sum).astype(jnp.bfloat16)
    decode_h = (decode_states.astype(jnp.float32) + decode_sum).astype(jnp.bfloat16)
    moe_in = jnp.concatenate([prefill_h, decode_h], axis=0)
    normed_moe = rms_norm(moe_in, ffn_gain)
    rows_dev, top_count = routes.shape
    capacity = 2 * ((rows_dev * top_count + EXPERTS - 1) // EXPERTS)
    capacity = -(-capacity // 8) * 8
    flat_routes = routes.reshape(rows_dev * top_count)
    expert_ids = jnp.arange(EXPERTS, dtype=jnp.int32)
    onehot = (flat_routes[:, None] == expert_ids[None, :]).astype(jnp.int32)
    slot_rank = jnp.sum(jnp.cumsum(onehot, axis=0) * onehot, axis=1) - 1
    slot_index = flat_routes * capacity + slot_rank
    repeated = jnp.repeat(normed_moe, top_count, axis=0)
    buffer = jnp.zeros((EXPERTS * capacity, model_width), jnp.bfloat16).at[slot_index].set(repeated)
    outgoing = buffer.reshape(seq_count, EXPERTS // seq_count, capacity, model_width)
    hidden = jnp.einsum(
        "secd,edf->secf",
        lax.all_to_all(outgoing, "seq", split_axis=0, concat_axis=0, tiled=True),
        expert_in,
        preferred_element_type=jnp.float32,
    )
    ff_width = expert_out.shape[1]
    active = (jax.nn.silu(hidden[..., :ff_width]) * hidden[..., ff_width:]).astype(jnp.bfloat16)
    results = jnp.einsum(
        "secf,efd->secd", active, expert_out, preferred_element_type=jnp.float32
    ).astype(jnp.bfloat16)
    returned = lax.all_to_all(results, "seq", split_axis=0, concat_axis=0, tiled=True)
    fetched = (
        returned.reshape(EXPERTS * capacity, model_width)[slot_index]
        .astype(jnp.float32)
        .reshape(rows_dev, top_count, model_width)
    )
    combined = jnp.sum(fetched * gate_values[..., None], axis=1)
    layer_out = (moe_in.astype(jnp.float32) + combined).astype(jnp.bfloat16)
    return (layer_out[:pre_share], layer_out[pre_share:])


def solution(mesh):
    return jax.shard_map(
        shards,
        mesh=mesh,
        in_specs=(
            P("seq", None),
            P(("seq", "tp"), None),
            P(),
            P(None, "tp"),
            P(None, "tp", None),
            P("tp", None),
            P(None, "seq", "tp", None),
            P(),
            P(),
            P(),
            P("seq", None, None),
            P("seq", None, None),
            P(("seq", "tp"), None),
            P(("seq", "tp"), None),
        ),
        out_specs=(P(("seq", "tp"), None), P(("seq", "tp"), None)),
        check_vma=False,
    )
```

```python
import math

import jax
import jax.numpy as jnp
from jax import lax
from jax.sharding import PartitionSpec as P
from jax.experimental import pallas as pl
from jax.experimental.pallas import tpu as pltpu

EXPERTS = 32
SPAN = 2048


eps_norm = 1e-05
rope_base = 10000.0
masked_score = -1e30
key_block = 512


def rms_norm(values, scales):
    floats = values.astype(jnp.float32)
    factor = lax.rsqrt(jnp.mean(floats * floats, axis=-1, keepdims=True) + eps_norm)
    return (floats * factor * scales.astype(jnp.float32)).astype(jnp.bfloat16)


def apply_rotary(values, token_positions):
    half_dim = values.shape[-1] // 2
    frequency = rope_base ** (-2.0 * jnp.arange(half_dim, dtype=jnp.float32) / values.shape[-1])
    angles = token_positions.astype(jnp.float32)[:, None] * frequency[None, :]
    cosine = jnp.cos(angles)[:, None, :]
    sine_part = jnp.sin(angles)[:, None, :]
    first_half = values[..., :half_dim]
    second_half = values[..., half_dim:]
    return jnp.concatenate(
        [
            first_half * cosine - second_half * sine_part,
            second_half * cosine + first_half * sine_part,
        ],
        axis=-1,
    )


def span_tables(span_tenant):
    span_count = span_tenant.shape[0]
    ordinal = jnp.arange(span_count, dtype=jnp.int32)
    same_tenant = span_tenant[:, None] == span_tenant[None, :]
    earlier = ordinal[None, :] < ordinal[:, None]
    return jnp.sum(jnp.where(same_tenant & earlier, 1, 0), axis=1).astype(jnp.int32)


def token_tables(token_index, span_tenant, before):
    span_count = span_tenant.shape[0]
    span_index = token_index // SPAN
    onehot = span_index[:, None] == jnp.arange(span_count, dtype=jnp.int32)[None, :]
    tenant = jnp.sum(jnp.where(onehot, span_tenant[None, :], 0), axis=1)
    offset = jnp.sum(jnp.where(onehot, before[None, :], 0), axis=1)
    return (tenant, offset * SPAN + token_index % SPAN)


def attend_keys(fold_state, keyvalue_rows, visible, query_matrix, score_scale):
    run_max, run_total, run_acc = fold_state
    head_dim = keyvalue_rows.shape[-1] // 2
    scores = (
        jnp.einsum(
            "qhgd,khd->qhgk",
            query_matrix,
            keyvalue_rows[..., :head_dim],
            preferred_element_type=jnp.float32,
        )
        * score_scale
    )
    mask_full = visible[:, None, None, :]
    scores = jnp.where(mask_full, scores, masked_score)
    new_max = jnp.maximum(run_max, jnp.max(scores, axis=-1))
    weights_exp = jnp.where(mask_full, jnp.exp(scores - new_max[..., None]), 0.0)
    factor = jnp.exp(run_max - new_max)
    new_total = run_total * factor + jnp.sum(weights_exp, axis=-1)
    new_acc = run_acc * factor[..., None] + jnp.einsum(
        "qhgk,khd->qhgd",
        weights_exp.astype(jnp.bfloat16),
        keyvalue_rows[..., head_dim:],
        preferred_element_type=jnp.float32,
    )
    return (new_max, new_total, new_acc)


def flash_kernel(
    flags_ref, q_ref, kv_ref, row_token_ref, row_tenant_ref, key_tenant_ref,
    o_ref, max_ref, total_ref, acc_ref, *, score_scale, block_len
):
    step = pl.program_id(0)

    @pl.when(step == 0)
    def _():
        max_ref[...] = jnp.full(max_ref.shape, masked_score, jnp.float32)
        total_ref[...] = jnp.zeros(total_ref.shape, jnp.float32)
        acc_ref[...] = jnp.zeros(acc_ref.shape, jnp.float32)

    @pl.when(flags_ref[step] != 0)
    def _():
        scores = (
            lax.dot_general(
                q_ref[...], kv_ref[...], (((1,), (1,)), ((), ())),
                preferred_element_type=jnp.float32,
            )
            * score_scale
        )
        key_index = step * block_len + lax.broadcasted_iota(jnp.int32, (1, block_len), 1)
        visible = (row_tenant_ref[...] == key_tenant_ref[...]) & (
            row_token_ref[...] >= key_index
        )
        scores = jnp.where(visible, scores, masked_score)
        run_max = max_ref[...]
        new_max = jnp.maximum(run_max, jnp.max(scores, axis=-1, keepdims=True))
        weights_exp = jnp.where(visible, jnp.exp(scores - new_max), 0.0)
        factor = jnp.exp(run_max - new_max)
        total_ref[...] = total_ref[...] * factor + jnp.sum(weights_exp, axis=-1, keepdims=True)
        acc_ref[...] = acc_ref[...] * factor + jnp.dot(
            weights_exp.astype(jnp.bfloat16), kv_ref[...], preferred_element_type=jnp.float32
        )
        max_ref[...] = new_max

    @pl.when(step == pl.num_programs(0) - 1)
    def _():
        o_ref[...] = (acc_ref[...] / total_ref[...]).astype(o_ref.dtype)


def flash_attend(flags, queries, keyvals, head, row_token, row_tenant, key_tenant, score_scale, block_len, interpret=False):
    query_count, head_dim = queries.shape
    key_count = keyvals.shape[0]
    full = lambda step, flags_ref: (0, 0)
    grid_spec = pltpu.PrefetchScalarGridSpec(
        num_scalar_prefetch=1,
        grid=(key_count // block_len,),
        in_specs=[
            pl.BlockSpec((query_count, head_dim), full),
            pl.BlockSpec((block_len, head_dim), lambda step, flags_ref: (step, head)),
            pl.BlockSpec((query_count, 1), full),
            pl.BlockSpec((query_count, 1), full),
            pl.BlockSpec((1, block_len), lambda step, flags_ref: (0, step)),
        ],
        out_specs=pl.BlockSpec((query_count, head_dim), full),
        scratch_shapes=[
            pltpu.VMEM((query_count, 1), jnp.float32),
            pltpu.VMEM((query_count, 1), jnp.float32),
            pltpu.VMEM((query_count, head_dim), jnp.float32),
        ],
    )
    body = lambda *refs: flash_kernel(*refs, score_scale=score_scale, block_len=block_len)
    return pl.pallas_call(
        body,
        grid_spec=grid_spec,
        out_shape=jax.ShapeDtypeStruct((query_count, head_dim), jnp.bfloat16),
        interpret=interpret,
    )(flags, queries, keyvals, row_token[:, None], row_tenant[:, None], key_tenant[None, :])


def swap_partner(values, axis_name, distance):
    count = lax.axis_size(axis_name)
    pairs = [(i, i ^ distance) for i in range(count)]
    return lax.ppermute(values, axis_name, pairs)


def lane_dense(values):
    flat = values.reshape(-1)
    return flat.reshape(-1, 128) if flat.shape[0] % 128 == 0 else flat.reshape(1, -1)


def gather_blocks(block, axis_name, distances):
    index = lax.axis_index(axis_name)
    shape = block.shape
    block = lane_dense(block)[None]
    stacked = block
    done = []
    for distance in distances:
        theirs = swap_partner(stacked, axis_name, distance)
        upper = (index // distance) % 2 == 1
        low = jnp.where(upper, theirs, stacked)
        high = jnp.where(upper, stacked, theirs)
        place = sum(1 for d in done if d > distance)
        stacked = jnp.stack([low, high], axis=place)
        done.append(distance)
    return stacked.reshape((-1,) + shape[1:])


def scatter_blocks(values, axis_name, distances, combine, send_type=None, dense=False):
    count = lax.axis_size(axis_name)
    index = lax.axis_index(axis_name)
    levels = count.bit_length() - 1
    rows = values.shape[0] // count
    part_shape = (rows,) + values.shape[1:]
    if dense:
        flat = math.prod(part_shape)
        part_shape = (flat // 128, 128) if flat % 128 == 0 else (1, flat)
    stacked = values.reshape((2,) * levels + part_shape)
    remaining = [count >> (j + 1) for j in range(levels)]
    for distance in distances:
        place = remaining.index(distance)
        low = lax.index_in_dim(stacked, 0, place, keepdims=False)
        high = lax.index_in_dim(stacked, 1, place, keepdims=False)
        upper = (index // distance) % 2 == 1
        keep = jnp.where(upper, high, low)
        send = jnp.where(upper, low, high)
        if send_type is not None:
            send = send.astype(send_type)
        received = swap_partner(send, axis_name, distance).astype(keep.dtype)
        stacked = combine(keep, received)
        remaining.pop(place)
    return stacked.reshape((rows,) + values.shape[1:])


def add_parts(first, second):
    return first + second


def merge_softmax(first, second, groups, head_dim):
    width = groups * head_dim
    first_max, second_max = first[..., width + groups:], second[..., width + groups:]
    top = jnp.maximum(first_max, second_max)
    first_scale = jnp.exp(first_max - top)
    second_scale = jnp.exp(second_max - top)
    acc = first[..., :width] * jnp.repeat(first_scale, head_dim, axis=-1) + second[
        ..., :width
    ] * jnp.repeat(second_scale, head_dim, axis=-1)
    total = first[..., width:width + groups] * first_scale + second[..., width:width + groups] * second_scale
    return jnp.concatenate([acc, total, top], axis=-1)

def shards(
    prefill_states,
    decode_states,
    attn_gain,
    query_weight,
    keyvalue_weight,
    output_weight,
    cache_keyval,
    cached_length,
    span_tenant,
    ffn_gain,
    expert_in,
    expert_out,
    routes,
    gate_values,
):
    seq_count = lax.axis_size("seq")
    tp_count = lax.axis_size("tp")
    seq_index = lax.axis_index("seq")
    tp_index = lax.axis_index("tp")
    pre_local, model_width = prefill_states.shape
    dec_local = decode_states.shape[0]
    heads_kv = keyvalue_weight.shape[1]
    head_dim = keyvalue_weight.shape[2] // 2
    heads_q = query_weight.shape[1] // head_dim
    query_group_count = heads_q // heads_kv
    score_scale = head_dim ** (-0.5)
    pre_share = pre_local // tp_count
    normalised_input = rms_norm(prefill_states, attn_gain)
    query_matrix = jnp.dot(
        normalised_input, query_weight, preferred_element_type=jnp.float32
    ).reshape(pre_local, heads_q, head_dim)
    keyvalue_rows = jnp.dot(
        normalised_input,
        keyvalue_weight.reshape(model_width, heads_kv * 2 * head_dim),
        preferred_element_type=jnp.float32,
    ).reshape(pre_local, heads_kv, 2 * head_dim)
    before = span_tables(span_tenant)
    token_index = seq_index * pre_local + jnp.arange(pre_local, dtype=jnp.int32)
    tenant, token_positions = token_tables(token_index, span_tenant, before)
    query_matrix = (
        apply_rotary(query_matrix, token_positions)
        .astype(jnp.bfloat16)
        .reshape(pre_local, heads_kv, query_group_count, head_dim)
    )
    rotated_keys = apply_rotary(keyvalue_rows[..., :head_dim], token_positions).astype(jnp.bfloat16)
    local_keyvals = jnp.concatenate(
        [rotated_keys, keyvalue_rows[..., head_dim:].astype(jnp.bfloat16)], axis=-1
    )
    seq_near_first = [1 << j for j in range(seq_count.bit_length() - 1)]
    key_piece = lax.all_gather(
        local_keyvals.reshape(pre_local, heads_kv * 2 * head_dim), "seq", axis=0, tiled=True
    ).reshape(-1, heads_kv, 2 * head_dim)
    piece_rows = key_piece.shape[0]
    block_len = math.gcd(piece_rows, key_block)
    blocks = key_piece.reshape(piece_rows // block_len, block_len, heads_kv, 2 * head_dim)
    query_count = pre_local * query_group_count
    query_rows = query_matrix.transpose(1, 0, 2, 3).reshape(heads_kv, query_count, head_dim)
    row_token = jnp.repeat(token_index, query_group_count)
    row_tenant = jnp.repeat(tenant, query_group_count)
    key_positions = jnp.arange(piece_rows, dtype=jnp.int32)
    key_tenant = token_tables(key_positions, span_tenant, before)[0]
    token_visible = (tenant[:, None] == key_tenant[None, :]) & (
        token_index[:, None] >= key_positions[None, :]
    )
    block_flags = jnp.any(
        token_visible.reshape(pre_local, piece_rows // block_len, block_len), axis=(0, 2)
    ).astype(jnp.int32)
    padded_queries = jnp.pad(query_rows, ((0, 0), (0, 0), (0, head_dim)))
    flat_keyvals = key_piece.reshape(piece_rows, heads_kv * 2 * head_dim)
    head_outputs = [
        flash_attend(
            block_flags,
            padded_queries[head],
            flat_keyvals,
            head,
            row_token,
            row_tenant,
            key_tenant,
            score_scale,
            block_len,
        )[:, head_dim:]
        for head in range(heads_kv)
    ]
    attended = (
        jnp.stack(head_outputs)
        .reshape(heads_kv, pre_local, query_group_count, head_dim)
        .transpose(1, 0, 2, 3)
        .reshape(pre_local, heads_q * head_dim)
    )
    prefill_part = jnp.dot(attended, output_weight, preferred_element_type=jnp.float32)
    tp_near_first = [1 << j for j in range(tp_count.bit_length() - 1)]
    prefill_sum = scatter_blocks(
        prefill_part, "tp", tp_near_first, add_parts, send_type=jnp.bfloat16, dense=True
    )
    group_states = gather_blocks(decode_states, "tp", tp_near_first[::-1])
    group_rows = group_states.shape[0]
    group_lengths = lax.dynamic_slice_in_dim(cached_length, seq_index * group_rows, group_rows, 0)
    decode_normalised = rms_norm(group_states, attn_gain)
    group_queries = jnp.dot(
        decode_normalised, query_weight, preferred_element_type=jnp.float32
    ).reshape(group_rows, heads_q, head_dim)
    group_queries = (
        apply_rotary(group_queries, group_lengths)
        .astype(jnp.bfloat16)
        .reshape(group_rows, heads_kv, query_group_count, head_dim)
    )
    decode_keyvalues = jnp.dot(
        decode_normalised,
        keyvalue_weight.reshape(model_width, heads_kv * 2 * head_dim),
        preferred_element_type=jnp.float32,
    ).reshape(group_rows, heads_kv, 2 * head_dim)
    new_keys = apply_rotary(decode_keyvalues[..., :head_dim], group_lengths).astype(jnp.bfloat16)
    new_vals = decode_keyvalues[..., head_dim:].astype(jnp.bfloat16)
    decode_queries = gather_blocks(group_queries, "seq", seq_near_first[::-1])
    cache_local = cache_keyval.shape[1]
    cache_pos = seq_index * cache_local + jnp.arange(cache_local, dtype=jnp.int32)
    visible = (cache_pos[None, :] < cached_length[:, None])[:, None, None, :]
    padded_decode = jnp.pad(decode_queries, ((0, 0), (0, 0), (0, 0), (0, head_dim)))
    scores = (
        jnp.einsum(
            "bhgd,bkhd->bhgk",
            padded_decode,
            cache_keyval,
            preferred_element_type=jnp.float32,
        )
        * score_scale
    )
    scores = jnp.where(visible, scores, masked_score)
    local_max = jnp.max(scores, axis=-1)
    weights_exp = jnp.where(visible, jnp.exp(scores - local_max[..., None]), 0.0)
    local_total = jnp.sum(weights_exp, axis=-1)
    local_acc = jnp.einsum(
        "bhgk,bkhd->bhgd",
        weights_exp.astype(jnp.bfloat16),
        cache_keyval,
        preferred_element_type=jnp.float32,
    )[..., head_dim:]
    dec_total = local_acc.shape[0]
    groups = heads_kv * query_group_count
    packed = jnp.concatenate(
        [
            local_acc.reshape(dec_total, groups * head_dim),
            local_total.reshape(dec_total, groups),
            local_max.reshape(dec_total, groups),
        ],
        axis=-1,
    )
    merged = scatter_blocks(
        packed, "seq", seq_near_first, lambda a, b: merge_softmax(a, b, groups, head_dim)
    )
    merged_acc = merged[:, : groups * head_dim].reshape(group_rows, heads_kv, query_group_count, head_dim)
    merged_total = merged[:, groups * head_dim : groups * (head_dim + 1)].reshape(
        group_rows, heads_kv, query_group_count
    )
    merged_max = merged[:, groups * (head_dim + 1) :].reshape(group_rows, heads_kv, query_group_count)
    own_score = (
        jnp.sum(
            group_queries.astype(jnp.float32) * new_keys.astype(jnp.float32)[:, :, None, :],
            axis=-1,
        )
        * score_scale
    )
    final_max = jnp.maximum(merged_max, own_score)
    rescale = jnp.exp(merged_max - final_max)
    own_exp = jnp.exp(own_score - final_max)
    final_total = merged_total * rescale + own_exp
    own_rounded = lax.optimization_barrier(own_exp.astype(jnp.bfloat16)).astype(jnp.float32)
    final_acc = (
        merged_acc * rescale[..., None]
        + own_rounded[..., None] * new_vals.astype(jnp.float32)[:, :, None, :]
    )
    decode_attended = (
        (final_acc / final_total[..., None])
        .astype(jnp.bfloat16)
        .reshape(group_rows, heads_q * head_dim)
    )
    decode_part = jnp.dot(decode_attended, output_weight, preferred_element_type=jnp.float32)
    decode_sum = scatter_blocks(decode_part, "tp", tp_near_first, add_parts, dense=True)
    own_states = lax.dynamic_slice_in_dim(prefill_states, tp_index * pre_share, pre_share, 0)
    prefill_h = (own_states.astype(jnp.float32) + prefill_sum).astype(jnp.bfloat16)
    decode_h = (decode_states.astype(jnp.float32) + decode_sum).astype(jnp.bfloat16)
    moe_in = jnp.concatenate([prefill_h, decode_h], axis=0)
    normed_moe = rms_norm(moe_in, ffn_gain)
    rows_dev, top_count = routes.shape
    capacity = 2 * ((rows_dev * top_count + EXPERTS - 1) // EXPERTS)
    capacity = -(-capacity // 8) * 8
    flat_routes = routes.reshape(rows_dev * top_count)
    expert_ids = jnp.arange(EXPERTS, dtype=jnp.int32)
    onehot = (flat_routes[:, None] == expert_ids[None, :]).astype(jnp.int32)
    slot_rank = jnp.sum(jnp.cumsum(onehot, axis=0) * onehot, axis=1) - 1
    slot_index = flat_routes * capacity + slot_rank
    repeated = jnp.repeat(normed_moe, top_count, axis=0)
    buffer = jnp.zeros((EXPERTS * capacity, model_width), jnp.bfloat16).at[slot_index].set(repeated)
    outgoing = buffer.reshape(seq_count, EXPERTS // seq_count, capacity, model_width)
    hidden = jnp.einsum(
        "secd,edf->secf",
        lax.all_to_all(outgoing, "seq", split_axis=0, concat_axis=0, tiled=True),
        expert_in,
        preferred_element_type=jnp.float32,
    )
    ff_width = expert_out.shape[1]
    active = (jax.nn.silu(hidden[..., :ff_width]) * hidden[..., ff_width:]).astype(jnp.bfloat16)
    results = jnp.einsum(
        "secf,efd->secd", active, expert_out, preferred_element_type=jnp.float32
    ).astype(jnp.bfloat16)
    returned = lax.all_to_all(results, "seq", split_axis=0, concat_axis=0, tiled=True)
    fetched = (
        returned.reshape(EXPERTS * capacity, model_width)[slot_index]
        .astype(jnp.float32)
        .reshape(rows_dev, top_count, model_width)
    )
    combined = jnp.sum(fetched * gate_values[..., None], axis=1)
    layer_out = (moe_in.astype(jnp.float32) + combined).astype(jnp.bfloat16)
    return (layer_out[:pre_share], layer_out[pre_share:])


def solution(mesh):
    return jax.shard_map(
        shards,
        mesh=mesh,
        in_specs=(
            P("seq", None),
            P(("seq", "tp"), None),
            P(),
            P(None, "tp"),
            P(None, "tp", None),
            P("tp", None),
            P(None, "seq", "tp", None),
            P(),
            P(),
            P(),
            P("seq", None, None),
            P("seq", None, None),
            P(("seq", "tp"), None),
            P(("seq", "tp"), None),
        ),
        out_specs=(P(("seq", "tp"), None), P(("seq", "tp"), None)),
        check_vma=False,
    )
```

```python
import math

import jax
import jax.numpy as jnp
from jax import lax
from jax.sharding import PartitionSpec as P
from jax.experimental import pallas as pl
from jax.experimental.pallas import tpu as pltpu

EXPERTS = 32
SPAN = 2048


eps_norm = 1e-05
rope_base = 10000.0
masked_score = -1e30
key_block = 1024


def rms_norm(values, scales):
    floats = values.astype(jnp.float32)
    factor = lax.rsqrt(jnp.mean(floats * floats, axis=-1, keepdims=True) + eps_norm)
    return (floats * factor * scales.astype(jnp.float32)).astype(jnp.bfloat16)


def apply_rotary(values, token_positions):
    half_dim = values.shape[-1] // 2
    frequency = rope_base ** (-2.0 * jnp.arange(half_dim, dtype=jnp.float32) / values.shape[-1])
    angles = token_positions.astype(jnp.float32)[:, None] * frequency[None, :]
    cosine = jnp.cos(angles)[:, None, :]
    sine_part = jnp.sin(angles)[:, None, :]
    first_half = values[..., :half_dim]
    second_half = values[..., half_dim:]
    return jnp.concatenate(
        [
            first_half * cosine - second_half * sine_part,
            second_half * cosine + first_half * sine_part,
        ],
        axis=-1,
    )


def span_tables(span_tenant):
    span_count = span_tenant.shape[0]
    ordinal = jnp.arange(span_count, dtype=jnp.int32)
    same_tenant = span_tenant[:, None] == span_tenant[None, :]
    earlier = ordinal[None, :] < ordinal[:, None]
    return jnp.sum(jnp.where(same_tenant & earlier, 1, 0), axis=1).astype(jnp.int32)


def token_tables(token_index, span_tenant, before):
    span_count = span_tenant.shape[0]
    span_index = token_index // SPAN
    onehot = span_index[:, None] == jnp.arange(span_count, dtype=jnp.int32)[None, :]
    tenant = jnp.sum(jnp.where(onehot, span_tenant[None, :], 0), axis=1)
    offset = jnp.sum(jnp.where(onehot, before[None, :], 0), axis=1)
    return (tenant, offset * SPAN + token_index % SPAN)


def attend_keys(fold_state, keyvalue_rows, visible, query_matrix, score_scale):
    run_max, run_total, run_acc = fold_state
    head_dim = keyvalue_rows.shape[-1] // 2
    scores = (
        jnp.einsum(
            "qhgd,khd->qhgk",
            query_matrix,
            keyvalue_rows[..., :head_dim],
            preferred_element_type=jnp.float32,
        )
        * score_scale
    )
    mask_full = visible[:, None, None, :]
    scores = jnp.where(mask_full, scores, masked_score)
    new_max = jnp.maximum(run_max, jnp.max(scores, axis=-1))
    weights_exp = jnp.where(mask_full, jnp.exp(scores - new_max[..., None]), 0.0)
    factor = jnp.exp(run_max - new_max)
    new_total = run_total * factor + jnp.sum(weights_exp, axis=-1)
    new_acc = run_acc * factor[..., None] + jnp.einsum(
        "qhgk,khd->qhgd",
        weights_exp.astype(jnp.bfloat16),
        keyvalue_rows[..., head_dim:],
        preferred_element_type=jnp.float32,
    )
    return (new_max, new_total, new_acc)


def flash_kernel(
    flags_ref, q_ref, k_ref, v_ref, row_token_ref, row_tenant_ref, key_tenant_ref,
    o_ref, max_ref, total_ref, acc_ref, *, score_scale, block_len
):
    step = pl.program_id(0)

    @pl.when(step == 0)
    def _():
        max_ref[...] = jnp.full(max_ref.shape, masked_score, jnp.float32)
        total_ref[...] = jnp.zeros(total_ref.shape, jnp.float32)
        acc_ref[...] = jnp.zeros(acc_ref.shape, jnp.float32)

    @pl.when(flags_ref[step] != 0)
    def _():
        scores = (
            lax.dot_general(
                q_ref[...], v_ref[...], (((1,), (1,)), ((), ())),
                preferred_element_type=jnp.float32,
            )
            * score_scale
        )
        key_index = step * block_len + lax.broadcasted_iota(jnp.int32, (1, block_len), 1)
        visible = (row_tenant_ref[...] == key_tenant_ref[...]) & (
            row_token_ref[...] >= key_index
        )
        scores = jnp.where(visible, scores, masked_score)
        run_max = max_ref[...]
        new_max = jnp.maximum(run_max, jnp.max(scores, axis=-1, keepdims=True))
        weights_exp = jnp.where(visible, jnp.exp(scores - new_max), 0.0)
        factor = jnp.exp(run_max - new_max)
        total_ref[...] = total_ref[...] * factor + jnp.sum(weights_exp, axis=-1, keepdims=True)
        acc_ref[...] = acc_ref[...] * factor + jnp.dot(
            weights_exp.astype(jnp.bfloat16), v_ref[...], preferred_element_type=jnp.float32
        )
        max_ref[...] = new_max

    @pl.when(step == pl.num_programs(0) - 1)
    def _():
        o_ref[...] = (acc_ref[...] / total_ref[...]).astype(o_ref.dtype)


def flash_attend(flags, queries, keyvals, head, row_token, row_tenant, key_tenant, score_scale, block_len, interpret=False):
    query_count, head_dim = queries.shape
    key_count = keyvals.shape[0]
    full = lambda step, flags_ref: (0, 0)
    grid_spec = pltpu.PrefetchScalarGridSpec(
        num_scalar_prefetch=1,
        grid=(key_count // block_len,),
        in_specs=[
            pl.BlockSpec((query_count, head_dim), full),
            pl.BlockSpec((block_len, head_dim), lambda step, flags_ref: (step, head)),
            pl.BlockSpec((block_len, head_dim), lambda step, flags_ref: (step, head)),
            pl.BlockSpec((query_count, 1), full),
            pl.BlockSpec((query_count, 1), full),
            pl.BlockSpec((1, block_len), lambda step, flags_ref: (0, step)),
        ],
        out_specs=pl.BlockSpec((query_count, head_dim), full),
        scratch_shapes=[
            pltpu.VMEM((query_count, 1), jnp.float32),
            pltpu.VMEM((query_count, 1), jnp.float32),
            pltpu.VMEM((query_count, head_dim), jnp.float32),
        ],
    )
    body = lambda *refs: flash_kernel(*refs, score_scale=score_scale, block_len=block_len)
    return pl.pallas_call(
        body,
        grid_spec=grid_spec,
        out_shape=jax.ShapeDtypeStruct((query_count, head_dim), jnp.bfloat16),
        interpret=interpret,
    )(flags, queries, keyvals, keyvals, row_token[:, None], row_tenant[:, None], key_tenant[None, :])


def swap_partner(values, axis_name, distance):
    count = lax.axis_size(axis_name)
    pairs = [(i, i ^ distance) for i in range(count)]
    return lax.ppermute(values, axis_name, pairs)


def lane_dense(values):
    flat = values.reshape(-1)
    return flat.reshape(-1, 128) if flat.shape[0] % 128 == 0 else flat.reshape(1, -1)


def gather_blocks(block, axis_name, distances):
    index = lax.axis_index(axis_name)
    shape = block.shape
    block = lane_dense(block)[None]
    stacked = block
    done = []
    for distance in distances:
        theirs = swap_partner(stacked, axis_name, distance)
        upper = (index // distance) % 2 == 1
        low = jnp.where(upper, theirs, stacked)
        high = jnp.where(upper, stacked, theirs)
        place = sum(1 for d in done if d > distance)
        stacked = jnp.stack([low, high], axis=place)
        done.append(distance)
    return stacked.reshape((-1,) + shape[1:])


def scatter_blocks(values, axis_name, distances, combine, send_type=None, dense=False):
    count = lax.axis_size(axis_name)
    index = lax.axis_index(axis_name)
    levels = count.bit_length() - 1
    rows = values.shape[0] // count
    part_shape = (rows,) + values.shape[1:]
    if dense:
        flat = math.prod(part_shape)
        part_shape = (flat // 128, 128) if flat % 128 == 0 else (1, flat)
    stacked = values.reshape((2,) * levels + part_shape)
    remaining = [count >> (j + 1) for j in range(levels)]
    for distance in distances:
        place = remaining.index(distance)
        low = lax.index_in_dim(stacked, 0, place, keepdims=False)
        high = lax.index_in_dim(stacked, 1, place, keepdims=False)
        upper = (index // distance) % 2 == 1
        keep = jnp.where(upper, high, low)
        send = jnp.where(upper, low, high)
        if send_type is not None:
            send = send.astype(send_type)
        received = swap_partner(send, axis_name, distance).astype(keep.dtype)
        stacked = combine(keep, received)
        remaining.pop(place)
    return stacked.reshape((rows,) + values.shape[1:])


def add_parts(first, second):
    return first + second


def merge_softmax(first, second, groups, head_dim):
    width = groups * head_dim
    first_max, second_max = first[..., width + groups:], second[..., width + groups:]
    top = jnp.maximum(first_max, second_max)
    first_scale = jnp.exp(first_max - top)
    second_scale = jnp.exp(second_max - top)
    acc = first[..., :width] * jnp.repeat(first_scale, head_dim, axis=-1) + second[
        ..., :width
    ] * jnp.repeat(second_scale, head_dim, axis=-1)
    total = first[..., width:width + groups] * first_scale + second[..., width:width + groups] * second_scale
    return jnp.concatenate([acc, total, top], axis=-1)

def shards(
    prefill_states,
    decode_states,
    attn_gain,
    query_weight,
    keyvalue_weight,
    output_weight,
    cache_keyval,
    cached_length,
    span_tenant,
    ffn_gain,
    expert_in,
    expert_out,
    routes,
    gate_values,
):
    seq_count = lax.axis_size("seq")
    tp_count = lax.axis_size("tp")
    seq_index = lax.axis_index("seq")
    tp_index = lax.axis_index("tp")
    pre_local, model_width = prefill_states.shape
    dec_local = decode_states.shape[0]
    heads_kv = keyvalue_weight.shape[1]
    head_dim = keyvalue_weight.shape[2] // 2
    heads_q = query_weight.shape[1] // head_dim
    query_group_count = heads_q // heads_kv
    score_scale = head_dim ** (-0.5)
    pre_share = pre_local // tp_count
    normalised_input = rms_norm(prefill_states, attn_gain)
    query_matrix = jnp.dot(
        normalised_input, query_weight, preferred_element_type=jnp.float32
    ).reshape(pre_local, heads_q, head_dim)
    keyvalue_rows = jnp.dot(
        normalised_input,
        keyvalue_weight.reshape(model_width, heads_kv * 2 * head_dim),
        preferred_element_type=jnp.float32,
    ).reshape(pre_local, heads_kv, 2 * head_dim)
    before = span_tables(span_tenant)
    token_index = seq_index * pre_local + jnp.arange(pre_local, dtype=jnp.int32)
    tenant, token_positions = token_tables(token_index, span_tenant, before)
    query_matrix = (
        apply_rotary(query_matrix, token_positions)
        .astype(jnp.bfloat16)
        .reshape(pre_local, heads_kv, query_group_count, head_dim)
    )
    rotated_keys = apply_rotary(keyvalue_rows[..., :head_dim], token_positions).astype(jnp.bfloat16)
    local_keyvals = jnp.concatenate(
        [rotated_keys, keyvalue_rows[..., head_dim:].astype(jnp.bfloat16)], axis=-1
    )
    seq_near_first = [1 << j for j in range(seq_count.bit_length() - 1)]
    key_piece = lax.all_gather(
        local_keyvals.reshape(pre_local, heads_kv * 2 * head_dim), "seq", axis=0, tiled=True
    ).reshape(-1, heads_kv, 2 * head_dim)
    piece_rows = key_piece.shape[0]
    block_len = math.gcd(piece_rows, key_block)
    blocks = key_piece.reshape(piece_rows // block_len, block_len, heads_kv, 2 * head_dim)
    query_count = pre_local * query_group_count
    query_rows = query_matrix.transpose(1, 0, 2, 3).reshape(heads_kv, query_count, head_dim)
    row_token = jnp.repeat(token_index, query_group_count)
    row_tenant = jnp.repeat(tenant, query_group_count)
    key_positions = jnp.arange(piece_rows, dtype=jnp.int32)
    key_tenant = token_tables(key_positions, span_tenant, before)[0]
    token_visible = (tenant[:, None] == key_tenant[None, :]) & (
        token_index[:, None] >= key_positions[None, :]
    )
    block_flags = jnp.any(
        token_visible.reshape(pre_local, piece_rows // block_len, block_len), axis=(0, 2)
    ).astype(jnp.int32)
    padded_queries = jnp.pad(query_rows, ((0, 0), (0, 0), (0, head_dim)))
    flat_keyvals = key_piece.reshape(piece_rows, heads_kv * 2 * head_dim)
    head_outputs = [
        flash_attend(
            block_flags,
            padded_queries[head],
            flat_keyvals,
            head,
            row_token,
            row_tenant,
            key_tenant,
            score_scale,
            block_len,
        )[:, head_dim:]
        for head in range(heads_kv)
    ]
    attended = (
        jnp.stack(head_outputs)
        .reshape(heads_kv, pre_local, query_group_count, head_dim)
        .transpose(1, 0, 2, 3)
        .reshape(pre_local, heads_q * head_dim)
    )
    prefill_part = jnp.dot(attended, output_weight, preferred_element_type=jnp.float32)
    tp_near_first = [1 << j for j in range(tp_count.bit_length() - 1)]
    prefill_sum = scatter_blocks(
        prefill_part, "tp", tp_near_first, add_parts, send_type=jnp.bfloat16, dense=True
    )
    group_states = gather_blocks(decode_states, "tp", tp_near_first[::-1])
    group_rows = group_states.shape[0]
    group_lengths = lax.dynamic_slice_in_dim(cached_length, seq_index * group_rows, group_rows, 0)
    decode_normalised = rms_norm(group_states, attn_gain)
    group_queries = jnp.dot(
        decode_normalised, query_weight, preferred_element_type=jnp.float32
    ).reshape(group_rows, heads_q, head_dim)
    group_queries = (
        apply_rotary(group_queries, group_lengths)
        .astype(jnp.bfloat16)
        .reshape(group_rows, heads_kv, query_group_count, head_dim)
    )
    decode_keyvalues = jnp.dot(
        decode_normalised,
        keyvalue_weight.reshape(model_width, heads_kv * 2 * head_dim),
        preferred_element_type=jnp.float32,
    ).reshape(group_rows, heads_kv, 2 * head_dim)
    new_keys = apply_rotary(decode_keyvalues[..., :head_dim], group_lengths).astype(jnp.bfloat16)
    new_vals = decode_keyvalues[..., head_dim:].astype(jnp.bfloat16)
    decode_queries = gather_blocks(group_queries, "seq", seq_near_first[::-1])
    cache_local = cache_keyval.shape[1]
    cache_pos = seq_index * cache_local + jnp.arange(cache_local, dtype=jnp.int32)
    visible = (cache_pos[None, :] < cached_length[:, None])[:, None, None, :]
    padded_decode = jnp.pad(decode_queries, ((0, 0), (0, 0), (0, 0), (0, head_dim)))
    scores = (
        jnp.einsum(
            "bhgd,bkhd->bhgk",
            padded_decode,
            cache_keyval,
            preferred_element_type=jnp.float32,
        )
        * score_scale
    )
    scores = jnp.where(visible, scores, masked_score)
    local_max = jnp.max(scores, axis=-1)
    weights_exp = jnp.where(visible, jnp.exp(scores - local_max[..., None]), 0.0)
    local_total = jnp.sum(weights_exp, axis=-1)
    local_acc = jnp.einsum(
        "bhgk,bkhd->bhgd",
        weights_exp.astype(jnp.bfloat16),
        cache_keyval,
        preferred_element_type=jnp.float32,
    )[..., head_dim:]
    dec_total = local_acc.shape[0]
    groups = heads_kv * query_group_count
    packed = jnp.concatenate(
        [
            local_acc.reshape(dec_total, groups * head_dim),
            local_total.reshape(dec_total, groups),
            local_max.reshape(dec_total, groups),
        ],
        axis=-1,
    )
    merged = scatter_blocks(
        packed, "seq", seq_near_first, lambda a, b: merge_softmax(a, b, groups, head_dim)
    )
    merged_acc = merged[:, : groups * head_dim].reshape(group_rows, heads_kv, query_group_count, head_dim)
    merged_total = merged[:, groups * head_dim : groups * (head_dim + 1)].reshape(
        group_rows, heads_kv, query_group_count
    )
    merged_max = merged[:, groups * (head_dim + 1) :].reshape(group_rows, heads_kv, query_group_count)
    own_score = (
        jnp.sum(
            group_queries.astype(jnp.float32) * new_keys.astype(jnp.float32)[:, :, None, :],
            axis=-1,
        )
        * score_scale
    )
    final_max = jnp.maximum(merged_max, own_score)
    rescale = jnp.exp(merged_max - final_max)
    own_exp = jnp.exp(own_score - final_max)
    final_total = merged_total * rescale + own_exp
    own_rounded = lax.optimization_barrier(own_exp.astype(jnp.bfloat16)).astype(jnp.float32)
    final_acc = (
        merged_acc * rescale[..., None]
        + own_rounded[..., None] * new_vals.astype(jnp.float32)[:, :, None, :]
    )
    decode_attended = (
        (final_acc / final_total[..., None])
        .astype(jnp.bfloat16)
        .reshape(group_rows, heads_q * head_dim)
    )
    decode_part = jnp.dot(decode_attended, output_weight, preferred_element_type=jnp.float32)
    decode_sum = scatter_blocks(decode_part, "tp", tp_near_first, add_parts, dense=True)
    own_states = lax.dynamic_slice_in_dim(prefill_states, tp_index * pre_share, pre_share, 0)
    prefill_h = (own_states.astype(jnp.float32) + prefill_sum).astype(jnp.bfloat16)
    decode_h = (decode_states.astype(jnp.float32) + decode_sum).astype(jnp.bfloat16)
    moe_in = jnp.concatenate([prefill_h, decode_h], axis=0)
    normed_moe = rms_norm(moe_in, ffn_gain)
    rows_dev, top_count = routes.shape
    capacity = 2 * ((rows_dev * top_count + EXPERTS - 1) // EXPERTS)
    capacity = -(-capacity // 8) * 8
    flat_routes = routes.reshape(rows_dev * top_count)
    expert_ids = jnp.arange(EXPERTS, dtype=jnp.int32)
    onehot = (flat_routes[:, None] == expert_ids[None, :]).astype(jnp.int32)
    slot_rank = jnp.sum(jnp.cumsum(onehot, axis=0) * onehot, axis=1) - 1
    slot_index = flat_routes * capacity + slot_rank
    repeated = jnp.repeat(normed_moe, top_count, axis=0)
    buffer = jnp.zeros((EXPERTS * capacity, model_width), jnp.bfloat16).at[slot_index].set(repeated)
    outgoing = buffer.reshape(seq_count, EXPERTS // seq_count, capacity, model_width)
    hidden = jnp.einsum(
        "secd,edf->secf",
        lax.all_to_all(outgoing, "seq", split_axis=0, concat_axis=0, tiled=True),
        expert_in,
        preferred_element_type=jnp.float32,
    )
    ff_width = expert_out.shape[1]
    active = (jax.nn.silu(hidden[..., :ff_width]) * hidden[..., ff_width:]).astype(jnp.bfloat16)
    results = jnp.einsum(
        "secf,efd->secd", active, expert_out, preferred_element_type=jnp.float32
    ).astype(jnp.bfloat16)
    returned = lax.all_to_all(results, "seq", split_axis=0, concat_axis=0, tiled=True)
    fetched = (
        returned.reshape(EXPERTS * capacity, model_width)[slot_index]
        .astype(jnp.float32)
        .reshape(rows_dev, top_count, model_width)
    )
    combined = jnp.sum(fetched * gate_values[..., None], axis=1)
    layer_out = (moe_in.astype(jnp.float32) + combined).astype(jnp.bfloat16)
    return (layer_out[:pre_share], layer_out[pre_share:])


def solution(mesh):
    return jax.shard_map(
        shards,
        mesh=mesh,
        in_specs=(
            P("seq", None),
            P(("seq", "tp"), None),
            P(),
            P(None, "tp"),
            P(None, "tp", None),
            P("tp", None),
            P(None, "seq", "tp", None),
            P(),
            P(),
            P(),
            P("seq", None, None),
            P("seq", None, None),
            P(("seq", "tp"), None),
            P(("seq", "tp"), None),
        ),
        out_specs=(P(("seq", "tp"), None), P(("seq", "tp"), None)),
        check_vma=False,
    )
```

```python
import math

import jax
import jax.numpy as jnp
from jax import lax
from jax.sharding import PartitionSpec as P
from jax.experimental import pallas as pl
from jax.experimental.pallas import tpu as pltpu

EXPERTS = 32
SPAN = 2048


eps_norm = 1e-05
rope_base = 10000.0
masked_score = -1e30
key_block = 256


def rms_norm(values, scales):
    floats = values.astype(jnp.float32)
    factor = lax.rsqrt(jnp.mean(floats * floats, axis=-1, keepdims=True) + eps_norm)
    return (floats * factor * scales.astype(jnp.float32)).astype(jnp.bfloat16)


def apply_rotary(values, token_positions):
    half_dim = values.shape[-1] // 2
    frequency = rope_base ** (-2.0 * jnp.arange(half_dim, dtype=jnp.float32) / values.shape[-1])
    angles = token_positions.astype(jnp.float32)[:, None] * frequency[None, :]
    cosine = jnp.cos(angles)[:, None, :]
    sine_part = jnp.sin(angles)[:, None, :]
    first_half = values[..., :half_dim]
    second_half = values[..., half_dim:]
    return jnp.concatenate(
        [
            first_half * cosine - second_half * sine_part,
            second_half * cosine + first_half * sine_part,
        ],
        axis=-1,
    )


def span_tables(span_tenant):
    span_count = span_tenant.shape[0]
    ordinal = jnp.arange(span_count, dtype=jnp.int32)
    same_tenant = span_tenant[:, None] == span_tenant[None, :]
    earlier = ordinal[None, :] < ordinal[:, None]
    return jnp.sum(jnp.where(same_tenant & earlier, 1, 0), axis=1).astype(jnp.int32)


def token_tables(token_index, span_tenant, before):
    span_count = span_tenant.shape[0]
    span_index = token_index // SPAN
    onehot = span_index[:, None] == jnp.arange(span_count, dtype=jnp.int32)[None, :]
    tenant = jnp.sum(jnp.where(onehot, span_tenant[None, :], 0), axis=1)
    offset = jnp.sum(jnp.where(onehot, before[None, :], 0), axis=1)
    return (tenant, offset * SPAN + token_index % SPAN)


def attend_keys(fold_state, keyvalue_rows, visible, query_matrix, score_scale):
    run_max, run_total, run_acc = fold_state
    head_dim = keyvalue_rows.shape[-1] // 2
    scores = (
        jnp.einsum(
            "qhgd,khd->qhgk",
            query_matrix,
            keyvalue_rows[..., :head_dim],
            preferred_element_type=jnp.float32,
        )
        * score_scale
    )
    mask_full = visible[:, None, None, :]
    scores = jnp.where(mask_full, scores, masked_score)
    new_max = jnp.maximum(run_max, jnp.max(scores, axis=-1))
    weights_exp = jnp.where(mask_full, jnp.exp(scores - new_max[..., None]), 0.0)
    factor = jnp.exp(run_max - new_max)
    new_total = run_total * factor + jnp.sum(weights_exp, axis=-1)
    new_acc = run_acc * factor[..., None] + jnp.einsum(
        "qhgk,khd->qhgd",
        weights_exp.astype(jnp.bfloat16),
        keyvalue_rows[..., head_dim:],
        preferred_element_type=jnp.float32,
    )
    return (new_max, new_total, new_acc)


def flash_kernel(
    flags_ref, q_ref, k_ref, v_ref, row_token_ref, row_tenant_ref, key_tenant_ref,
    o_ref, max_ref, total_ref, acc_ref, *, score_scale, block_len
):
    step = pl.program_id(0)

    @pl.when(step == 0)
    def _():
        max_ref[...] = jnp.full(max_ref.shape, masked_score, jnp.float32)
        total_ref[...] = jnp.zeros(total_ref.shape, jnp.float32)
        acc_ref[...] = jnp.zeros(acc_ref.shape, jnp.float32)

    @pl.when(flags_ref[step] != 0)
    def _():
        scores = (
            lax.dot_general(
                q_ref[...], v_ref[...], (((1,), (1,)), ((), ())),
                preferred_element_type=jnp.float32,
            )
            * score_scale
        )
        key_index = step * block_len + lax.broadcasted_iota(jnp.int32, (1, block_len), 1)
        visible = (row_tenant_ref[...] == key_tenant_ref[...]) & (
            row_token_ref[...] >= key_index
        )
        scores = jnp.where(visible, scores, masked_score)
        run_max = max_ref[...]
        new_max = jnp.maximum(run_max, jnp.max(scores, axis=-1, keepdims=True))
        weights_exp = jnp.where(visible, jnp.exp(scores - new_max), 0.0)
        factor = jnp.exp(run_max - new_max)
        total_ref[...] = total_ref[...] * factor + jnp.sum(weights_exp, axis=-1, keepdims=True)
        acc_ref[...] = acc_ref[...] * factor + jnp.dot(
            weights_exp.astype(jnp.bfloat16), v_ref[...], preferred_element_type=jnp.float32
        )
        max_ref[...] = new_max

    @pl.when(step == pl.num_programs(0) - 1)
    def _():
        o_ref[...] = (acc_ref[...] / total_ref[...]).astype(o_ref.dtype)


def flash_attend(flags, queries, keyvals, head, row_token, row_tenant, key_tenant, score_scale, block_len, interpret=False):
    query_count, head_dim = queries.shape
    key_count = keyvals.shape[0]
    full = lambda step, flags_ref: (0, 0)
    grid_spec = pltpu.PrefetchScalarGridSpec(
        num_scalar_prefetch=1,
        grid=(key_count // block_len,),
        in_specs=[
            pl.BlockSpec((query_count, head_dim), full),
            pl.BlockSpec((block_len, head_dim), lambda step, flags_ref: (step, head)),
            pl.BlockSpec((block_len, head_dim), lambda step, flags_ref: (step, head)),
            pl.BlockSpec((query_count, 1), full),
            pl.BlockSpec((query_count, 1), full),
            pl.BlockSpec((1, block_len), lambda step, flags_ref: (0, step)),
        ],
        out_specs=pl.BlockSpec((query_count, head_dim), full),
        scratch_shapes=[
            pltpu.VMEM((query_count, 1), jnp.float32),
            pltpu.VMEM((query_count, 1), jnp.float32),
            pltpu.VMEM((query_count, head_dim), jnp.float32),
        ],
    )
    body = lambda *refs: flash_kernel(*refs, score_scale=score_scale, block_len=block_len)
    return pl.pallas_call(
        body,
        grid_spec=grid_spec,
        out_shape=jax.ShapeDtypeStruct((query_count, head_dim), jnp.bfloat16),
        interpret=interpret,
    )(flags, queries, keyvals, keyvals, row_token[:, None], row_tenant[:, None], key_tenant[None, :])


def swap_partner(values, axis_name, distance):
    count = lax.axis_size(axis_name)
    pairs = [(i, i ^ distance) for i in range(count)]
    return lax.ppermute(values, axis_name, pairs)


def lane_dense(values):
    flat = values.reshape(-1)
    return flat.reshape(-1, 128) if flat.shape[0] % 128 == 0 else flat.reshape(1, -1)


def gather_blocks(block, axis_name, distances):
    index = lax.axis_index(axis_name)
    shape = block.shape
    block = lane_dense(block)[None]
    stacked = block
    done = []
    for distance in distances:
        theirs = swap_partner(stacked, axis_name, distance)
        upper = (index // distance) % 2 == 1
        low = jnp.where(upper, theirs, stacked)
        high = jnp.where(upper, stacked, theirs)
        place = sum(1 for d in done if d > distance)
        stacked = jnp.stack([low, high], axis=place)
        done.append(distance)
    return stacked.reshape((-1,) + shape[1:])


def scatter_blocks(values, axis_name, distances, combine, send_type=None, dense=False):
    count = lax.axis_size(axis_name)
    index = lax.axis_index(axis_name)
    levels = count.bit_length() - 1
    rows = values.shape[0] // count
    part_shape = (rows,) + values.shape[1:]
    if dense:
        flat = math.prod(part_shape)
        part_shape = (flat // 128, 128) if flat % 128 == 0 else (1, flat)
    stacked = values.reshape((2,) * levels + part_shape)
    remaining = [count >> (j + 1) for j in range(levels)]
    for distance in distances:
        place = remaining.index(distance)
        low = lax.index_in_dim(stacked, 0, place, keepdims=False)
        high = lax.index_in_dim(stacked, 1, place, keepdims=False)
        upper = (index // distance) % 2 == 1
        keep = jnp.where(upper, high, low)
        send = jnp.where(upper, low, high)
        if send_type is not None:
            send = send.astype(send_type)
        received = swap_partner(send, axis_name, distance).astype(keep.dtype)
        stacked = combine(keep, received)
        remaining.pop(place)
    return stacked.reshape((rows,) + values.shape[1:])


def add_parts(first, second):
    return first + second


def merge_softmax(first, second, groups, head_dim):
    width = groups * head_dim
    first_max, second_max = first[..., width + groups:], second[..., width + groups:]
    top = jnp.maximum(first_max, second_max)
    first_scale = jnp.exp(first_max - top)
    second_scale = jnp.exp(second_max - top)
    acc = first[..., :width] * jnp.repeat(first_scale, head_dim, axis=-1) + second[
        ..., :width
    ] * jnp.repeat(second_scale, head_dim, axis=-1)
    total = first[..., width:width + groups] * first_scale + second[..., width:width + groups] * second_scale
    return jnp.concatenate([acc, total, top], axis=-1)

def shards(
    prefill_states,
    decode_states,
    attn_gain,
    query_weight,
    keyvalue_weight,
    output_weight,
    cache_keyval,
    cached_length,
    span_tenant,
    ffn_gain,
    expert_in,
    expert_out,
    routes,
    gate_values,
):
    seq_count = lax.axis_size("seq")
    tp_count = lax.axis_size("tp")
    seq_index = lax.axis_index("seq")
    tp_index = lax.axis_index("tp")
    pre_local, model_width = prefill_states.shape
    dec_local = decode_states.shape[0]
    heads_kv = keyvalue_weight.shape[1]
    head_dim = keyvalue_weight.shape[2] // 2
    heads_q = query_weight.shape[1] // head_dim
    query_group_count = heads_q // heads_kv
    score_scale = head_dim ** (-0.5)
    pre_share = pre_local // tp_count
    normalised_input = rms_norm(prefill_states, attn_gain)
    query_matrix = jnp.dot(
        normalised_input, query_weight, preferred_element_type=jnp.float32
    ).reshape(pre_local, heads_q, head_dim)
    keyvalue_rows = jnp.dot(
        normalised_input,
        keyvalue_weight.reshape(model_width, heads_kv * 2 * head_dim),
        preferred_element_type=jnp.float32,
    ).reshape(pre_local, heads_kv, 2 * head_dim)
    before = span_tables(span_tenant)
    token_index = seq_index * pre_local + jnp.arange(pre_local, dtype=jnp.int32)
    tenant, token_positions = token_tables(token_index, span_tenant, before)
    query_matrix = (
        apply_rotary(query_matrix, token_positions)
        .astype(jnp.bfloat16)
        .reshape(pre_local, heads_kv, query_group_count, head_dim)
    )
    rotated_keys = apply_rotary(keyvalue_rows[..., :head_dim], token_positions).astype(jnp.bfloat16)
    local_keyvals = jnp.concatenate(
        [rotated_keys, keyvalue_rows[..., head_dim:].astype(jnp.bfloat16)], axis=-1
    )
    seq_near_first = [1 << j for j in range(seq_count.bit_length() - 1)]
    key_piece = lax.all_gather(
        local_keyvals.reshape(pre_local, heads_kv * 2 * head_dim), "seq", axis=0, tiled=True
    ).reshape(-1, heads_kv, 2 * head_dim)
    piece_rows = key_piece.shape[0]
    block_len = math.gcd(piece_rows, key_block)
    blocks = key_piece.reshape(piece_rows // block_len, block_len, heads_kv, 2 * head_dim)
    query_count = pre_local * query_group_count
    query_rows = query_matrix.transpose(1, 0, 2, 3).reshape(heads_kv, query_count, head_dim)
    row_token = jnp.repeat(token_index, query_group_count)
    row_tenant = jnp.repeat(tenant, query_group_count)
    key_positions = jnp.arange(piece_rows, dtype=jnp.int32)
    key_tenant = token_tables(key_positions, span_tenant, before)[0]
    token_visible = (tenant[:, None] == key_tenant[None, :]) & (
        token_index[:, None] >= key_positions[None, :]
    )
    block_flags = jnp.any(
        token_visible.reshape(pre_local, piece_rows // block_len, block_len), axis=(0, 2)
    ).astype(jnp.int32)
    padded_queries = jnp.pad(query_rows, ((0, 0), (0, 0), (0, head_dim)))
    flat_keyvals = key_piece.reshape(piece_rows, heads_kv * 2 * head_dim)
    head_outputs = [
        flash_attend(
            block_flags,
            padded_queries[head],
            flat_keyvals,
            head,
            row_token,
            row_tenant,
            key_tenant,
            score_scale,
            block_len,
        )[:, head_dim:]
        for head in range(heads_kv)
    ]
    attended = (
        jnp.stack(head_outputs)
        .reshape(heads_kv, pre_local, query_group_count, head_dim)
        .transpose(1, 0, 2, 3)
        .reshape(pre_local, heads_q * head_dim)
    )
    prefill_part = jnp.dot(attended, output_weight, preferred_element_type=jnp.float32)
    tp_near_first = [1 << j for j in range(tp_count.bit_length() - 1)]
    prefill_sum = scatter_blocks(
        prefill_part, "tp", tp_near_first, add_parts, send_type=jnp.bfloat16, dense=True
    )
    group_states = gather_blocks(decode_states, "tp", tp_near_first[::-1])
    group_rows = group_states.shape[0]
    group_lengths = lax.dynamic_slice_in_dim(cached_length, seq_index * group_rows, group_rows, 0)
    decode_normalised = rms_norm(group_states, attn_gain)
    group_queries = jnp.dot(
        decode_normalised, query_weight, preferred_element_type=jnp.float32
    ).reshape(group_rows, heads_q, head_dim)
    group_queries = (
        apply_rotary(group_queries, group_lengths)
        .astype(jnp.bfloat16)
        .reshape(group_rows, heads_kv, query_group_count, head_dim)
    )
    decode_keyvalues = jnp.dot(
        decode_normalised,
        keyvalue_weight.reshape(model_width, heads_kv * 2 * head_dim),
        preferred_element_type=jnp.float32,
    ).reshape(group_rows, heads_kv, 2 * head_dim)
    new_keys = apply_rotary(decode_keyvalues[..., :head_dim], group_lengths).astype(jnp.bfloat16)
    new_vals = decode_keyvalues[..., head_dim:].astype(jnp.bfloat16)
    decode_queries = gather_blocks(group_queries, "seq", seq_near_first[::-1])
    cache_local = cache_keyval.shape[1]
    cache_pos = seq_index * cache_local + jnp.arange(cache_local, dtype=jnp.int32)
    visible = (cache_pos[None, :] < cached_length[:, None])[:, None, None, :]
    padded_decode = jnp.pad(decode_queries, ((0, 0), (0, 0), (0, 0), (0, head_dim)))
    scores = (
        jnp.einsum(
            "bhgd,bkhd->bhgk",
            padded_decode,
            cache_keyval,
            preferred_element_type=jnp.float32,
        )
        * score_scale
    )
    scores = jnp.where(visible, scores, masked_score)
    local_max = jnp.max(scores, axis=-1)
    weights_exp = jnp.where(visible, jnp.exp(scores - local_max[..., None]), 0.0)
    local_total = jnp.sum(weights_exp, axis=-1)
    local_acc = jnp.einsum(
        "bhgk,bkhd->bhgd",
        weights_exp.astype(jnp.bfloat16),
        cache_keyval,
        preferred_element_type=jnp.float32,
    )[..., head_dim:]
    dec_total = local_acc.shape[0]
    groups = heads_kv * query_group_count
    packed = jnp.concatenate(
        [
            local_acc.reshape(dec_total, groups * head_dim),
            local_total.reshape(dec_total, groups),
            local_max.reshape(dec_total, groups),
        ],
        axis=-1,
    )
    merged = scatter_blocks(
        packed, "seq", seq_near_first, lambda a, b: merge_softmax(a, b, groups, head_dim)
    )
    merged_acc = merged[:, : groups * head_dim].reshape(group_rows, heads_kv, query_group_count, head_dim)
    merged_total = merged[:, groups * head_dim : groups * (head_dim + 1)].reshape(
        group_rows, heads_kv, query_group_count
    )
    merged_max = merged[:, groups * (head_dim + 1) :].reshape(group_rows, heads_kv, query_group_count)
    own_score = (
        jnp.sum(
            group_queries.astype(jnp.float32) * new_keys.astype(jnp.float32)[:, :, None, :],
            axis=-1,
        )
        * score_scale
    )
    final_max = jnp.maximum(merged_max, own_score)
    rescale = jnp.exp(merged_max - final_max)
    own_exp = jnp.exp(own_score - final_max)
    final_total = merged_total * rescale + own_exp
    own_rounded = lax.optimization_barrier(own_exp.astype(jnp.bfloat16)).astype(jnp.float32)
    final_acc = (
        merged_acc * rescale[..., None]
        + own_rounded[..., None] * new_vals.astype(jnp.float32)[:, :, None, :]
    )
    decode_attended = (
        (final_acc / final_total[..., None])
        .astype(jnp.bfloat16)
        .reshape(group_rows, heads_q * head_dim)
    )
    decode_part = jnp.dot(decode_attended, output_weight, preferred_element_type=jnp.float32)
    decode_sum = scatter_blocks(decode_part, "tp", tp_near_first, add_parts, dense=True)
    own_states = lax.dynamic_slice_in_dim(prefill_states, tp_index * pre_share, pre_share, 0)
    prefill_h = (own_states.astype(jnp.float32) + prefill_sum).astype(jnp.bfloat16)
    decode_h = (decode_states.astype(jnp.float32) + decode_sum).astype(jnp.bfloat16)
    moe_in = jnp.concatenate([prefill_h, decode_h], axis=0)
    normed_moe = rms_norm(moe_in, ffn_gain)
    rows_dev, top_count = routes.shape
    capacity = 2 * ((rows_dev * top_count + EXPERTS - 1) // EXPERTS)
    capacity = -(-capacity // 8) * 8
    flat_routes = routes.reshape(rows_dev * top_count)
    expert_ids = jnp.arange(EXPERTS, dtype=jnp.int32)
    onehot = (flat_routes[:, None] == expert_ids[None, :]).astype(jnp.int32)
    slot_rank = jnp.sum(jnp.cumsum(onehot, axis=0) * onehot, axis=1) - 1
    slot_index = flat_routes * capacity + slot_rank
    repeated = jnp.repeat(normed_moe, top_count, axis=0)
    buffer = jnp.zeros((EXPERTS * capacity, model_width), jnp.bfloat16).at[slot_index].set(repeated)
    outgoing = buffer.reshape(seq_count, EXPERTS // seq_count, capacity, model_width)
    hidden = jnp.einsum(
        "secd,edf->secf",
        lax.all_to_all(outgoing, "seq", split_axis=0, concat_axis=0, tiled=True),
        expert_in,
        preferred_element_type=jnp.float32,
    )
    ff_width = expert_out.shape[1]
    active = (jax.nn.silu(hidden[..., :ff_width]) * hidden[..., ff_width:]).astype(jnp.bfloat16)
    results = jnp.einsum(
        "secf,efd->secd", active, expert_out, preferred_element_type=jnp.float32
    ).astype(jnp.bfloat16)
    returned = lax.all_to_all(results, "seq", split_axis=0, concat_axis=0, tiled=True)
    fetched = (
        returned.reshape(EXPERTS * capacity, model_width)[slot_index]
        .astype(jnp.float32)
        .reshape(rows_dev, top_count, model_width)
    )
    combined = jnp.sum(fetched * gate_values[..., None], axis=1)
    layer_out = (moe_in.astype(jnp.float32) + combined).astype(jnp.bfloat16)
    return (layer_out[:pre_share], layer_out[pre_share:])


def solution(mesh):
    return jax.shard_map(
        shards,
        mesh=mesh,
        in_specs=(
            P("seq", None),
            P(("seq", "tp"), None),
            P(),
            P(None, "tp"),
            P(None, "tp", None),
            P("tp", None),
            P(None, "seq", "tp", None),
            P(),
            P(),
            P(),
            P("seq", None, None),
            P("seq", None, None),
            P(("seq", "tp"), None),
            P(("seq", "tp"), None),
        ),
        out_specs=(P(("seq", "tp"), None), P(("seq", "tp"), None)),
        check_vma=False,
    )
```
